32 devices in a mesh: dp: 16 (over z, x, core), tensor: 2 (over y).
Axes of the slice: x: 2, y: 2, z: 4, core: 2. Of those that a mesh axis runs over, the one named last changes fastest.
Arguments:
- block_input: bfloat16 [4096, 768], P(('dp', 'tensor')), may hold values from -24 to 24
- cotangent: bfloat16 [4096, 768], P(('dp', 'tensor')), may hold values from -6 to 6
- segments: int32 [16, 256], P('dp'), may hold values from 0 to 3, never falling along the last dimension, each value on 1 to 128 neighbouring positions
- qkv_weight: bfloat16 [2, 768, 3, 768], P(None, 'dp', None, 'tensor'), may hold values from -0.21875 to 0.21875
- proj_weight: bfloat16 [2, 768, 768], P(None, 'tensor', 'dp'), may hold values from -1.75 to 1.75
- up_weight: bfloat16 [2, 768, 3072], P(None, 'dp', 'tensor'), may hold values from -0.21875 to 0.21875
- down_weight: bfloat16 [2, 3072, 768], P(None, 'tensor', 'dp'), may hold values from -0.109375 to 0.109375
- norm_gains: float32 [2, 2, 768], replicated, may hold values from 0.5 to 1.5
- biases: float32 [2, 4, 768], replicated, may hold values from -3 to 3
- qkv_bias: float32 [2, 3, 768], replicated, may hold values from -2.5 to 2.5
- up_bias: float32 [2, 3072], replicated, may hold values from -3 to 3
- qkv_state: float32 [2, 768, 3, 768], P(None, 'dp', None, 'tensor'), may hold values from -40 to 40
- proj_state: float32 [2, 768, 768], P(None, 'tensor', 'dp'), may hold values from -40 to 40
- up_state: float32 [2, 768, 3072], P(None, 'dp', 'tensor'), may hold values from -40 to 40
- down_state: float32 [2, 3072, 768], P(None, 'tensor', 'dp'), may hold values from -40 to 40
Outputs:
- block_output: float32 [4096, 768], P(('dp', 'tensor'))
- input_grad: float32 [4096, 768], P(('dp', 'tensor'))
- qkv_grad: float32 [2, 768, 3, 768], P(None, 'dp', None, 'tensor')
- proj_grad: float32 [2, 768, 768], P(None, 'tensor', 'dp')
- up_grad: float32 [2, 768, 3072], P(None, 'dp', 'tensor')
- down_grad: float32 [2, 3072, 768], P(None, 'tensor', 'dp')
- gains_grad: float32 [2, 2, 768], replicated
- biases_grad: float32 [2, 4, 768], replicated
- qkv_bias_grad: float32 [2, 3, 768], replicated
- up_bias_grad: float32 [2, 3072], replicated
- qkv_new: float32 [2, 768, 3, 768], P(None, 'dp', None, 'tensor')
- proj_new: float32 [2, 768, 768], P(None, 'tensor', 'dp')
- up_new: float32 [2, 768, 3072], P(None, 'dp', 'tensor')
- down_new: float32 [2, 3072, 768], P(None, 'tensor', 'dp')
- gains_new: float32 [2, 2, 768], replicated
- biases_new: float32 [2, 4, 768], replicated
- qkv_bias_new: float32 [2, 3, 768], replicated
- up_bias_new: float32 [2, 3072], replicated
- qkv_state_new: float32 [2, 768, 3, 768], P(None, 'dp', None, 'tensor')
- proj_state_new: float32 [2, 768, 768], P(None, 'tensor', 'dp')
- up_state_new: float32 [2, 768, 3072], P(None, 'dp', 'tensor')
- down_state_new: float32 [2, 3072, 768], P(None, 'tensor', 'dp')
The draws below stay inside these ranges and needn't reach their ends.
All inputs are finite; a program needn't handle non-finite values.
Results may differ from the reference program's by a relative error of at most 0.02.
Values may be sent and summed in bfloat16 or wider, within the bound.
No kernel may reach another device: no remote copies, remote signals or barrier semaphores. Data moves between devices by JAX's collectives and lax.ppermute only.
A program may use at most 192 MiB of HBM per device.

```python
import math
import jax
import jax.numpy as jnp
import numpy as np
from jax import lax

D = 768
H = 12
HD = 64
FF = 3072
ROT = 16
LAYERS = 2
NS_ITERS = 5
DOCS = 4
TOK_DP = 256
ROWS = 16
TOKENS = 4096
N_DP = 16


def draw_block_input(key, part):
    key_base, key_cols, key_rows = jax.random.split(key, 3)
    col_scale = jnp.exp(jax.random.uniform(key_cols, (1, D), minval=math.log(0.3), maxval=math.log(3.0)))
    row_scale = jnp.exp(jax.random.uniform(key_rows, (TOKENS, 1), minval=math.log(0.5), maxval=math.log(2.0)))
    base = jax.random.normal(key_base, (TOKENS, D))
    return jnp.clip(base * col_scale * row_scale, -24.0, 24.0).astype(jnp.bfloat16)


def draw_qkv_bias(key, part):
    key_base = jax.random.fold_in(key, 0)
    base = 0.5 * jax.random.normal(key_base, (LAYERS, 3, D))
    return jnp.clip(base, -2.5, 2.5).astype(jnp.float32)


def level_of(own_key, extent, cuts, least, largest):
    def one(position, blocks):
        steps = jax.random.uniform(jax.random.fold_in(jax.random.fold_in(own_key, 6), position), (blocks,), jnp.float32, least / len(cuts), largest / len(cuts))
        return jnp.repeat(jnp.exp(steps), extent[position] // blocks).reshape((-1,) + (1,) * (len(extent) - position - 1))

    factor_of = one(*cuts[0])
    for cut in cuts[1:]:
        factor_of = factor_of * one(*cut)
    return factor_of


def split_up(amount, total, reach, slope):
    portions = [(1 << 20) // math.isqrt(standing ** slope) + 1 for standing in range(2, amount + 1)]
    surplus, holding = total - reach - (amount - 1), [1] * (amount - 1)
    while surplus > 0:
        free = [i for i in range(amount - 1) if holding[i] < reach]
        mass, budget = sum([portions[i] for i in free]), surplus
        for i in free:
            addition = min(reach - holding[i], max(1, budget * portions[i] // mass), surplus)
            holding[i] = holding[i] + addition
            surplus = surplus - addition
    return np.array([reach] + holding)


def uneven(stream_key, count, total, reach, lean):
    if count == 2:
        one = jax.random.randint(stream_key, (), max(1, total - reach), min(reach, total - 1) + 1)
        return jnp.stack([one, total - one])
    tallies = jnp.asarray(split_up(count, total, reach, lean), jnp.int32)
    couples = (count - 1) // 2
    source_of, taker = tallies[1:1 + 2 * couples:2], tallies[2:2 + 2 * couples:2]
    room = jnp.minimum(source_of - 1, reach - taker)
    moved = jax.random.randint(jax.random.fold_in(stream_key, 1), (couples,), 0, 1 << 20) % (room + 1)
    tallies = tallies.at[1:1 + 2 * couples:2].set(source_of - moved).at[2:2 + 2 * couples:2].set(taker + moved)
    return tallies[jax.random.permutation(jax.random.fold_in(stream_key, 2), count)]


def noise(stream_key, shape, scale, bound, shards=(), kind=jnp.bfloat16):
    array = jax.random.normal(stream_key, shape, jnp.float32) * scale
    if len(shards) > 0:
        array = level_of(stream_key, shape, shards, -0.22, 0.18) * array
    return jnp.clip(array, min=-bound, max=bound).astype(kind)


def setup_inputs(seed: int = 0) -> dict:
    splits = jax.random.split(jax.random.key(seed), 16)
    block_input = draw_block_input(jax.random.fold_in(splits[15], 71), 0)
    cotangent = noise(splits[1], (TOKENS, D), 1.0, 6.0, ((0, 32),))
    segments = jax.vmap(lambda own: jnp.searchsorted(jnp.cumsum(uneven(own, DOCS, TOK_DP, TOK_DP // 2, 2)), jnp.arange(TOK_DP), side="right"))(jax.random.split(splits[2], ROWS)).reshape((ROWS, TOK_DP)).astype(jnp.int32)
    qkv_weight = noise(splits[3], (LAYERS, D, 3, D), D ** -0.5, 0.21875, ((1, 16), (3, 2)))
    proj_weight = noise(splits[4], (LAYERS, D, D), (D // 64) ** -0.5, 1.75, ((1, 2), (2, 16)))
    up_weight = noise(splits[5], (LAYERS, D, FF), D ** -0.5, 0.21875, ((1, 16), (2, 2)))
    down_weight = noise(splits[6], (LAYERS, FF, D), FF ** -0.5, 0.109375, ((1, 2), (2, 16)))
    norm_gains = jnp.clip(1.0 + 0.1 * jax.random.normal(splits[7], (LAYERS, 2, D), jnp.float32), 0.5, 1.5)
    biases = noise(splits[8], (LAYERS, 4, D), 0.5, 3.0, (), jnp.float32)
    qkv_bias = draw_qkv_bias(jax.random.fold_in(splits[15], 71), 0)
    up_bias = noise(splits[10], (LAYERS, FF), 0.5, 3.0, (), jnp.float32)
    qkv_state = noise(splits[11], (LAYERS, D, 3, D), (0.1 * (N_DP * TOK_DP) ** 0.5), 40.0, ((1, 16), (3, 2)), jnp.float32)
    proj_state = noise(splits[12], (LAYERS, D, D), (0.1 * (N_DP * TOK_DP) ** 0.5), 40.0, ((1, 2), (2, 16)), jnp.float32)
    up_state = noise(splits[13], (LAYERS, D, FF), (0.1 * (N_DP * TOK_DP) ** 0.5), 40.0, ((1, 16), (2, 2)), jnp.float32)
    down_state = noise(splits[14], (LAYERS, FF, D), (0.1 * (N_DP * TOK_DP) ** 0.5), 40.0, ((1, 2), (2, 16)), jnp.float32)
    return {"block_input": block_input, "cotangent": cotangent, "segments": segments, "qkv_weight": qkv_weight, "proj_weight": proj_weight, "up_weight": up_weight, "down_weight": down_weight, "norm_gains": norm_gains, "biases": biases, "qkv_bias": qkv_bias, "up_bias": up_bias, "qkv_state": qkv_state, "proj_state": proj_state, "up_state": up_state, "down_state": down_state}


highest = lax.Precision.HIGHEST
norm_eps = 1e-05
masked_score = -1e+30
coef_first = 3.4445
coef_second = -4.775
coef_third = 2.0315
momentum = 0.9
muon_rate = 0.2
match_rms = 0.2
vector_rate = 0.2
vector_eps = 1e-06
frobenius_eps = 1e-07

@jax.custom_vjp
def low(v):
    return lax.optimization_barrier(v.astype(jnp.bfloat16)).astype(jnp.float32)

@jax.custom_vjp
def low_back(v):
    return v

def low_keep(v):
    return (low(v), None)

def low_pass(kept, grad):
    return (grad,)

def back_keep(v):
    return (v, None)

def back_low(kept, grad):
    return (low(grad),)
low.defvjp(low_keep, low_pass)
low_back.defvjp(back_keep, back_low)

def rotary_tables(segment_row):
    length = segment_row.shape[0]
    indices = jnp.arange(length, dtype=jnp.int32)
    change = jnp.concatenate([jnp.ones((1,), dtype=bool), segment_row[1:] != segment_row[:-1]])
    starts = lax.cummax(jnp.where(change, indices, jnp.zeros_like(indices)), axis=0)
    positions = (indices - starts).astype(jnp.float32)
    half_rot = ROT // 2
    frequency = 10000.0 ** (-2.0 * jnp.arange(half_rot, dtype=jnp.float32) / ROT)
    angles = positions[:, None] * frequency[None, :]
    return (jnp.cos(angles), jnp.sin(angles))

def rotate(values, cosine_table, sine_table):
    half_rot = ROT // 2
    first_half = values[..., :half_rot]
    second_half = values[..., half_rot:ROT]
    cos_b = cosine_table[:, None, :]
    sin_b = sine_table[:, None, :]
    return jnp.concatenate([first_half * cos_b - second_half * sin_b, second_half * cos_b + first_half * sin_b, values[..., ROT:]], axis=-1)

def normalize(stream):
    centered = stream - lax.optimization_barrier(jnp.mean(stream, axis=-1, keepdims=True))
    inverse = lax.rsqrt(lax.optimization_barrier(jnp.mean(centered * centered, axis=-1, keepdims=True)) + norm_eps)
    return centered * inverse

def gelu_exact(values):
    return jax.nn.gelu(values, approximate=False)

def forward_row(row_input, segment_row, qkv_full, proj_full, up_full, down_full, gains_all, shifts_all, qkv_shift, up_shift):
    cosine_table, sine_table = rotary_tables(segment_row)
    length = row_input.shape[0]
    indices = jnp.arange(length, dtype=jnp.int32)
    allowed = (segment_row[:, None] == segment_row[None, :]) & (indices[:, None] >= indices[None, :])
    stream = row_input
    for layer_id in range(LAYERS):
        normed = normalize(stream)
        attn_in = low(normed * gains_all[layer_id, 0] + shifts_all[layer_id, 0])
        mlp_in = low(normed * gains_all[layer_id, 1] + shifts_all[layer_id, 1])
        qkv_pre = low_back(jnp.einsum('ld,dcf->lcf', attn_in, qkv_full[layer_id], precision=highest) + qkv_shift[layer_id])
        shaped = qkv_pre.reshape(length, 3, H, HD)
        queries = low(rotate(shaped[:, 0], cosine_table, sine_table))
        key_rows = low(rotate(shaped[:, 1], cosine_table, sine_table))
        values = low(shaped[:, 2])
        scores = low_back(jnp.einsum('qhe,khe->hqk', queries, key_rows, precision=highest) * HD ** (-0.5))
        scores = jnp.where(allowed[None], scores, masked_score)
        row_peak = lax.optimization_barrier(jnp.max(scores, axis=-1, keepdims=True))
        exponent = jnp.exp(scores - row_peak)
        probs_full = exponent / lax.optimization_barrier(jnp.sum(exponent, axis=-1, keepdims=True))
        heads_out = low_back(low(jnp.einsum('hqk,khe->qhe', low(probs_full), values, precision=highest)))
        attn_part = jnp.dot(heads_out.reshape(length, D), proj_full[layer_id], precision=highest)
        up_pre = low_back(jnp.dot(mlp_in, up_full[layer_id], precision=highest) + up_shift[layer_id])
        act_low = low(gelu_exact(up_pre))
        mlp_part = jnp.dot(act_low, down_full[layer_id], precision=highest)
        stream = stream + low_back(attn_part + mlp_part) + shifts_all[layer_id, 2] + shifts_all[layer_id, 3]
    return stream

def orthogonal(matrix):
    current = matrix / (jnp.sqrt(jnp.sum(matrix * matrix)) + frobenius_eps)
    for iteration in range(NS_ITERS):
        gram_now = jnp.dot(current, current.T, precision=highest)
        polynomial = coef_second * gram_now + coef_third * jnp.dot(gram_now, gram_now, precision=highest)
        current = coef_first * current + jnp.dot(polynomial, current, precision=highest)
    return current

def vector_step(params, gradients):
    return params - vector_rate * gradients * lax.rsqrt(lax.optimization_barrier(jnp.mean(gradients * gradients, axis=-1, keepdims=True)) + vector_eps)

def reference(block_input, cotangent, segments, qkv_weight, proj_weight, up_weight, down_weight, norm_gains, biases, qkv_bias, up_bias, qkv_state, proj_state, up_state, down_state):

    def forward(inputs, qkv_full, proj_full, up_full, down_full, gains_all, shifts_all, qkv_shift, up_shift):

        def one_row(carried):
            return forward_row(carried[0], carried[1], qkv_full, proj_full, up_full, down_full, gains_all, shifts_all, qkv_shift, up_shift)
        row_blocks = inputs.reshape(ROWS, TOK_DP, D)
        return lax.map(jax.checkpoint(one_row), (row_blocks, segments)).reshape(TOKENS, D)
    floats = tuple((argument.astype(jnp.float32) for argument in (block_input, qkv_weight, proj_weight, up_weight, down_weight, norm_gains, biases, qkv_bias, up_bias)))
    block_output, pullback = jax.vjp(forward, *floats)
    input_grad, qkv_grad, proj_grad, up_grad, down_grad, gains_grad, biases_grad, qkv_bias_grad, up_bias_grad = pullback(cotangent.astype(jnp.float32))
    qkv_state_new = momentum * qkv_state + qkv_grad
    proj_state_new = momentum * proj_state + proj_grad
    up_state_new = momentum * up_state + up_grad
    down_state_new = momentum * down_state + down_grad
    muon_step = muon_rate * match_rms
    qkv_ortho = jnp.stack([orthogonal(qkv_state_new[layer_id].reshape(D, 3 * D)).reshape(D, 3, D) for layer_id in range(LAYERS)])
    proj_ortho = jnp.stack([orthogonal(proj_state_new[layer_id].T).T for layer_id in range(LAYERS)])
    up_ortho = jnp.stack([orthogonal(up_state_new[layer_id]) for layer_id in range(LAYERS)])
    down_ortho = jnp.stack([orthogonal(down_state_new[layer_id].T).T for layer_id in range(LAYERS)])
    qkv_new = qkv_weight.astype(jnp.float32) - muon_step * math.sqrt(3 * D) * qkv_ortho
    proj_new = proj_weight.astype(jnp.float32) - muon_step * math.sqrt(D) * proj_ortho
    up_new = up_weight.astype(jnp.float32) - muon_step * math.sqrt(FF) * up_ortho
    down_new = down_weight.astype(jnp.float32) - muon_step * math.sqrt(FF) * down_ortho
    gains_new = vector_step(norm_gains, gains_grad)
    biases_new = vector_step(biases, biases_grad)
    qkv_bias_new = vector_step(qkv_bias, qkv_bias_grad)
    up_bias_new = vector_step(up_bias, up_bias_grad)
    return (block_output, input_grad, qkv_grad, proj_grad, up_grad, down_grad, gains_grad, biases_grad, qkv_bias_grad, up_bias_grad, qkv_new, proj_new, up_new, down_new, gains_new, biases_new, qkv_bias_new, up_bias_new, qkv_state_new, proj_state_new, up_state_new, down_state_new)
```

```python
import math

import jax
import jax.numpy as jnp
from jax import lax
from jax.sharding import PartitionSpec as P

D = 768
HD = 64
FF = 3072
ROT = 16
LAYERS = 2
NS_ITERS = 5


highest = lax.Precision.HIGHEST
ns_precision = lax.Precision.HIGH
norm_eps = 1e-05
masked_score = -1e30
coef_first = 3.4445
coef_second = -4.775
coef_third = 2.0315
momentum = 0.9
muon_rate = 0.2
match_rms = 0.2
vector_rate = 0.2
vector_eps = 1e-06
frobenius_eps = 1e-07


def rotary_tables(segment_row):
    length = segment_row.shape[0]
    indices = jnp.arange(length, dtype=jnp.int32)
    change = jnp.concatenate([jnp.ones((1,), dtype=bool), segment_row[1:] != segment_row[:-1]])
    starts = lax.cummax(jnp.where(change, indices, jnp.zeros_like(indices)), axis=0)
    positions = (indices - starts).astype(jnp.float32)
    half_rot = ROT // 2
    frequency = 10000.0 ** (-2.0 * jnp.arange(half_rot, dtype=jnp.float32) / ROT)
    angles = positions[:, None] * frequency[None, :]
    return (jnp.cos(angles), jnp.sin(angles))


def rotate(values, cosine_table, sine_table):
    half_rot = ROT // 2
    first_half = values[..., :half_rot]
    second_half = values[..., half_rot:ROT]
    cos_b = cosine_table[:, None, :]
    sin_b = sine_table[:, None, :]
    return jnp.concatenate(
        [
            first_half * cos_b - second_half * sin_b,
            second_half * cos_b + first_half * sin_b,
            values[..., ROT:],
        ],
        axis=-1,
    )


def unrotate(gradient, cosine_table, sine_table):
    half_rot = ROT // 2
    first_half = gradient[..., :half_rot]
    second_half = gradient[..., half_rot:ROT]
    cos_b = cosine_table[:, None, :]
    sin_b = sine_table[:, None, :]
    return jnp.concatenate(
        [
            first_half * cos_b + second_half * sin_b,
            second_half * cos_b - first_half * sin_b,
            gradient[..., ROT:],
        ],
        axis=-1,
    )


def normalize(stream):
    centered = stream - jnp.mean(stream, axis=-1, keepdims=True)
    inverse = lax.rsqrt(jnp.mean(centered * centered, axis=-1, keepdims=True) + norm_eps)
    return (centered * inverse, inverse)


def gelu_exact(values):
    return jax.nn.gelu(values, approximate=False)


def block_mask(segment_row, block_rows):
    query_pos = jnp.arange(block_rows, dtype=jnp.int32)
    key_pos = jnp.arange(segment_row.shape[0], dtype=jnp.int32)
    return (segment_row[:, None] == segment_row[None, :]) & (query_pos[:, None] >= key_pos[None, :])


def block_scores(queries, key_rows, allowed):
    scores = jnp.einsum(
        "qhe,khe->hqk", queries, key_rows, preferred_element_type=jnp.float32
    ) * queries.shape[-1] ** (-0.5)
    return jnp.where(allowed[None], scores, masked_score)


def attend(queries, key_rows, values, segment_row):
    length = queries.shape[0]
    block_rows = min(512, length)
    allowed = block_mask(segment_row, block_rows)
    scores = block_scores(queries, key_rows, allowed)
    row_peak = jnp.max(scores, axis=-1, keepdims=True)
    exponent = jnp.exp(scores - row_peak)
    row_total = jnp.sum(exponent, axis=-1, keepdims=True)
    probs_low = (exponent / row_total).astype(jnp.bfloat16)
    outputs = jnp.einsum(
        "hqk,khe->qhe", probs_low, values, preferred_element_type=jnp.float32
    ).astype(jnp.bfloat16)
    log_sums = row_peak + jnp.log(row_total)
    return (outputs, log_sums)


def attend_back(queries, key_rows, values, heads_grad, log_sums, segment_row):
    length = queries.shape[0]
    block_rows = min(512, length)
    scale_factor = queries.shape[-1] ** (-0.5)
    allowed = block_mask(segment_row, block_rows)
    scores = block_scores(queries, key_rows, allowed)
    probs_full = jnp.exp(scores - log_sums)
    probs_grad = jnp.einsum("qhe,khe->hqk", heads_grad, values, preferred_element_type=jnp.float32)
    row_dot = jnp.sum(probs_full * probs_grad, axis=-1, keepdims=True)
    score_grad = (probs_full * (probs_grad - row_dot)).astype(jnp.bfloat16)
    value_grad = jnp.einsum(
        "hqk,qhe->khe",
        probs_full.astype(jnp.bfloat16),
        heads_grad,
        preferred_element_type=jnp.float32,
    )
    query_grads = (
        jnp.einsum("hqk,khe->qhe", score_grad, key_rows, preferred_element_type=jnp.float32)
        * scale_factor
    )
    key_grad = (
        jnp.einsum("hqk,qhe->khe", score_grad, queries, preferred_element_type=jnp.float32)
        * scale_factor
    )
    return (query_grads, key_grad, value_grad)


def dp_scatter(partial, dimension):
    return lax.psum_scatter(partial, "dp", scatter_dimension=dimension, tiled=True)


def vector_step(params, gradients):
    return params - vector_rate * gradients * lax.rsqrt(
        jnp.mean(gradients * gradients, axis=-1, keepdims=True) + vector_eps
    )


def local(
    block_input,
    cotangent,
    segments,
    qkv_weight,
    proj_weight,
    up_weight,
    down_weight,
    norm_gains,
    biases,
    qkv_bias,
    up_bias,
    qkv_state,
    proj_state,
    up_state,
    down_state,
):
    tensor_rank = lax.axis_index("tensor")
    local_width = qkv_weight.shape[3]
    local_hidden = up_weight.shape[2]
    head_count = local_width // HD
    model_width = block_input.shape[1]
    segment_row = segments[0]
    cosine_table, sine_table = rotary_tables(segment_row)
    stream = block_input.astype(jnp.float32)
    saved_layers = []
    for layer_id in range(LAYERS):
        layer_weights = (
            lax.all_gather(qkv_weight[layer_id], "dp", axis=0, tiled=True),
            lax.all_gather(proj_weight[layer_id], "dp", axis=1, tiled=True),
            lax.all_gather(up_weight[layer_id], "dp", axis=0, tiled=True),
            lax.all_gather(down_weight[layer_id], "dp", axis=1, tiled=True),
        )
        qkv_full, proj_full, up_full, down_full = layer_weights
        normed, inverse = normalize(stream)
        attn_rows = (normed * norm_gains[layer_id, 0] + biases[layer_id, 0]).astype(jnp.bfloat16)
        mlp_rows = (normed * norm_gains[layer_id, 1] + biases[layer_id, 1]).astype(jnp.bfloat16)
        attn_in, mlp_in = (
            lax.all_gather(attn_rows, "tensor", axis=0, tiled=True),
            lax.all_gather(mlp_rows, "tensor", axis=0, tiled=True),
        )
        length = attn_in.shape[0]
        qkv_local_bias = lax.dynamic_slice_in_dim(
            qkv_bias[layer_id], tensor_rank * local_width, local_width, 1
        )
        qkv_pre = (
            jnp.einsum("ld,dcf->lcf", attn_in, qkv_full, preferred_element_type=jnp.float32)
            + qkv_local_bias
        )
        shaped = qkv_pre.reshape(length, 3, head_count, HD)
        queries = rotate(shaped[:, 0], cosine_table, sine_table).astype(jnp.bfloat16)
        key_rows = rotate(shaped[:, 1], cosine_table, sine_table).astype(jnp.bfloat16)
        values = shaped[:, 2].astype(jnp.bfloat16)
        heads_out, log_sums = attend(queries, key_rows, values, segment_row)
        heads_flat = heads_out.reshape(length, local_width)
        up_local_bias = lax.dynamic_slice_in_dim(
            up_bias[layer_id], tensor_rank * local_hidden, local_hidden, 0
        )
        up_pre = jnp.dot(mlp_in, up_full, preferred_element_type=jnp.float32) + up_local_bias
        act_low = gelu_exact(up_pre).astype(jnp.bfloat16)
        partial_sum = jnp.dot(heads_flat, proj_full, preferred_element_type=jnp.float32) + jnp.dot(
            act_low, down_full, preferred_element_type=jnp.float32
        )
        branch = lax.psum_scatter(partial_sum, "tensor", scatter_dimension=0, tiled=True)
        saved_layers.append(
            (
                normed,
                inverse,
                attn_in,
                mlp_in,
                queries,
                key_rows,
                values,
                log_sums,
                heads_flat,
                up_pre,
                act_low,
                layer_weights,
            )
        )
        stream = stream + branch + biases[layer_id, 2] + biases[layer_id, 3]
    grad_stream = cotangent.astype(jnp.float32)
    gains_list = [None] * LAYERS
    biases_list = [None] * LAYERS
    qkv_bias_list = [None] * LAYERS
    up_bias_list = [None] * LAYERS
    weight_list = [None] * LAYERS
    for layer_id in reversed(range(LAYERS)):
        (
            normed,
            inverse,
            attn_in,
            mlp_in,
            queries,
            key_rows,
            values,
            log_sums,
            heads_flat,
            up_pre,
            act_low,
            layer_weights,
        ) = saved_layers[layer_id]
        layer_weights = (
            lax.all_gather(qkv_weight[layer_id], "dp", axis=0, tiled=True),
            lax.all_gather(proj_weight[layer_id], "dp", axis=1, tiled=True),
            lax.all_gather(up_weight[layer_id], "dp", axis=0, tiled=True),
            lax.all_gather(down_weight[layer_id], "dp", axis=1, tiled=True),
        )
        qkv_full, proj_full, up_full, down_full = layer_weights
        length = attn_in.shape[0]
        out_bias_grad = jnp.sum(grad_stream, axis=0)
        branch_grad = lax.all_gather(grad_stream.astype(jnp.bfloat16), "tensor", axis=0, tiled=True)
        down_part = jnp.einsum(
            "lf,ld->fd", act_low, branch_grad, preferred_element_type=jnp.float32
        )
        act_grad = jnp.einsum(
            "ld,fd->lf", branch_grad, down_full, preferred_element_type=jnp.float32
        )
        gelu_back = jax.vjp(gelu_exact, up_pre)[1]
        up_pre_grad = gelu_back(act_grad)[0].astype(jnp.bfloat16)
        up_bias_part = jnp.sum(up_pre_grad, axis=0, dtype=jnp.float32)
        up_part = jnp.einsum("ld,lf->df", mlp_in, up_pre_grad, preferred_element_type=jnp.float32)
        mlp_in_grad = jnp.einsum(
            "lf,df->ld", up_pre_grad, up_full, preferred_element_type=jnp.float32
        )
        proj_part = jnp.einsum(
            "lf,ld->fd", heads_flat, branch_grad, preferred_element_type=jnp.float32
        )
        heads_grad = (
            jnp.einsum("ld,fd->lf", branch_grad, proj_full, preferred_element_type=jnp.float32)
            .astype(jnp.bfloat16)
            .reshape(length, head_count, HD)
        )
        query_grad, key_grad, value_grad = attend_back(
            queries, key_rows, values, heads_grad, log_sums, segment_row
        )
        qkv_pre_grad = jnp.stack(
            [
                unrotate(query_grad, cosine_table, sine_table),
                unrotate(key_grad, cosine_table, sine_table),
                value_grad,
            ],
            axis=1,
        )
        qkv_pre_grad = qkv_pre_grad.reshape(length, 3, local_width).astype(jnp.bfloat16)
        qkv_bias_part = jnp.sum(qkv_pre_grad, axis=0, dtype=jnp.float32)
        qkv_part = jnp.einsum(
            "ld,lcf->dcf", attn_in, qkv_pre_grad, preferred_element_type=jnp.float32
        )
        attn_in_grad = jnp.einsum(
            "lcf,dcf->ld", qkv_pre_grad, qkv_full, preferred_element_type=jnp.float32
        )
        attn_rows_grad, mlp_rows_grad = (
            lax.psum_scatter(attn_in_grad, "tensor", scatter_dimension=0, tiled=True),
            lax.psum_scatter(mlp_in_grad, "tensor", scatter_dimension=0, tiled=True),
        )
        gains_list[layer_id] = jnp.stack(
            [jnp.sum(attn_rows_grad * normed, axis=0), jnp.sum(mlp_rows_grad * normed, axis=0)]
        )
        biases_list[layer_id] = jnp.stack(
            [
                jnp.sum(attn_rows_grad, axis=0),
                jnp.sum(mlp_rows_grad, axis=0),
                out_bias_grad,
                out_bias_grad,
            ]
        )
        qkv_bias_list[layer_id] = lax.dynamic_update_slice_in_dim(
            jnp.zeros((3, model_width), jnp.float32), qkv_bias_part, tensor_rank * local_width, 1
        )
        up_bias_list[layer_id] = lax.dynamic_update_slice_in_dim(
            jnp.zeros((up_bias.shape[1],), jnp.float32), up_bias_part, tensor_rank * local_hidden, 0
        )
        normed_grad = (
            attn_rows_grad * norm_gains[layer_id, 0] + mlp_rows_grad * norm_gains[layer_id, 1]
        )
        normed_mean = jnp.mean(normed_grad, axis=-1, keepdims=True)
        product_mean = jnp.mean(normed_grad * normed, axis=-1, keepdims=True)
        grad_stream = grad_stream + inverse * (normed_grad - normed_mean - normed * product_mean)
        weight_list[layer_id] = (
            dp_scatter(qkv_part, 0),
            dp_scatter(proj_part, 1),
            dp_scatter(up_part, 0),
            dp_scatter(down_part, 1),
        )
    gains_grad, biases_grad, qkv_bias_grad, up_bias_grad = lax.psum(
        (
            jnp.stack(gains_list),
            jnp.stack(biases_list),
            jnp.stack(qkv_bias_list),
            jnp.stack(up_bias_list),
        ),
        ("dp", "tensor"),
    )
    qkv_grad = jnp.stack([weight_list[layer_id][0] for layer_id in range(LAYERS)])
    proj_grad = jnp.stack([weight_list[layer_id][1] for layer_id in range(LAYERS)])
    up_grad = jnp.stack([weight_list[layer_id][2] for layer_id in range(LAYERS)])
    down_grad = jnp.stack([weight_list[layer_id][3] for layer_id in range(LAYERS)])
    qkv_state_new = momentum * qkv_state + qkv_grad
    proj_state_new = momentum * proj_state + proj_grad
    up_state_new = momentum * up_state + up_grad
    down_state_new = momentum * down_state + down_grad
    rows_local = qkv_state.shape[1]
    dp_count = lax.axis_size("dp")
    dp_rank = lax.axis_index("dp")
    slot_count = 4 * LAYERS
    sub = dp_count // slot_count
    piece_width = up_state.shape[2] // sub
    slot_mats = []
    for layer_id in range(LAYERS):
        slot_mats.append(qkv_state_new[layer_id].reshape(rows_local, 3 * local_width))
        slot_mats.append(proj_state_new[layer_id].T)
        slot_mats.append(up_state_new[layer_id])
        slot_mats.append(down_state_new[layer_id].T)
    pieces = []
    for mat in slot_mats:
        width = mat.shape[1] // sub
        split = mat.reshape(rows_local, sub, width).transpose(1, 0, 2)
        pieces.append(jnp.pad(split, ((0, 0), (0, 0), (0, piece_width - width))))
    outgoing = jnp.concatenate(pieces, axis=0)
    owned = lax.all_to_all(outgoing, "dp", split_axis=0, concat_axis=0, tiled=True)
    owned = owned.reshape(dp_count * rows_local, piece_width)
    gram = jnp.dot(owned, owned.T, precision=ns_precision)
    bit = 1
    while bit < sub:
        pairs = [(i, i ^ bit) for i in range(dp_count)]
        gram = gram + lax.ppermute(gram, "dp", pairs)
        bit *= 2
    gram = gram + lax.ppermute(gram, "tensor", [(0, 1), (1, 0)])
    norm_sq = jnp.trace(gram)
    scale = 1.0 / (jnp.sqrt(norm_sq) + frobenius_eps)
    current_gram = gram * (scale * scale)
    identity = jnp.eye(current_gram.shape[0], dtype=jnp.float32)
    accumulated = None
    for iteration in range(NS_ITERS):
        squared = jnp.dot(current_gram, current_gram, precision=ns_precision)
        polynomial = coef_first * identity + coef_second * current_gram + coef_third * squared
        if accumulated is None:
            accumulated = polynomial
        else:
            accumulated = jnp.dot(polynomial, accumulated, precision=ns_precision)
        if iteration + 1 < NS_ITERS:
            current_gram = jnp.dot(
                polynomial,
                jnp.dot(current_gram, polynomial, precision=ns_precision),
                precision=ns_precision,
            )
    current = jnp.dot(accumulated, owned * scale, precision=ns_precision)
    returned = lax.all_to_all(
        current.reshape(dp_count, rows_local, piece_width),
        "dp",
        split_axis=0,
        concat_axis=0,
        tiled=True,
    ).reshape(slot_count, sub, rows_local, piece_width)
    my_rows = []
    for slot_id, mat in enumerate(slot_mats):
        width = mat.shape[1] // sub
        my_rows.append(returned[slot_id, :, :, :width].transpose(1, 0, 2).reshape(rows_local, sub * width))
    muon_step = muon_rate * match_rms
    qkv_list, proj_list, up_list, down_list = ([], [], [], [])
    for layer_id in range(LAYERS):
        base_slot = 4 * layer_id
        qkv_ortho = my_rows[base_slot].reshape(rows_local, 3, local_width)
        proj_ortho = my_rows[base_slot + 1].T
        up_ortho = my_rows[base_slot + 2]
        down_ortho = my_rows[base_slot + 3].T
        qkv_list.append(
            qkv_weight[layer_id].astype(jnp.float32) - muon_step * math.sqrt(3 * D) * qkv_ortho
        )
        proj_list.append(
            proj_weight[layer_id].astype(jnp.float32) - muon_step * math.sqrt(D) * proj_ortho
        )
        up_list.append(
            up_weight[layer_id].astype(jnp.float32) - muon_step * math.sqrt(FF) * up_ortho
        )
        down_list.append(
            down_weight[layer_id].astype(jnp.float32) - muon_step * math.sqrt(FF) * down_ortho
        )
    qkv_new = jnp.stack(qkv_list)
    proj_new = jnp.stack(proj_list)
    up_new = jnp.stack(up_list)
    down_new = jnp.stack(down_list)
    gains_new = vector_step(norm_gains, gains_grad)
    biases_new = vector_step(biases, biases_grad)
    qkv_bias_new = vector_step(qkv_bias, qkv_bias_grad)
    up_bias_new = vector_step(up_bias, up_bias_grad)
    return (
        stream,
        grad_stream,
        qkv_grad,
        proj_grad,
        up_grad,
        down_grad,
        gains_grad,
        biases_grad,
        qkv_bias_grad,
        up_bias_grad,
        qkv_new,
        proj_new,
        up_new,
        down_new,
        gains_new,
        biases_new,
        qkv_bias_new,
        up_bias_new,
        qkv_state_new,
        proj_state_new,
        up_state_new,
        down_state_new,
    )


def solution(mesh):
    return jax.shard_map(
        local,
        mesh=mesh,
        in_specs=(
            P(("dp", "tensor"), None),
            P(("dp", "tensor"), None),
            P("dp", None),
            P(None, "dp", None, "tensor"),
            P(None, "tensor", "dp"),
            P(None, "dp", "tensor"),
            P(None, "tensor", "dp"),
            P(),
            P(),
            P(),
            P(),
            P(None, "dp", None, "tensor"),
            P(None, "tensor", "dp"),
            P(None, "dp", "tensor"),
            P(None, "tensor", "dp"),
        ),
        out_specs=(
            P(("dp", "tensor"), None),
            P(("dp", "tensor"), None),
            P(None, "dp", None, "tensor"),
            P(None, "tensor", "dp"),
            P(None, "dp", "tensor"),
            P(None, "tensor", "dp"),
            P(),
            P(),
            P(),
            P(),
            P(None, "dp", None, "tensor"),
            P(None, "tensor", "dp"),
            P(None, "dp", "tensor"),
            P(None, "tensor", "dp"),
            P(),
            P(),
            P(),
            P(),
            P(None, "dp", None, "tensor"),
            P(None, "tensor", "dp"),
            P(None, "dp", "tensor"),
            P(None, "tensor", "dp"),
        ),
        check_vma=False,
    )
```

```python
import math

import jax
import jax.numpy as jnp
from jax import lax
from jax.sharding import PartitionSpec as P

D = 768
HD = 64
FF = 3072
ROT = 16
LAYERS = 2
NS_ITERS = 5


highest = lax.Precision.HIGHEST
ns_precision = lax.Precision.HIGH
norm_eps = 1e-05
masked_score = -1e30
coef_first = 3.4445
coef_second = -4.775
coef_third = 2.0315
momentum = 0.9
muon_rate = 0.2
match_rms = 0.2
vector_rate = 0.2
vector_eps = 1e-06
frobenius_eps = 1e-07


def rotary_tables(segment_row):
    length = segment_row.shape[0]
    indices = jnp.arange(length, dtype=jnp.int32)
    change = jnp.concatenate([jnp.ones((1,), dtype=bool), segment_row[1:] != segment_row[:-1]])
    starts = lax.cummax(jnp.where(change, indices, jnp.zeros_like(indices)), axis=0)
    positions = (indices - starts).astype(jnp.float32)
    half_rot = ROT // 2
    frequency = 10000.0 ** (-2.0 * jnp.arange(half_rot, dtype=jnp.float32) / ROT)
    angles = positions[:, None] * frequency[None, :]
    return (jnp.cos(angles), jnp.sin(angles))


def rotate(values, cosine_table, sine_table):
    half_rot = ROT // 2
    first_half = values[..., :half_rot]
    second_half = values[..., half_rot:ROT]
    cos_b = cosine_table[:, None, :]
    sin_b = sine_table[:, None, :]
    return jnp.concatenate(
        [
            first_half * cos_b - second_half * sin_b,
            second_half * cos_b + first_half * sin_b,
            values[..., ROT:],
        ],
        axis=-1,
    )


def unrotate(gradient, cosine_table, sine_table):
    half_rot = ROT // 2
    first_half = gradient[..., :half_rot]
    second_half = gradient[..., half_rot:ROT]
    cos_b = cosine_table[:, None, :]
    sin_b = sine_table[:, None, :]
    return jnp.concatenate(
        [
            first_half * cos_b + second_half * sin_b,
            second_half * cos_b - first_half * sin_b,
            gradient[..., ROT:],
        ],
        axis=-1,
    )


def normalize(stream):
    centered = stream - jnp.mean(stream, axis=-1, keepdims=True)
    inverse = lax.rsqrt(jnp.mean(centered * centered, axis=-1, keepdims=True) + norm_eps)
    return (centered * inverse, inverse)


def gelu_exact(values):
    return jax.nn.gelu(values, approximate=False)


def block_mask(segment_row, block_rows):
    query_pos = jnp.arange(block_rows, dtype=jnp.int32)
    key_pos = jnp.arange(segment_row.shape[0], dtype=jnp.int32)
    return (segment_row[:, None] == segment_row[None, :]) & (query_pos[:, None] >= key_pos[None, :])


def block_scores(queries, key_rows, allowed):
    scores = jnp.einsum(
        "qhe,khe->hqk", queries, key_rows, preferred_element_type=jnp.float32
    ) * queries.shape[-1] ** (-0.5)
    return jnp.where(allowed[None], scores, masked_score)


def attend(queries, key_rows, values, segment_row):
    length = queries.shape[0]
    block_rows = min(512, length)
    allowed = block_mask(segment_row, block_rows)
    scores = block_scores(queries, key_rows, allowed)
    row_peak = jnp.max(scores, axis=-1, keepdims=True)
    exponent = jnp.exp(scores - row_peak)
    row_total = jnp.sum(exponent, axis=-1, keepdims=True)
    probs_low = (exponent / row_total).astype(jnp.bfloat16)
    outputs = jnp.einsum(
        "hqk,khe->qhe", probs_low, values, preferred_element_type=jnp.float32
    ).astype(jnp.bfloat16)
    log_sums = row_peak + jnp.log(row_total)
    return (outputs, log_sums)


def attend_back(queries, key_rows, values, heads_grad, log_sums, segment_row):
    length = queries.shape[0]
    block_rows = min(512, length)
    scale_factor = queries.shape[-1] ** (-0.5)
    allowed = block_mask(segment_row, block_rows)
    scores = block_scores(queries, key_rows, allowed)
    probs_full = jnp.exp(scores - log_sums)
    probs_grad = jnp.einsum("qhe,khe->hqk", heads_grad, values, preferred_element_type=jnp.float32)
    row_dot = jnp.sum(probs_full * probs_grad, axis=-1, keepdims=True)
    score_grad = (probs_full * (probs_grad - row_dot)).astype(jnp.bfloat16)
    value_grad = jnp.einsum(
        "hqk,qhe->khe",
        probs_full.astype(jnp.bfloat16),
        heads_grad,
        preferred_element_type=jnp.float32,
    )
    query_grads = (
        jnp.einsum("hqk,khe->qhe", score_grad, key_rows, preferred_element_type=jnp.float32)
        * scale_factor
    )
    key_grad = (
        jnp.einsum("hqk,qhe->khe", score_grad, queries, preferred_element_type=jnp.float32)
        * scale_factor
    )
    return (query_grads, key_grad, value_grad)


def dp_scatter(partial, dimension):
    return lax.psum_scatter(partial, "dp", scatter_dimension=dimension, tiled=True)


def dp_gather(block, axis):
    return lax.all_gather(block, "dp", axis=axis, tiled=True)


def a2a_gather(block, axis):
    count = lax.axis_size("dp")
    copies = jnp.broadcast_to(block[None], (count,) + block.shape)
    got = lax.all_to_all(copies, "dp", split_axis=0, concat_axis=0, tiled=True)
    got = jnp.moveaxis(got, 0, axis)
    return got.reshape(block.shape[:axis] + (count * block.shape[axis],) + block.shape[axis + 1 :])


def a2a_scatter(partial, dimension):
    count = lax.axis_size("dp")
    shape = partial.shape
    chunks = partial.reshape(shape[:dimension] + (count, shape[dimension] // count) + shape[dimension + 1 :])
    chunks = jnp.moveaxis(chunks, dimension, 0)
    got = lax.all_to_all(chunks, "dp", split_axis=0, concat_axis=0, tiled=True)
    return jnp.sum(got, axis=0)


def swap_pairs(count, bit):
    return [(i, i ^ bit) for i in range(count)]


def butterfly_sum(flat):
    count = lax.axis_size("dp")
    bit = 1
    while bit < count:
        flat = flat + lax.ppermute(flat, "dp", swap_pairs(count, bit))
        bit *= 2
    return flat + lax.ppermute(flat, "tensor", [(0, 1), (1, 0)])


def vector_step(params, gradients):
    return params - vector_rate * gradients * lax.rsqrt(
        jnp.mean(gradients * gradients, axis=-1, keepdims=True) + vector_eps
    )


def local(
    block_input,
    cotangent,
    segments,
    qkv_weight,
    proj_weight,
    up_weight,
    down_weight,
    norm_gains,
    biases,
    qkv_bias,
    up_bias,
    qkv_state,
    proj_state,
    up_state,
    down_state,
):
    tensor_rank = lax.axis_index("tensor")
    local_width = qkv_weight.shape[3]
    local_hidden = up_weight.shape[2]
    head_count = local_width // HD
    model_width = block_input.shape[1]
    segment_row = segments[0]
    cosine_table, sine_table = rotary_tables(segment_row)
    stream = block_input.astype(jnp.float32)
    saved_layers = []
    for layer_id in range(LAYERS):
        layer_weights = (
            a2a_gather(qkv_weight[layer_id], 0),
            a2a_gather(proj_weight[layer_id], 1),
            dp_gather(up_weight[layer_id], 0),
            dp_gather(down_weight[layer_id], 1),
        )
        qkv_full, proj_full, up_full, down_full = layer_weights
        normed, inverse = normalize(stream)
        attn_rows = (normed * norm_gains[layer_id, 0] + biases[layer_id, 0]).astype(jnp.bfloat16)
        mlp_rows = (normed * norm_gains[layer_id, 1] + biases[layer_id, 1]).astype(jnp.bfloat16)
        attn_in, mlp_in = (
            lax.all_gather(attn_rows, "tensor", axis=0, tiled=True),
            lax.all_gather(mlp_rows, "tensor", axis=0, tiled=True),
        )
        length = attn_in.shape[0]
        qkv_local_bias = lax.dynamic_slice_in_dim(
            qkv_bias[layer_id], tensor_rank * local_width, local_width, 1
        )
        qkv_pre = (
            jnp.einsum("ld,dcf->lcf", attn_in, qkv_full, preferred_element_type=jnp.float32)
            + qkv_local_bias
        )
        shaped = qkv_pre.reshape(length, 3, head_count, HD)
        queries = rotate(shaped[:, 0], cosine_table, sine_table).astype(jnp.bfloat16)
        key_rows = rotate(shaped[:, 1], cosine_table, sine_table).astype(jnp.bfloat16)
        values = shaped[:, 2].astype(jnp.bfloat16)
        heads_out, log_sums = attend(queries, key_rows, values, segment_row)
        heads_flat = heads_out.reshape(length, local_width)
        up_local_bias = lax.dynamic_slice_in_dim(
            up_bias[layer_id], tensor_rank * local_hidden, local_hidden, 0
        )
        up_pre = jnp.dot(mlp_in, up_full, preferred_element_type=jnp.float32) + up_local_bias
        act_low = gelu_exact(up_pre).astype(jnp.bfloat16)
        partial_sum = jnp.dot(heads_flat, proj_full, preferred_element_type=jnp.float32) + jnp.dot(
            act_low, down_full, preferred_element_type=jnp.float32
        )
        branch = lax.psum_scatter(partial_sum, "tensor", scatter_dimension=0, tiled=True)
        saved_layers.append(
            (
                normed,
                inverse,
                attn_in,
                mlp_in,
                queries,
                key_rows,
                values,
                log_sums,
                heads_flat,
                up_pre,
                act_low,
                layer_weights,
            )
        )
        stream = stream + branch + biases[layer_id, 2] + biases[layer_id, 3]
    grad_stream = cotangent.astype(jnp.float32)
    gains_list = [None] * LAYERS
    biases_list = [None] * LAYERS
    qkv_bias_list = [None] * LAYERS
    up_bias_list = [None] * LAYERS
    weight_list = [None] * LAYERS
    for layer_id in reversed(range(LAYERS)):
        (
            normed,
            inverse,
            attn_in,
            mlp_in,
            queries,
            key_rows,
            values,
            log_sums,
            heads_flat,
            up_pre,
            act_low,
            layer_weights,
        ) = saved_layers[layer_id]
        qkv_full, proj_full, up_full, down_full = layer_weights
        length = attn_in.shape[0]
        out_bias_grad = jnp.sum(grad_stream, axis=0)
        branch_grad = lax.all_gather(grad_stream.astype(jnp.bfloat16), "tensor", axis=0, tiled=True)
        down_part = jnp.einsum(
            "lf,ld->fd", act_low, branch_grad, preferred_element_type=jnp.float32
        )
        act_grad = jnp.einsum(
            "ld,fd->lf", branch_grad, down_full, preferred_element_type=jnp.float32
        )
        gelu_back = jax.vjp(gelu_exact, up_pre)[1]
        up_pre_grad = gelu_back(act_grad)[0].astype(jnp.bfloat16)
        up_bias_part = jnp.sum(up_pre_grad, axis=0, dtype=jnp.float32)
        up_part = jnp.einsum("ld,lf->df", mlp_in, up_pre_grad, preferred_element_type=jnp.float32)
        mlp_in_grad = jnp.einsum(
            "lf,df->ld", up_pre_grad, up_full, preferred_element_type=jnp.float32
        )
        proj_part = jnp.einsum(
            "lf,ld->fd", heads_flat, branch_grad, preferred_element_type=jnp.float32
        )
        heads_grad = (
            jnp.einsum("ld,fd->lf", branch_grad, proj_full, preferred_element_type=jnp.float32)
            .astype(jnp.bfloat16)
            .reshape(length, head_count, HD)
        )
        query_grad, key_grad, value_grad = attend_back(
            queries, key_rows, values, heads_grad, log_sums, segment_row
        )
        qkv_pre_grad = jnp.stack(
            [
                unrotate(query_grad, cosine_table, sine_table),
                unrotate(key_grad, cosine_table, sine_table),
                value_grad,
            ],
            axis=1,
        )
        qkv_pre_grad = qkv_pre_grad.reshape(length, 3, local_width).astype(jnp.bfloat16)
        qkv_bias_part = jnp.sum(qkv_pre_grad, axis=0, dtype=jnp.float32)
        qkv_part = jnp.einsum(
            "ld,lcf->dcf", attn_in, qkv_pre_grad, preferred_element_type=jnp.float32
        )
        attn_in_grad = jnp.einsum(
            "lcf,dcf->ld", qkv_pre_grad, qkv_full, preferred_element_type=jnp.float32
        )
        attn_rows_grad, mlp_rows_grad = (
            lax.psum_scatter(attn_in_grad, "tensor", scatter_dimension=0, tiled=True),
            lax.psum_scatter(mlp_in_grad, "tensor", scatter_dimension=0, tiled=True),
        )
        gains_list[layer_id] = jnp.stack(
            [jnp.sum(attn_rows_grad * normed, axis=0), jnp.sum(mlp_rows_grad * normed, axis=0)]
        )
        biases_list[layer_id] = jnp.stack(
            [
                jnp.sum(attn_rows_grad, axis=0),
                jnp.sum(mlp_rows_grad, axis=0),
                out_bias_grad,
                out_bias_grad,
            ]
        )
        qkv_bias_list[layer_id] = lax.dynamic_update_slice_in_dim(
            jnp.zeros((3, model_width), jnp.float32), qkv_bias_part, tensor_rank * local_width, 1
        )
        up_bias_list[layer_id] = lax.dynamic_update_slice_in_dim(
            jnp.zeros((up_bias.shape[1],), jnp.float32), up_bias_part, tensor_rank * local_hidden, 0
        )
        normed_grad = (
            attn_rows_grad * norm_gains[layer_id, 0] + mlp_rows_grad * norm_gains[layer_id, 1]
        )
        normed_mean = jnp.mean(normed_grad, axis=-1, keepdims=True)
        product_mean = jnp.mean(normed_grad * normed, axis=-1, keepdims=True)
        grad_stream = grad_stream + inverse * (normed_grad - normed_mean - normed * product_mean)
        weight_list[layer_id] = (
            a2a_scatter(qkv_part, 0),
            a2a_scatter(proj_part, 1),
            dp_scatter(up_part, 0),
            dp_scatter(down_part, 1),
        )
    small_parts = (
        jnp.stack(gains_list),
        jnp.stack(biases_list),
        jnp.stack(qkv_bias_list),
        jnp.stack(up_bias_list),
    )
    flat = butterfly_sum(jnp.concatenate([part.reshape(-1) for part in small_parts]))
    small_sums = []
    offset = 0
    for part in small_parts:
        small_sums.append(flat[offset : offset + part.size].reshape(part.shape))
        offset += part.size
    gains_grad, biases_grad, qkv_bias_grad, up_bias_grad = small_sums
    qkv_grad = jnp.stack([weight_list[layer_id][0] for layer_id in range(LAYERS)])
    proj_grad = jnp.stack([weight_list[layer_id][1] for layer_id in range(LAYERS)])
    up_grad = jnp.stack([weight_list[layer_id][2] for layer_id in range(LAYERS)])
    down_grad = jnp.stack([weight_list[layer_id][3] for layer_id in range(LAYERS)])
    qkv_state_new = momentum * qkv_state + qkv_grad
    proj_state_new = momentum * proj_state + proj_grad
    up_state_new = momentum * up_state + up_grad
    down_state_new = momentum * down_state + down_grad
    rows_local = qkv_state.shape[1]
    dp_count = lax.axis_size("dp")
    dp_rank = lax.axis_index("dp")
    slot_count = 4 * LAYERS
    sub = dp_count // slot_count
    piece_width = up_state.shape[2] // sub
    slot_mats = []
    for layer_id in range(LAYERS):
        slot_mats.append(qkv_state_new[layer_id].reshape(rows_local, 3 * local_width))
        slot_mats.append(proj_state_new[layer_id].T)
        slot_mats.append(up_state_new[layer_id])
        slot_mats.append(down_state_new[layer_id].T)
    pieces = []
    for mat in slot_mats:
        width = mat.shape[1] // sub
        split = mat.reshape(rows_local, sub, width).transpose(1, 0, 2)
        pieces.append(jnp.pad(split, ((0, 0), (0, 0), (0, piece_width - width))))
    outgoing = jnp.concatenate(pieces, axis=0)
    owned = lax.all_to_all(outgoing, "dp", split_axis=0, concat_axis=0, tiled=True)
    owned = owned.reshape(dp_count * rows_local, piece_width)
    gram = jnp.dot(owned, owned.T, precision=ns_precision)
    bit = 1
    while bit < sub:
        gram = gram + lax.ppermute(gram, "dp", swap_pairs(dp_count, bit))
        bit *= 2
    core_half = dp_rank % 2
    half_rows = gram.shape[0] // 2
    mine = lax.dynamic_slice_in_dim(gram, core_half * half_rows, half_rows, 0)
    mine = mine + lax.ppermute(mine, "tensor", [(0, 1), (1, 0)])
    other = lax.ppermute(mine, "dp", swap_pairs(dp_count, 1))
    gram = jnp.where(
        core_half == 0,
        jnp.concatenate([mine, other], axis=0),
        jnp.concatenate([other, mine], axis=0),
    )
    norm_sq = jnp.trace(gram)
    scale = 1.0 / (jnp.sqrt(norm_sq) + frobenius_eps)
    current_gram = gram * (scale * scale)
    identity = jnp.eye(current_gram.shape[0], dtype=jnp.float32)
    accumulated = None
    for iteration in range(NS_ITERS):
        squared = jnp.dot(current_gram, current_gram, precision=ns_precision)
        polynomial = coef_first * identity + coef_second * current_gram + coef_third * squared
        if accumulated is None:
            accumulated = polynomial
        else:
            accumulated = jnp.dot(polynomial, accumulated, precision=ns_precision)
        if iteration + 1 < NS_ITERS:
            current_gram = jnp.dot(
                polynomial,
                jnp.dot(current_gram, polynomial, precision=ns_precision),
                precision=ns_precision,
            )
    current = jnp.dot(accumulated, owned * scale, precision=ns_precision)
    returned = lax.all_to_all(
        current.reshape(dp_count, rows_local, piece_width),
        "dp",
        split_axis=0,
        concat_axis=0,
        tiled=True,
    ).reshape(slot_count, sub, rows_local, piece_width)
    my_rows = []
    for slot_id, mat in enumerate(slot_mats):
        width = mat.shape[1] // sub
        my_rows.append(returned[slot_id, :, :, :width].transpose(1, 0, 2).reshape(rows_local, sub * width))
    muon_step = muon_rate * match_rms
    qkv_list, proj_list, up_list, down_list = ([], [], [], [])
    for layer_id in range(LAYERS):
        base_slot = 4 * layer_id
        qkv_ortho = my_rows[base_slot].reshape(rows_local, 3, local_width)
        proj_ortho = my_rows[base_slot + 1].T
        up_ortho = my_rows[base_slot + 2]
        down_ortho = my_rows[base_slot + 3].T
        qkv_list.append(
            qkv_weight[layer_id].astype(jnp.float32) - muon_step * math.sqrt(3 * D) * qkv_ortho
        )
        proj_list.append(
            proj_weight[layer_id].astype(jnp.float32) - muon_step * math.sqrt(D) * proj_ortho
        )
        up_list.append(
            up_weight[layer_id].astype(jnp.float32) - muon_step * math.sqrt(FF) * up_ortho
        )
        down_list.append(
            down_weight[layer_id].astype(jnp.float32) - muon_step * math.sqrt(FF) * down_ortho
        )
    qkv_new = jnp.stack(qkv_list)
    proj_new = jnp.stack(proj_list)
    up_new = jnp.stack(up_list)
    down_new = jnp.stack(down_list)
    gains_new = vector_step(norm_gains, gains_grad)
    biases_new = vector_step(biases, biases_grad)
    qkv_bias_new = vector_step(qkv_bias, qkv_bias_grad)
    up_bias_new = vector_step(up_bias, up_bias_grad)
    return (
        stream,
        grad_stream,
        qkv_grad,
        proj_grad,
        up_grad,
        down_grad,
        gains_grad,
        biases_grad,
        qkv_bias_grad,
        up_bias_grad,
        qkv_new,
        proj_new,
        up_new,
        down_new,
        gains_new,
        biases_new,
        qkv_bias_new,
        up_bias_new,
        qkv_state_new,
        proj_state_new,
        up_state_new,
        down_state_new,
    )


def solution(mesh):
    return jax.shard_map(
        local,
        mesh=mesh,
        in_specs=(
            P(("dp", "tensor"), None),
            P(("dp", "tensor"), None),
            P("dp", None),
            P(None, "dp", None, "tensor"),
            P(None, "tensor", "dp"),
            P(None, "dp", "tensor"),
            P(None, "tensor", "dp"),
            P(),
            P(),
            P(),
            P(),
            P(None, "dp", None, "tensor"),
            P(None, "tensor", "dp"),
            P(None, "dp", "tensor"),
            P(None, "tensor", "dp"),
        ),
        out_specs=(
            P(("dp", "tensor"), None),
            P(("dp", "tensor"), None),
            P(None, "dp", None, "tensor"),
            P(None, "tensor", "dp"),
            P(None, "dp", "tensor"),
            P(None, "tensor", "dp"),
            P(),
            P(),
            P(),
            P(),
            P(None, "dp", None, "tensor"),
            P(None, "tensor", "dp"),
            P(None, "dp", "tensor"),
            P(None, "tensor", "dp"),
            P(),
            P(),
            P(),
            P(),
            P(None, "dp", None, "tensor"),
            P(None, "tensor", "dp"),
            P(None, "dp", "tensor"),
            P(None, "tensor", "dp"),
        ),
        check_vma=False,
    )
```

```python
import math

import jax
import jax.numpy as jnp
from jax import lax
from jax.sharding import PartitionSpec as P

D = 768
HD = 64
FF = 3072
ROT = 16
LAYERS = 2
NS_ITERS = 5


highest = lax.Precision.HIGHEST
ns_precision = lax.Precision.HIGH
norm_eps = 1e-05
masked_score = -1e30
coef_first = 3.4445
coef_second = -4.775
coef_third = 2.0315
momentum = 0.9
muon_rate = 0.2
match_rms = 0.2
vector_rate = 0.2
vector_eps = 1e-06
frobenius_eps = 1e-07


def rotary_tables(segment_row):
    length = segment_row.shape[0]
    indices = jnp.arange(length, dtype=jnp.int32)
    change = jnp.concatenate([jnp.ones((1,), dtype=bool), segment_row[1:] != segment_row[:-1]])
    starts = lax.cummax(jnp.where(change, indices, jnp.zeros_like(indices)), axis=0)
    positions = (indices - starts).astype(jnp.float32)
    half_rot = ROT // 2
    frequency = 10000.0 ** (-2.0 * jnp.arange(half_rot, dtype=jnp.float32) / ROT)
    angles = positions[:, None] * frequency[None, :]
    return (jnp.cos(angles), jnp.sin(angles))


def rotate(values, cosine_table, sine_table):
    half_rot = ROT // 2
    first_half = values[..., :half_rot]
    second_half = values[..., half_rot:ROT]
    cos_b = cosine_table[:, None, :]
    sin_b = sine_table[:, None, :]
    return jnp.concatenate(
        [
            first_half * cos_b - second_half * sin_b,
            second_half * cos_b + first_half * sin_b,
            values[..., ROT:],
        ],
        axis=-1,
    )


def unrotate(gradient, cosine_table, sine_table):
    half_rot = ROT // 2
    first_half = gradient[..., :half_rot]
    second_half = gradient[..., half_rot:ROT]
    cos_b = cosine_table[:, None, :]
    sin_b = sine_table[:, None, :]
    return jnp.concatenate(
        [
            first_half * cos_b + second_half * sin_b,
            second_half * cos_b - first_half * sin_b,
            gradient[..., ROT:],
        ],
        axis=-1,
    )


def normalize(stream):
    centered = stream - jnp.mean(stream, axis=-1, keepdims=True)
    inverse = lax.rsqrt(jnp.mean(centered * centered, axis=-1, keepdims=True) + norm_eps)
    return (centered * inverse, inverse)


def gelu_exact(values):
    return jax.nn.gelu(values, approximate=False)


def block_mask(segment_row, block_rows):
    query_pos = jnp.arange(block_rows, dtype=jnp.int32)
    key_pos = jnp.arange(segment_row.shape[0], dtype=jnp.int32)
    return (segment_row[:, None] == segment_row[None, :]) & (query_pos[:, None] >= key_pos[None, :])


def block_scores(queries, key_rows, allowed):
    scores = jnp.einsum(
        "qhe,khe->hqk", queries, key_rows, preferred_element_type=jnp.float32
    ) * queries.shape[-1] ** (-0.5)
    return jnp.where(allowed[None], scores, masked_score)


def attend(queries, key_rows, values, segment_row):
    length = queries.shape[0]
    block_rows = min(512, length)
    allowed = block_mask(segment_row, block_rows)
    scores = block_scores(queries, key_rows, allowed)
    row_peak = jnp.max(scores, axis=-1, keepdims=True)
    exponent = jnp.exp(scores - row_peak)
    row_total = jnp.sum(exponent, axis=-1, keepdims=True)
    probs_low = (exponent / row_total).astype(jnp.bfloat16)
    outputs = jnp.einsum(
        "hqk,khe->qhe", probs_low, values, preferred_element_type=jnp.float32
    ).astype(jnp.bfloat16)
    log_sums = row_peak + jnp.log(row_total)
    return (outputs, log_sums)


def attend_back(queries, key_rows, values, heads_grad, log_sums, segment_row):
    length = queries.shape[0]
    block_rows = min(512, length)
    scale_factor = queries.shape[-1] ** (-0.5)
    allowed = block_mask(segment_row, block_rows)
    scores = block_scores(queries, key_rows, allowed)
    probs_full = jnp.exp(scores - log_sums)
    probs_grad = jnp.einsum("qhe,khe->hqk", heads_grad, values, preferred_element_type=jnp.float32)
    row_dot = jnp.sum(probs_full * probs_grad, axis=-1, keepdims=True)
    score_grad = (probs_full * (probs_grad - row_dot)).astype(jnp.bfloat16)
    value_grad = jnp.einsum(
        "hqk,qhe->khe",
        probs_full.astype(jnp.bfloat16),
        heads_grad,
        preferred_element_type=jnp.float32,
    )
    query_grads = (
        jnp.einsum("hqk,khe->qhe", score_grad, key_rows, preferred_element_type=jnp.float32)
        * scale_factor
    )
    key_grad = (
        jnp.einsum("hqk,qhe->khe", score_grad, queries, preferred_element_type=jnp.float32)
        * scale_factor
    )
    return (query_grads, key_grad, value_grad)


def dp_scatter(partial, dimension):
    return lax.psum_scatter(partial, "dp", scatter_dimension=dimension, tiled=True)


def dp_gather(block, axis):
    return lax.all_gather(block, "dp", axis=axis, tiled=True)


def a2a_gather(block, axis):
    count = lax.axis_size("dp")
    copies = jnp.broadcast_to(block[None], (count,) + block.shape)
    got = lax.all_to_all(copies, "dp", split_axis=0, concat_axis=0, tiled=True)
    got = jnp.moveaxis(got, 0, axis)
    return got.reshape(block.shape[:axis] + (count * block.shape[axis],) + block.shape[axis + 1 :])


def a2a_scatter(partial, dimension):
    count = lax.axis_size("dp")
    shape = partial.shape
    chunks = partial.reshape(shape[:dimension] + (count, shape[dimension] // count) + shape[dimension + 1 :])
    chunks = jnp.moveaxis(chunks, dimension, 0)
    got = lax.all_to_all(chunks, "dp", split_axis=0, concat_axis=0, tiled=True)
    return jnp.sum(got, axis=0)


def swap_pairs(count, bit):
    return [(i, i ^ bit) for i in range(count)]


def butterfly_sum(flat):
    count = lax.axis_size("dp")
    bit = 1
    while bit < count:
        flat = flat + lax.ppermute(flat, "dp", swap_pairs(count, bit))
        bit *= 2
    return flat + lax.ppermute(flat, "tensor", [(0, 1), (1, 0)])


def chip_gather(block, gather_axis, split_axis):
    count = lax.axis_size("dp")
    parity = lax.axis_index("dp") % 2
    width = block.shape[split_axis] // 2
    halves = jnp.stack(
        [lax.slice_in_dim(block, 0, width, axis=split_axis), lax.slice_in_dim(block, width, 2 * width, axis=split_axis)]
    )
    outgoing = jnp.tile(halves, (count // 2,) + (1,) * block.ndim)
    got = lax.all_to_all(outgoing, "dp", split_axis=0, concat_axis=0, tiled=True)
    got = jnp.moveaxis(got, 0, gather_axis)
    shape = got.shape
    mine = got.reshape(shape[:gather_axis] + (shape[gather_axis] * shape[gather_axis + 1],) + shape[gather_axis + 2 :])
    theirs = lax.ppermute(mine, "dp", swap_pairs(count, 1))
    return jnp.where(
        parity == 0,
        jnp.concatenate([mine, theirs], axis=split_axis),
        jnp.concatenate([theirs, mine], axis=split_axis),
    )


def chip_scatter(partial, scatter_axis, split_axis):
    count = lax.axis_size("dp")
    parity = lax.axis_index("dp") % 2
    width = partial.shape[split_axis] // 2
    keep = lax.dynamic_slice_in_dim(partial, parity * width, width, split_axis)
    send = lax.dynamic_slice_in_dim(partial, (1 - parity) * width, width, split_axis)
    chip_sum = keep + lax.ppermute(send, "dp", swap_pairs(count, 1))
    shape = chip_sum.shape
    chunks = chip_sum.reshape(
        shape[:scatter_axis] + (count, shape[scatter_axis] // count) + shape[scatter_axis + 1 :]
    )
    chunks = jnp.moveaxis(chunks, scatter_axis, 0)
    got = lax.all_to_all(chunks, "dp", split_axis=0, concat_axis=0, tiled=True)
    got = got.reshape((count // 2, 2) + got.shape[1:])
    even = jnp.sum(got[:, 0], axis=0)
    odd = jnp.sum(got[:, 1], axis=0)
    return jnp.concatenate([even, odd], axis=split_axis)


def vector_step(params, gradients):
    return params - vector_rate * gradients * lax.rsqrt(
        jnp.mean(gradients * gradients, axis=-1, keepdims=True) + vector_eps
    )


def local(
    block_input,
    cotangent,
    segments,
    qkv_weight,
    proj_weight,
    up_weight,
    down_weight,
    norm_gains,
    biases,
    qkv_bias,
    up_bias,
    qkv_state,
    proj_state,
    up_state,
    down_state,
):
    tensor_rank = lax.axis_index("tensor")
    local_width = qkv_weight.shape[3]
    local_hidden = up_weight.shape[2]
    head_count = local_width // HD
    model_width = block_input.shape[1]
    segment_row = segments[0]
    cosine_table, sine_table = rotary_tables(segment_row)
    stream = block_input.astype(jnp.float32)
    saved_layers = []
    for layer_id in range(LAYERS):
        layer_weights = (
            chip_gather(qkv_weight[layer_id], 0, 2),
            chip_gather(proj_weight[layer_id], 1, 0),
            chip_gather(up_weight[layer_id], 0, 1),
            chip_gather(down_weight[layer_id], 1, 0),
        )
        qkv_full, proj_full, up_full, down_full = layer_weights
        normed, inverse = normalize(stream)
        attn_rows = (normed * norm_gains[layer_id, 0] + biases[layer_id, 0]).astype(jnp.bfloat16)
        mlp_rows = (normed * norm_gains[layer_id, 1] + biases[layer_id, 1]).astype(jnp.bfloat16)
        attn_in, mlp_in = (
            lax.all_gather(attn_rows, "tensor", axis=0, tiled=True),
            lax.all_gather(mlp_rows, "tensor", axis=0, tiled=True),
        )
        length = attn_in.shape[0]
        qkv_local_bias = lax.dynamic_slice_in_dim(
            qkv_bias[layer_id], tensor_rank * local_width, local_width, 1
        )
        qkv_pre = (
            jnp.einsum("ld,dcf->lcf", attn_in, qkv_full, preferred_element_type=jnp.float32)
            + qkv_local_bias
        )
        shaped = qkv_pre.reshape(length, 3, head_count, HD)
        queries = rotate(shaped[:, 0], cosine_table, sine_table).astype(jnp.bfloat16)
        key_rows = rotate(shaped[:, 1], cosine_table, sine_table).astype(jnp.bfloat16)
        values = shaped[:, 2].astype(jnp.bfloat16)
        heads_out, log_sums = attend(queries, key_rows, values, segment_row)
        heads_flat = heads_out.reshape(length, local_width)
        up_local_bias = lax.dynamic_slice_in_dim(
            up_bias[layer_id], tensor_rank * local_hidden, local_hidden, 0
        )
        up_pre = jnp.dot(mlp_in, up_full, preferred_element_type=jnp.float32) + up_local_bias
        act_low = gelu_exact(up_pre).astype(jnp.bfloat16)
        partial_sum = jnp.dot(heads_flat, proj_full, preferred_element_type=jnp.float32) + jnp.dot(
            act_low, down_full, preferred_element_type=jnp.float32
        )
        branch = lax.psum_scatter(partial_sum, "tensor", scatter_dimension=0, tiled=True)
        saved_layers.append(
            (
                normed,
                inverse,
                attn_in,
                mlp_in,
                queries,
                key_rows,
                values,
                log_sums,
                heads_flat,
                up_pre,
                act_low,
                layer_weights,
            )
        )
        stream = stream + branch + biases[layer_id, 2] + biases[layer_id, 3]
    grad_stream = cotangent.astype(jnp.float32)
    gains_list = [None] * LAYERS
    biases_list = [None] * LAYERS
    qkv_bias_list = [None] * LAYERS
    up_bias_list = [None] * LAYERS
    weight_list = [None] * LAYERS
    for layer_id in reversed(range(LAYERS)):
        (
            normed,
            inverse,
            attn_in,
            mlp_in,
            queries,
            key_rows,
            values,
            log_sums,
            heads_flat,
            up_pre,
            act_low,
            layer_weights,
        ) = saved_layers[layer_id]
        qkv_full, proj_full, up_full, down_full = layer_weights
        length = attn_in.shape[0]
        out_bias_grad = jnp.sum(grad_stream, axis=0)
        branch_grad = lax.all_gather(grad_stream.astype(jnp.bfloat16), "tensor", axis=0, tiled=True)
        down_part = jnp.einsum(
            "lf,ld->fd", act_low, branch_grad, preferred_element_type=jnp.float32
        )
        act_grad = jnp.einsum(
            "ld,fd->lf", branch_grad, down_full, preferred_element_type=jnp.float32
        )
        gelu_back = jax.vjp(gelu_exact, up_pre)[1]
        up_pre_grad = gelu_back(act_grad)[0].astype(jnp.bfloat16)
        up_bias_part = jnp.sum(up_pre_grad, axis=0, dtype=jnp.float32)
        up_part = jnp.einsum("ld,lf->df", mlp_in, up_pre_grad, preferred_element_type=jnp.float32)
        mlp_in_grad = jnp.einsum(
            "lf,df->ld", up_pre_grad, up_full, preferred_element_type=jnp.float32
        )
        proj_part = jnp.einsum(
            "lf,ld->fd", heads_flat, branch_grad, preferred_element_type=jnp.float32
        )
        heads_grad = (
            jnp.einsum("ld,fd->lf", branch_grad, proj_full, preferred_element_type=jnp.float32)
            .astype(jnp.bfloat16)
            .reshape(length, head_count, HD)
        )
        query_grad, key_grad, value_grad = attend_back(
            queries, key_rows, values, heads_grad, log_sums, segment_row
        )
        qkv_pre_grad = jnp.stack(
            [
                unrotate(query_grad, cosine_table, sine_table),
                unrotate(key_grad, cosine_table, sine_table),
                value_grad,
            ],
            axis=1,
        )
        qkv_pre_grad = qkv_pre_grad.reshape(length, 3, local_width).astype(jnp.bfloat16)
        qkv_bias_part = jnp.sum(qkv_pre_grad, axis=0, dtype=jnp.float32)
        qkv_part = jnp.einsum(
            "ld,lcf->dcf", attn_in, qkv_pre_grad, preferred_element_type=jnp.float32
        )
        attn_in_grad = jnp.einsum(
            "lcf,dcf->ld", qkv_pre_grad, qkv_full, preferred_element_type=jnp.float32
        )
        attn_rows_grad, mlp_rows_grad = (
            lax.psum_scatter(attn_in_grad, "tensor", scatter_dimension=0, tiled=True),
            lax.psum_scatter(mlp_in_grad, "tensor", scatter_dimension=0, tiled=True),
        )
        gains_list[layer_id] = jnp.stack(
            [jnp.sum(attn_rows_grad * normed, axis=0), jnp.sum(mlp_rows_grad * normed, axis=0)]
        )
        biases_list[layer_id] = jnp.stack(
            [
                jnp.sum(attn_rows_grad, axis=0),
                jnp.sum(mlp_rows_grad, axis=0),
                out_bias_grad,
                out_bias_grad,
            ]
        )
        qkv_bias_list[layer_id] = lax.dynamic_update_slice_in_dim(
            jnp.zeros((3, model_width), jnp.float32), qkv_bias_part, tensor_rank * local_width, 1
        )
        up_bias_list[layer_id] = lax.dynamic_update_slice_in_dim(
            jnp.zeros((up_bias.shape[1],), jnp.float32), up_bias_part, tensor_rank * local_hidden, 0
        )
        normed_grad = (
            attn_rows_grad * norm_gains[layer_id, 0] + mlp_rows_grad * norm_gains[layer_id, 1]
        )
        normed_mean = jnp.mean(normed_grad, axis=-1, keepdims=True)
        product_mean = jnp.mean(normed_grad * normed, axis=-1, keepdims=True)
        grad_stream = grad_stream + inverse * (normed_grad - normed_mean - normed * product_mean)
        weight_list[layer_id] = (
            chip_scatter(qkv_part, 0, 2),
            chip_scatter(proj_part, 1, 0),
            chip_scatter(up_part, 0, 1),
            chip_scatter(down_part, 1, 0),
        )
    small_parts = (
        jnp.stack(gains_list),
        jnp.stack(biases_list),
        jnp.stack(qkv_bias_list),
        jnp.stack(up_bias_list),
    )
    flat = butterfly_sum(jnp.concatenate([part.reshape(-1) for part in small_parts]))
    small_sums = []
    offset = 0
    for part in small_parts:
        small_sums.append(flat[offset : offset + part.size].reshape(part.shape))
        offset += part.size
    gains_grad, biases_grad, qkv_bias_grad, up_bias_grad = small_sums
    qkv_grad = jnp.stack([weight_list[layer_id][0] for layer_id in range(LAYERS)])
    proj_grad = jnp.stack([weight_list[layer_id][1] for layer_id in range(LAYERS)])
    up_grad = jnp.stack([weight_list[layer_id][2] for layer_id in range(LAYERS)])
    down_grad = jnp.stack([weight_list[layer_id][3] for layer_id in range(LAYERS)])
    qkv_state_new = momentum * qkv_state + qkv_grad
    proj_state_new = momentum * proj_state + proj_grad
    up_state_new = momentum * up_state + up_grad
    down_state_new = momentum * down_state + down_grad
    rows_local = qkv_state.shape[1]
    dp_count = lax.axis_size("dp")
    dp_rank = lax.axis_index("dp")
    slot_count = 4 * LAYERS
    sub = dp_count // slot_count
    piece_width = up_state.shape[2] // sub
    slot_mats = []
    for layer_id in range(LAYERS):
        slot_mats.append(qkv_state_new[layer_id].reshape(rows_local, 3 * local_width))
        slot_mats.append(proj_state_new[layer_id].T)
        slot_mats.append(up_state_new[layer_id])
        slot_mats.append(down_state_new[layer_id].T)
    pieces = []
    for mat in slot_mats:
        width = mat.shape[1] // sub
        split = mat.reshape(rows_local, sub, width).transpose(1, 0, 2)
        pieces.append(jnp.pad(split, ((0, 0), (0, 0), (0, piece_width - width))))
    outgoing = jnp.concatenate(pieces, axis=0)
    owned = lax.all_to_all(outgoing, "dp", split_axis=0, concat_axis=0, tiled=True)
    owned = owned.reshape(dp_count * rows_local, piece_width)
    gram = jnp.dot(owned, owned.T, precision=ns_precision)
    bit = 1
    while bit < sub:
        gram = gram + lax.ppermute(gram, "dp", swap_pairs(dp_count, bit))
        bit *= 2
    core_half = dp_rank % 2
    half_rows = gram.shape[0] // 2
    mine = lax.dynamic_slice_in_dim(gram, core_half * half_rows, half_rows, 0)
    mine = mine + lax.ppermute(mine, "tensor", [(0, 1), (1, 0)])
    other = lax.ppermute(mine, "dp", swap_pairs(dp_count, 1))
    gram = jnp.where(
        core_half == 0,
        jnp.concatenate([mine, other], axis=0),
        jnp.concatenate([other, mine], axis=0),
    )
    norm_sq = jnp.trace(gram)
    scale = 1.0 / (jnp.sqrt(norm_sq) + frobenius_eps)
    current_gram = gram * (scale * scale)
    identity = jnp.eye(current_gram.shape[0], dtype=jnp.float32)
    accumulated = None
    for iteration in range(NS_ITERS):
        squared = jnp.dot(current_gram, current_gram, precision=ns_precision)
        polynomial = coef_first * identity + coef_second * current_gram + coef_third * squared
        if accumulated is None:
            accumulated = polynomial
        else:
            accumulated = jnp.dot(polynomial, accumulated, precision=ns_precision)
        if iteration + 1 < NS_ITERS:
            current_gram = jnp.dot(
                polynomial,
                jnp.dot(current_gram, polynomial, precision=ns_precision),
                precision=ns_precision,
            )
    current = jnp.dot(accumulated, owned * scale, precision=ns_precision)
    returned = lax.all_to_all(
        current.reshape(dp_count, rows_local, piece_width),
        "dp",
        split_axis=0,
        concat_axis=0,
        tiled=True,
    ).reshape(slot_count, sub, rows_local, piece_width)
    my_rows = []
    for slot_id, mat in enumerate(slot_mats):
        width = mat.shape[1] // sub
        my_rows.append(returned[slot_id, :, :, :width].transpose(1, 0, 2).reshape(rows_local, sub * width))
    muon_step = muon_rate * match_rms
    qkv_list, proj_list, up_list, down_list = ([], [], [], [])
    for layer_id in range(LAYERS):
        base_slot = 4 * layer_id
        qkv_ortho = my_rows[base_slot].reshape(rows_local, 3, local_width)
        proj_ortho = my_rows[base_slot + 1].T
        up_ortho = my_rows[base_slot + 2]
        down_ortho = my_rows[base_slot + 3].T
        qkv_list.append(
            qkv_weight[layer_id].astype(jnp.float32) - muon_step * math.sqrt(3 * D) * qkv_ortho
        )
        proj_list.append(
            proj_weight[layer_id].astype(jnp.float32) - muon_step * math.sqrt(D) * proj_ortho
        )
        up_list.append(
            up_weight[layer_id].astype(jnp.float32) - muon_step * math.sqrt(FF) * up_ortho
        )
        down_list.append(
            down_weight[layer_id].astype(jnp.float32) - muon_step * math.sqrt(FF) * down_ortho
        )
    qkv_new = jnp.stack(qkv_list)
    proj_new = jnp.stack(proj_list)
    up_new = jnp.stack(up_list)
    down_new = jnp.stack(down_list)
    gains_new = vector_step(norm_gains, gains_grad)
    biases_new = vector_step(biases, biases_grad)
    qkv_bias_new = vector_step(qkv_bias, qkv_bias_grad)
    up_bias_new = vector_step(up_bias, up_bias_grad)
    return (
        stream,
        grad_stream,
        qkv_grad,
        proj_grad,
        up_grad,
        down_grad,
        gains_grad,
        biases_grad,
        qkv_bias_grad,
        up_bias_grad,
        qkv_new,
        proj_new,
        up_new,
        down_new,
        gains_new,
        biases_new,
        qkv_bias_new,
        up_bias_new,
        qkv_state_new,
        proj_state_new,
        up_state_new,
        down_state_new,
    )


def solution(mesh):
    return jax.shard_map(
        local,
        mesh=mesh,
        in_specs=(
            P(("dp", "tensor"), None),
            P(("dp", "tensor"), None),
            P("dp", None),
            P(None, "dp", None, "tensor"),
            P(None, "tensor", "dp"),
            P(None, "dp", "tensor"),
            P(None, "tensor", "dp"),
            P(),
            P(),
            P(),
            P(),
            P(None, "dp", None, "tensor"),
            P(None, "tensor", "dp"),
            P(None, "dp", "tensor"),
            P(None, "tensor", "dp"),
        ),
        out_specs=(
            P(("dp", "tensor"), None),
            P(("dp", "tensor"), None),
            P(None, "dp", None, "tensor"),
            P(None, "tensor", "dp"),
            P(None, "dp", "tensor"),
            P(None, "tensor", "dp"),
            P(),
            P(),
            P(),
            P(),
            P(None, "dp", None, "tensor"),
            P(None, "tensor", "dp"),
            P(None, "dp", "tensor"),
            P(None, "tensor", "dp"),
            P(),
            P(),
            P(),
            P(),
            P(None, "dp", None, "tensor"),
            P(None, "tensor", "dp"),
            P(None, "dp", "tensor"),
            P(None, "tensor", "dp"),
        ),
        check_vma=False,
    )
```

```python
import math

import jax
import jax.numpy as jnp
from jax import lax
from jax.sharding import PartitionSpec as P

D = 768
HD = 64
FF = 3072
ROT = 16
LAYERS = 2
NS_ITERS = 5


highest = lax.Precision.HIGHEST
ns_precision = lax.Precision.HIGH
norm_eps = 1e-05
masked_score = -1e30
coef_first = 3.4445
coef_second = -4.775
coef_third = 2.0315
momentum = 0.9
muon_rate = 0.2
match_rms = 0.2
vector_rate = 0.2
vector_eps = 1e-06
frobenius_eps = 1e-07


def rotary_tables(segment_row):
    length = segment_row.shape[0]
    indices = jnp.arange(length, dtype=jnp.int32)
    change = jnp.concatenate([jnp.ones((1,), dtype=bool), segment_row[1:] != segment_row[:-1]])
    starts = lax.cummax(jnp.where(change, indices, jnp.zeros_like(indices)), axis=0)
    positions = (indices - starts).astype(jnp.float32)
    half_rot = ROT // 2
    frequency = 10000.0 ** (-2.0 * jnp.arange(half_rot, dtype=jnp.float32) / ROT)
    angles = positions[:, None] * frequency[None, :]
    return (jnp.cos(angles), jnp.sin(angles))


def rotate(values, cosine_table, sine_table):
    half_rot = ROT // 2
    first_half = values[..., :half_rot]
    second_half = values[..., half_rot:ROT]
    cos_b = cosine_table[:, None, :]
    sin_b = sine_table[:, None, :]
    return jnp.concatenate(
        [
            first_half * cos_b - second_half * sin_b,
            second_half * cos_b + first_half * sin_b,
            values[..., ROT:],
        ],
        axis=-1,
    )


def unrotate(gradient, cosine_table, sine_table):
    half_rot = ROT // 2
    first_half = gradient[..., :half_rot]
    second_half = gradient[..., half_rot:ROT]
    cos_b = cosine_table[:, None, :]
    sin_b = sine_table[:, None, :]
    return jnp.concatenate(
        [
            first_half * cos_b + second_half * sin_b,
            second_half * cos_b - first_half * sin_b,
            gradient[..., ROT:],
        ],
        axis=-1,
    )


def normalize(stream):
    centered = stream - jnp.mean(stream, axis=-1, keepdims=True)
    inverse = lax.rsqrt(jnp.mean(centered * centered, axis=-1, keepdims=True) + norm_eps)
    return (centered * inverse, inverse)


def gelu_exact(values):
    return jax.nn.gelu(values, approximate=False)


def block_mask(segment_row, block_rows):
    query_pos = jnp.arange(block_rows, dtype=jnp.int32)
    key_pos = jnp.arange(segment_row.shape[0], dtype=jnp.int32)
    return (segment_row[:, None] == segment_row[None, :]) & (query_pos[:, None] >= key_pos[None, :])


def block_scores(queries, key_rows, allowed):
    scores = jnp.einsum(
        "qhe,khe->hqk", queries, key_rows, preferred_element_type=jnp.float32
    ) * queries.shape[-1] ** (-0.5)
    return jnp.where(allowed[None], scores, masked_score)


def attend(queries, key_rows, values, segment_row):
    length = queries.shape[0]
    block_rows = min(512, length)
    allowed = block_mask(segment_row, block_rows)
    scores = block_scores(queries, key_rows, allowed)
    row_peak = jnp.max(scores, axis=-1, keepdims=True)
    exponent = jnp.exp(scores - row_peak)
    row_total = jnp.sum(exponent, axis=-1, keepdims=True)
    probs_low = (exponent / row_total).astype(jnp.bfloat16)
    outputs = jnp.einsum(
        "hqk,khe->qhe", probs_low, values, preferred_element_type=jnp.float32
    ).astype(jnp.bfloat16)
    log_sums = row_peak + jnp.log(row_total)
    return (outputs, log_sums)


def attend_back(queries, key_rows, values, heads_grad, log_sums, segment_row):
    length = queries.shape[0]
    block_rows = min(512, length)
    scale_factor = queries.shape[-1] ** (-0.5)
    allowed = block_mask(segment_row, block_rows)
    scores = block_scores(queries, key_rows, allowed)
    probs_full = jnp.exp(scores - log_sums)
    probs_grad = jnp.einsum("qhe,khe->hqk", heads_grad, values, preferred_element_type=jnp.float32)
    row_dot = jnp.sum(probs_full * probs_grad, axis=-1, keepdims=True)
    score_grad = (probs_full * (probs_grad - row_dot)).astype(jnp.bfloat16)
    value_grad = jnp.einsum(
        "hqk,qhe->khe",
        probs_full.astype(jnp.bfloat16),
        heads_grad,
        preferred_element_type=jnp.float32,
    )
    query_grads = (
        jnp.einsum("hqk,khe->qhe", score_grad, key_rows, preferred_element_type=jnp.float32)
        * scale_factor
    )
    key_grad = (
        jnp.einsum("hqk,qhe->khe", score_grad, queries, preferred_element_type=jnp.float32)
        * scale_factor
    )
    return (query_grads, key_grad, value_grad)


def dp_scatter(partial, dimension):
    return lax.psum_scatter(partial, "dp", scatter_dimension=dimension, tiled=True)


def dp_gather(block, axis):
    return lax.all_gather(block, "dp", axis=axis, tiled=True)


def a2a_gather(block, axis):
    count = lax.axis_size("dp")
    copies = jnp.broadcast_to(block[None], (count,) + block.shape)
    got = lax.all_to_all(copies, "dp", split_axis=0, concat_axis=0, tiled=True)
    got = jnp.moveaxis(got, 0, axis)
    return got.reshape(block.shape[:axis] + (count * block.shape[axis],) + block.shape[axis + 1 :])


def a2a_scatter(partial, dimension):
    count = lax.axis_size("dp")
    shape = partial.shape
    chunks = partial.reshape(shape[:dimension] + (count, shape[dimension] // count) + shape[dimension + 1 :])
    chunks = jnp.moveaxis(chunks, dimension, 0)
    got = lax.all_to_all(chunks, "dp", split_axis=0, concat_axis=0, tiled=True)
    return jnp.sum(got, axis=0)


def swap_pairs(count, bit):
    return [(i, i ^ bit) for i in range(count)]


def butterfly_sum(flat):
    count = lax.axis_size("dp")
    bit = 1
    while bit < count:
        flat = flat + lax.ppermute(flat, "dp", swap_pairs(count, bit))
        bit *= 2
    return flat + lax.ppermute(flat, "tensor", [(0, 1), (1, 0)])


def chip_gather(block, gather_axis, split_axis):
    count = lax.axis_size("dp")
    parity = lax.axis_index("dp") % 2
    width = block.shape[split_axis] // 2
    halves = jnp.stack(
        [lax.slice_in_dim(block, 0, width, axis=split_axis), lax.slice_in_dim(block, width, 2 * width, axis=split_axis)]
    )
    outgoing = jnp.tile(halves, (count // 2,) + (1,) * block.ndim)
    got = lax.all_to_all(outgoing, "dp", split_axis=0, concat_axis=0, tiled=True)
    got = jnp.moveaxis(got, 0, gather_axis)
    shape = got.shape
    mine = got.reshape(shape[:gather_axis] + (shape[gather_axis] * shape[gather_axis + 1],) + shape[gather_axis + 2 :])
    theirs = lax.ppermute(mine, "dp", swap_pairs(count, 1))
    return jnp.where(
        parity == 0,
        jnp.concatenate([mine, theirs], axis=split_axis),
        jnp.concatenate([theirs, mine], axis=split_axis),
    )


def chip_scatter(partial, scatter_axis, split_axis):
    count = lax.axis_size("dp")
    parity = lax.axis_index("dp") % 2
    width = partial.shape[split_axis] // 2
    keep = lax.dynamic_slice_in_dim(partial, parity * width, width, split_axis)
    send = lax.dynamic_slice_in_dim(partial, (1 - parity) * width, width, split_axis)
    chip_sum = keep + lax.ppermute(send, "dp", swap_pairs(count, 1))
    shape = chip_sum.shape
    chunks = chip_sum.reshape(
        shape[:scatter_axis] + (count, shape[scatter_axis] // count) + shape[scatter_axis + 1 :]
    )
    chunks = jnp.moveaxis(chunks, scatter_axis, 0)
    got = lax.all_to_all(chunks, "dp", split_axis=0, concat_axis=0, tiled=True)
    got = got.reshape((count // 2, 2) + got.shape[1:])
    even = jnp.sum(got[:, 0], axis=0)
    odd = jnp.sum(got[:, 1], axis=0)
    return jnp.concatenate([even, odd], axis=split_axis)


def vector_step(params, gradients):
    return params - vector_rate * gradients * lax.rsqrt(
        jnp.mean(gradients * gradients, axis=-1, keepdims=True) + vector_eps
    )


def local(
    block_input,
    cotangent,
    segments,
    qkv_weight,
    proj_weight,
    up_weight,
    down_weight,
    norm_gains,
    biases,
    qkv_bias,
    up_bias,
    qkv_state,
    proj_state,
    up_state,
    down_state,
):
    tensor_rank = lax.axis_index("tensor")
    local_width = qkv_weight.shape[3]
    local_hidden = up_weight.shape[2]
    head_count = local_width // HD
    model_width = block_input.shape[1]
    segment_row = segments[0]
    cosine_table, sine_table = rotary_tables(segment_row)
    stream = block_input.astype(jnp.float32)
    saved_layers = []
    for layer_id in range(LAYERS):
        layer_weights = (
            chip_gather(qkv_weight[layer_id], 0, 2),
            chip_gather(proj_weight[layer_id], 1, 0),
            dp_gather(up_weight[layer_id], 0),
            chip_gather(down_weight[layer_id], 1, 0),
        )
        qkv_full, proj_full, up_full, down_full = layer_weights
        normed, inverse = normalize(stream)
        attn_rows = (normed * norm_gains[layer_id, 0] + biases[layer_id, 0]).astype(jnp.bfloat16)
        mlp_rows = (normed * norm_gains[layer_id, 1] + biases[layer_id, 1]).astype(jnp.bfloat16)
        attn_in, mlp_in = (
            lax.all_gather(attn_rows, "tensor", axis=0, tiled=True),
            lax.all_gather(mlp_rows, "tensor", axis=0, tiled=True),
        )
        length = attn_in.shape[0]
        qkv_local_bias = lax.dynamic_slice_in_dim(
            qkv_bias[layer_id], tensor_rank * local_width, local_width, 1
        )
        qkv_pre = (
            jnp.einsum("ld,dcf->lcf", attn_in, qkv_full, preferred_element_type=jnp.float32)
            + qkv_local_bias
        )
        shaped = qkv_pre.reshape(length, 3, head_count, HD)
        queries = rotate(shaped[:, 0], cosine_table, sine_table).astype(jnp.bfloat16)
        key_rows = rotate(shaped[:, 1], cosine_table, sine_table).astype(jnp.bfloat16)
        values = shaped[:, 2].astype(jnp.bfloat16)
        heads_out, log_sums = attend(queries, key_rows, values, segment_row)
        heads_flat = heads_out.reshape(length, local_width)
        up_local_bias = lax.dynamic_slice_in_dim(
            up_bias[layer_id], tensor_rank * local_hidden, local_hidden, 0
        )
        up_pre = jnp.dot(mlp_in, up_full, preferred_element_type=jnp.float32) + up_local_bias
        act_low = gelu_exact(up_pre).astype(jnp.bfloat16)
        partial_sum = jnp.dot(heads_flat, proj_full, preferred_element_type=jnp.float32) + jnp.dot(
            act_low, down_full, preferred_element_type=jnp.float32
        )
        branch = lax.psum_scatter(partial_sum, "tensor", scatter_dimension=0, tiled=True)
        saved_layers.append(
            (
                normed,
                inverse,
                attn_in,
                mlp_in,
                queries,
                key_rows,
                values,
                log_sums,
                heads_flat,
                up_pre,
                act_low,
                layer_weights,
            )
        )
        stream = stream + branch + biases[layer_id, 2] + biases[layer_id, 3]
    grad_stream = cotangent.astype(jnp.float32)
    gains_list = [None] * LAYERS
    biases_list = [None] * LAYERS
    qkv_bias_list = [None] * LAYERS
    up_bias_list = [None] * LAYERS
    weight_list = [None] * LAYERS
    for layer_id in reversed(range(LAYERS)):
        (
            normed,
            inverse,
            attn_in,
            mlp_in,
            queries,
            key_rows,
            values,
            log_sums,
            heads_flat,
            up_pre,
            act_low,
            layer_weights,
        ) = saved_layers[layer_id]
        qkv_full, proj_full, up_full, down_full = layer_weights
        length = attn_in.shape[0]
        out_bias_grad = jnp.sum(grad_stream, axis=0)
        branch_grad = lax.all_gather(grad_stream.astype(jnp.bfloat16), "tensor", axis=0, tiled=True)
        down_part = jnp.einsum(
            "lf,ld->fd", act_low, branch_grad, preferred_element_type=jnp.float32
        )
        act_grad = jnp.einsum(
            "ld,fd->lf", branch_grad, down_full, preferred_element_type=jnp.float32
        )
        gelu_back = jax.vjp(gelu_exact, up_pre)[1]
        up_pre_grad = gelu_back(act_grad)[0].astype(jnp.bfloat16)
        up_bias_part = jnp.sum(up_pre_grad, axis=0, dtype=jnp.float32)
        up_part = jnp.einsum("ld,lf->df", mlp_in, up_pre_grad, preferred_element_type=jnp.float32)
        mlp_in_grad = jnp.einsum(
            "lf,df->ld", up_pre_grad, up_full, preferred_element_type=jnp.float32
        )
        proj_part = jnp.einsum(
            "lf,ld->fd", heads_flat, branch_grad, preferred_element_type=jnp.float32
        )
        heads_grad = (
            jnp.einsum("ld,fd->lf", branch_grad, proj_full, preferred_element_type=jnp.float32)
            .astype(jnp.bfloat16)
            .reshape(length, head_count, HD)
        )
        query_grad, key_grad, value_grad = attend_back(
            queries, key_rows, values, heads_grad, log_sums, segment_row
        )
        qkv_pre_grad = jnp.stack(
            [
                unrotate(query_grad, cosine_table, sine_table),
                unrotate(key_grad, cosine_table, sine_table),
                value_grad,
            ],
            axis=1,
        )
        qkv_pre_grad = qkv_pre_grad.reshape(length, 3, local_width).astype(jnp.bfloat16)
        qkv_bias_part = jnp.sum(qkv_pre_grad, axis=0, dtype=jnp.float32)
        qkv_part = jnp.einsum(
            "ld,lcf->dcf", attn_in, qkv_pre_grad, preferred_element_type=jnp.float32
        )
        attn_in_grad = jnp.einsum(
            "lcf,dcf->ld", qkv_pre_grad, qkv_full, preferred_element_type=jnp.float32
        )
        attn_rows_grad, mlp_rows_grad = (
            lax.psum_scatter(attn_in_grad, "tensor", scatter_dimension=0, tiled=True),
            lax.psum_scatter(mlp_in_grad, "tensor", scatter_dimension=0, tiled=True),
        )
        gains_list[layer_id] = jnp.stack(
            [jnp.sum(attn_rows_grad * normed, axis=0), jnp.sum(mlp_rows_grad * normed, axis=0)]
        )
        biases_list[layer_id] = jnp.stack(
            [
                jnp.sum(attn_rows_grad, axis=0),
                jnp.sum(mlp_rows_grad, axis=0),
                out_bias_grad,
                out_bias_grad,
            ]
        )
        qkv_bias_list[layer_id] = lax.dynamic_update_slice_in_dim(
            jnp.zeros((3, model_width), jnp.float32), qkv_bias_part, tensor_rank * local_width, 1
        )
        up_bias_list[layer_id] = lax.dynamic_update_slice_in_dim(
            jnp.zeros((up_bias.shape[1],), jnp.float32), up_bias_part, tensor_rank * local_hidden, 0
        )
        normed_grad = (
            attn_rows_grad * norm_gains[layer_id, 0] + mlp_rows_grad * norm_gains[layer_id, 1]
        )
        normed_mean = jnp.mean(normed_grad, axis=-1, keepdims=True)
        product_mean = jnp.mean(normed_grad * normed, axis=-1, keepdims=True)
        grad_stream = grad_stream + inverse * (normed_grad - normed_mean - normed * product_mean)
        weight_list[layer_id] = (
            chip_scatter(qkv_part, 0, 2),
            chip_scatter(proj_part, 1, 0),
            dp_scatter(up_part, 0),
            chip_scatter(down_part, 1, 0),
        )
    small_parts = (
        jnp.stack(gains_list),
        jnp.stack(biases_list),
        jnp.stack(qkv_bias_list),
        jnp.stack(up_bias_list),
    )
    flat = butterfly_sum(jnp.concatenate([part.reshape(-1) for part in small_parts]))
    small_sums = []
    offset = 0
    for part in small_parts:
        small_sums.append(flat[offset : offset + part.size].reshape(part.shape))
        offset += part.size
    gains_grad, biases_grad, qkv_bias_grad, up_bias_grad = small_sums
    qkv_grad = jnp.stack([weight_list[layer_id][0] for layer_id in range(LAYERS)])
    proj_grad = jnp.stack([weight_list[layer_id][1] for layer_id in range(LAYERS)])
    up_grad = jnp.stack([weight_list[layer_id][2] for layer_id in range(LAYERS)])
    down_grad = jnp.stack([weight_list[layer_id][3] for layer_id in range(LAYERS)])
    qkv_state_new = momentum * qkv_state + qkv_grad
    proj_state_new = momentum * proj_state + proj_grad
    up_state_new = momentum * up_state + up_grad
    down_state_new = momentum * down_state + down_grad
    rows_local = qkv_state.shape[1]
    dp_count = lax.axis_size("dp")
    dp_rank = lax.axis_index("dp")
    slot_count = 4 * LAYERS
    sub = dp_count // slot_count
    piece_width = up_state.shape[2] // sub
    slot_mats = []
    for layer_id in range(LAYERS):
        slot_mats.append(qkv_state_new[layer_id].reshape(rows_local, 3 * local_width))
        slot_mats.append(proj_state_new[layer_id].T)
        slot_mats.append(up_state_new[layer_id])
        slot_mats.append(down_state_new[layer_id].T)
    pieces = []
    for mat in slot_mats:
        width = mat.shape[1] // sub
        split = mat.reshape(rows_local, sub, width).transpose(1, 0, 2)
        pieces.append(jnp.pad(split, ((0, 0), (0, 0), (0, piece_width - width))))
    outgoing = jnp.concatenate(pieces, axis=0)
    owned = lax.all_to_all(outgoing, "dp", split_axis=0, concat_axis=0, tiled=True)
    owned = owned.reshape(dp_count * rows_local, piece_width)
    owned, flat, grad_stream = lax.optimization_barrier((owned, flat, grad_stream))
    gram = jnp.dot(owned, owned.T, precision=ns_precision)
    bit = 1
    while bit < sub:
        gram = gram + lax.ppermute(gram, "dp", swap_pairs(dp_count, bit))
        bit *= 2
    core_half = dp_rank % 2
    half_rows = gram.shape[0] // 2
    mine = lax.dynamic_slice_in_dim(gram, core_half * half_rows, half_rows, 0)
    mine = mine + lax.ppermute(mine, "tensor", [(0, 1), (1, 0)])
    other = lax.ppermute(mine, "dp", swap_pairs(dp_count, 1))
    gram = jnp.where(
        core_half == 0,
        jnp.concatenate([mine, other], axis=0),
        jnp.concatenate([other, mine], axis=0),
    )
    norm_sq = jnp.trace(gram)
    scale = 1.0 / (jnp.sqrt(norm_sq) + frobenius_eps)
    current_gram = gram * (scale * scale)
    identity = jnp.eye(current_gram.shape[0], dtype=jnp.float32)
    accumulated = None
    for iteration in range(NS_ITERS):
        squared = jnp.dot(current_gram, current_gram, precision=ns_precision)
        polynomial = coef_first * identity + coef_second * current_gram + coef_third * squared
        if accumulated is None:
            accumulated = polynomial
        else:
            accumulated = jnp.dot(polynomial, accumulated, precision=ns_precision)
        if iteration + 1 < NS_ITERS:
            current_gram = jnp.dot(
                polynomial,
                jnp.dot(current_gram, polynomial, precision=ns_precision),
                precision=ns_precision,
            )
    current = jnp.dot(accumulated, owned * scale, precision=ns_precision)
    returned = lax.all_to_all(
        current.reshape(dp_count, rows_local, piece_width),
        "dp",
        split_axis=0,
        concat_axis=0,
        tiled=True,
    ).reshape(slot_count, sub, rows_local, piece_width)
    my_rows = []
    for slot_id, mat in enumerate(slot_mats):
        width = mat.shape[1] // sub
        my_rows.append(returned[slot_id, :, :, :width].transpose(1, 0, 2).reshape(rows_local, sub * width))
    muon_step = muon_rate * match_rms
    qkv_list, proj_list, up_list, down_list = ([], [], [], [])
    for layer_id in range(LAYERS):
        base_slot = 4 * layer_id
        qkv_ortho = my_rows[base_slot].reshape(rows_local, 3, local_width)
        proj_ortho = my_rows[base_slot + 1].T
        up_ortho = my_rows[base_slot + 2]
        down_ortho = my_rows[base_slot + 3].T
        qkv_list.append(
            qkv_weight[layer_id].astype(jnp.float32) - muon_step * math.sqrt(3 * D) * qkv_ortho
        )
        proj_list.append(
            proj_weight[layer_id].astype(jnp.float32) - muon_step * math.sqrt(D) * proj_ortho
        )
        up_list.append(
            up_weight[layer_id].astype(jnp.float32) - muon_step * math.sqrt(FF) * up_ortho
        )
        down_list.append(
            down_weight[layer_id].astype(jnp.float32) - muon_step * math.sqrt(FF) * down_ortho
        )
    qkv_new = jnp.stack(qkv_list)
    proj_new = jnp.stack(proj_list)
    up_new = jnp.stack(up_list)
    down_new = jnp.stack(down_list)
    gains_new = vector_step(norm_gains, gains_grad)
    biases_new = vector_step(biases, biases_grad)
    qkv_bias_new = vector_step(qkv_bias, qkv_bias_grad)
    up_bias_new = vector_step(up_bias, up_bias_grad)
    return (
        stream,
        grad_stream,
        qkv_grad,
        proj_grad,
        up_grad,
        down_grad,
        gains_grad,
        biases_grad,
        qkv_bias_grad,
        up_bias_grad,
        qkv_new,
        proj_new,
        up_new,
        down_new,
        gains_new,
        biases_new,
        qkv_bias_new,
        up_bias_new,
        qkv_state_new,
        proj_state_new,
        up_state_new,
        down_state_new,
    )


def solution(mesh):
    return jax.shard_map(
        local,
        mesh=mesh,
        in_specs=(
            P(("dp", "tensor"), None),
            P(("dp", "tensor"), None),
            P("dp", None),
            P(None, "dp", None, "tensor"),
            P(None, "tensor", "dp"),
            P(None, "dp", "tensor"),
            P(None, "tensor", "dp"),
            P(),
            P(),
            P(),
            P(),
            P(None, "dp", None, "tensor"),
            P(None, "tensor", "dp"),
            P(None, "dp", "tensor"),
            P(None, "tensor", "dp"),
        ),
        out_specs=(
            P(("dp", "tensor"), None),
            P(("dp", "tensor"), None),
            P(None, "dp", None, "tensor"),
            P(None, "tensor", "dp"),
            P(None, "dp", "tensor"),
            P(None, "tensor", "dp"),
            P(),
            P(),
            P(),
            P(),
            P(None, "dp", None, "tensor"),
            P(None, "tensor", "dp"),
            P(None, "dp", "tensor"),
            P(None, "tensor", "dp"),
            P(),
            P(),
            P(),
            P(),
            P(None, "dp", None, "tensor"),
            P(None, "tensor", "dp"),
            P(None, "dp", "tensor"),
            P(None, "tensor", "dp"),
        ),
        check_vma=False,
    )
```

```python
import math

import jax
import jax.numpy as jnp
from jax import lax
from jax.sharding import PartitionSpec as P

D = 768
HD = 64
FF = 3072
ROT = 16
LAYERS = 2
NS_ITERS = 5


highest = lax.Precision.HIGHEST
ns_precision = lax.Precision.HIGH
norm_eps = 1e-05
masked_score = -1e30
coef_first = 3.4445
coef_second = -4.775
coef_third = 2.0315
momentum = 0.9
muon_rate = 0.2
match_rms = 0.2
vector_rate = 0.2
vector_eps = 1e-06
frobenius_eps = 1e-07


def rotary_tables(segment_row):
    length = segment_row.shape[0]
    indices = jnp.arange(length, dtype=jnp.int32)
    change = jnp.concatenate([jnp.ones((1,), dtype=bool), segment_row[1:] != segment_row[:-1]])
    starts = lax.cummax(jnp.where(change, indices, jnp.zeros_like(indices)), axis=0)
    positions = (indices - starts).astype(jnp.float32)
    half_rot = ROT // 2
    frequency = 10000.0 ** (-2.0 * jnp.arange(half_rot, dtype=jnp.float32) / ROT)
    angles = positions[:, None] * frequency[None, :]
    return (jnp.cos(angles), jnp.sin(angles))


def rotate(values, cosine_table, sine_table):
    half_rot = ROT // 2
    first_half = values[..., :half_rot]
    second_half = values[..., half_rot:ROT]
    cos_b = cosine_table[:, None, :]
    sin_b = sine_table[:, None, :]
    return jnp.concatenate(
        [
            first_half * cos_b - second_half * sin_b,
            second_half * cos_b + first_half * sin_b,
            values[..., ROT:],
        ],
        axis=-1,
    )


def unrotate(gradient, cosine_table, sine_table):
    half_rot = ROT // 2
    first_half = gradient[..., :half_rot]
    second_half = gradient[..., half_rot:ROT]
    cos_b = cosine_table[:, None, :]
    sin_b = sine_table[:, None, :]
    return jnp.concatenate(
        [
            first_half * cos_b + second_half * sin_b,
            second_half * cos_b - first_half * sin_b,
            gradient[..., ROT:],
        ],
        axis=-1,
    )


def normalize(stream):
    centered = stream - jnp.mean(stream, axis=-1, keepdims=True)
    inverse = lax.rsqrt(jnp.mean(centered * centered, axis=-1, keepdims=True) + norm_eps)
    return (centered * inverse, inverse)


def gelu_exact(values):
    return jax.nn.gelu(values, approximate=False)


def block_mask(segment_row, block_rows):
    query_pos = jnp.arange(block_rows, dtype=jnp.int32)
    key_pos = jnp.arange(segment_row.shape[0], dtype=jnp.int32)
    return (segment_row[:, None] == segment_row[None, :]) & (query_pos[:, None] >= key_pos[None, :])


def block_scores(queries, key_rows, allowed):
    scores = jnp.einsum(
        "qhe,khe->hqk", queries, key_rows, preferred_element_type=jnp.float32
    ) * queries.shape[-1] ** (-0.5)
    return jnp.where(allowed[None], scores, masked_score)


def attend(queries, key_rows, values, segment_row):
    length = queries.shape[0]
    block_rows = min(512, length)
    allowed = block_mask(segment_row, block_rows)
    scores = block_scores(queries, key_rows, allowed)
    row_peak = jnp.max(scores, axis=-1, keepdims=True)
    exponent = jnp.exp(scores - row_peak)
    row_total = jnp.sum(exponent, axis=-1, keepdims=True)
    probs_low = (exponent / row_total).astype(jnp.bfloat16)
    outputs = jnp.einsum(
        "hqk,khe->qhe", probs_low, values, preferred_element_type=jnp.float32
    ).astype(jnp.bfloat16)
    log_sums = row_peak + jnp.log(row_total)
    return (outputs, log_sums)


def attend_back(queries, key_rows, values, heads_grad, log_sums, segment_row):
    length = queries.shape[0]
    block_rows = min(512, length)
    scale_factor = queries.shape[-1] ** (-0.5)
    allowed = block_mask(segment_row, block_rows)
    scores = block_scores(queries, key_rows, allowed)
    probs_full = jnp.exp(scores - log_sums)
    probs_grad = jnp.einsum("qhe,khe->hqk", heads_grad, values, preferred_element_type=jnp.float32)
    row_dot = jnp.sum(probs_full * probs_grad, axis=-1, keepdims=True)
    score_grad = (probs_full * (probs_grad - row_dot)).astype(jnp.bfloat16)
    value_grad = jnp.einsum(
        "hqk,qhe->khe",
        probs_full.astype(jnp.bfloat16),
        heads_grad,
        preferred_element_type=jnp.float32,
    )
    query_grads = (
        jnp.einsum("hqk,khe->qhe", score_grad, key_rows, preferred_element_type=jnp.float32)
        * scale_factor
    )
    key_grad = (
        jnp.einsum("hqk,qhe->khe", score_grad, queries, preferred_element_type=jnp.float32)
        * scale_factor
    )
    return (query_grads, key_grad, value_grad)


def dp_scatter(partial, dimension):
    return lax.psum_scatter(partial, "dp", scatter_dimension=dimension, tiled=True)


def dp_gather(block, axis):
    return lax.all_gather(block, "dp", axis=axis, tiled=True)


def swap_pairs(count, bit):
    return [(i, i ^ bit) for i in range(count)]


def butterfly_sum(flat):
    count = lax.axis_size("dp")
    bit = 1
    while bit < count:
        flat = flat + lax.ppermute(flat, "dp", swap_pairs(count, bit))
        bit *= 2
    return flat + lax.ppermute(flat, "tensor", [(0, 1), (1, 0)])


def tensor_swap(block):
    return lax.ppermute(block, "tensor", [(0, 1), (1, 0)])


def tensor_gather(block):
    other = tensor_swap(block)
    first = lax.axis_index("tensor") == 0
    return jnp.where(
        first, jnp.concatenate([block, other], axis=0), jnp.concatenate([other, block], axis=0)
    )


def tensor_scatter(partial):
    rank = lax.axis_index("tensor")
    half = partial.shape[0] // 2
    mine = lax.dynamic_slice_in_dim(partial, rank * half, half, 0)
    theirs = lax.dynamic_slice_in_dim(partial, (1 - rank) * half, half, 0)
    return mine + tensor_swap(theirs)


def unpack(flat_rows, shapes):
    pieces = []
    offset = 0
    for shape in shapes:
        size = math.prod(shape)
        pieces.append(flat_rows[..., offset : offset + size].reshape(flat_rows.shape[:-1] + shape))
        offset += size
    return pieces


def merge_axis(array, axis):
    shape = array.shape
    return array.reshape(shape[:axis] + (shape[axis] * shape[axis + 1],) + shape[axis + 2 :])


def chip_gather_many(blocks, gather_axes, split_axes):
    count = lax.axis_size("dp")
    parity = lax.axis_index("dp") % 2
    packed, shapes = [], []
    for block, split_axis in zip(blocks, split_axes):
        width = block.shape[split_axis] // 2
        halves = jnp.stack(
            [
                lax.slice_in_dim(block, 0, width, axis=split_axis),
                lax.slice_in_dim(block, width, 2 * width, axis=split_axis),
            ]
        )
        shapes.append(halves.shape[1:])
        packed.append(halves.reshape(2, -1))
    packed = jnp.concatenate(packed, axis=1)
    outgoing = jnp.tile(packed, (count // 2, 1))
    got = lax.all_to_all(outgoing, "dp", split_axis=0, concat_axis=0, tiled=True)
    mines = []
    for piece, gather_axis in zip(unpack(got, shapes), gather_axes):
        mines.append(merge_axis(jnp.moveaxis(piece, 0, gather_axis), gather_axis))
    flat_mine = jnp.concatenate([mine.reshape(-1) for mine in mines])
    flat_theirs = lax.ppermute(flat_mine, "dp", swap_pairs(count, 1))
    results = []
    for mine, theirs, split_axis in zip(mines, unpack(flat_theirs, [m.shape for m in mines]), split_axes):
        results.append(
            jnp.where(
                parity == 0,
                jnp.concatenate([mine, theirs], axis=split_axis),
                jnp.concatenate([theirs, mine], axis=split_axis),
            )
        )
    return results


def chip_scatter_many(partials, scatter_axes, split_axes):
    count = lax.axis_size("dp")
    parity = lax.axis_index("dp") % 2
    keeps, sends = [], []
    for partial, split_axis in zip(partials, split_axes):
        width = partial.shape[split_axis] // 2
        keeps.append(lax.dynamic_slice_in_dim(partial, parity * width, width, split_axis))
        sends.append(lax.dynamic_slice_in_dim(partial, (1 - parity) * width, width, split_axis))
    flat_send = jnp.concatenate([send.reshape(-1) for send in sends])
    flat_recv = lax.ppermute(flat_send, "dp", swap_pairs(count, 1))
    packed, shapes = [], []
    for keep, received, scatter_axis in zip(keeps, unpack(flat_recv, [k.shape for k in keeps]), scatter_axes):
        chip_sum = keep + received
        shape = chip_sum.shape
        chunks = chip_sum.reshape(
            shape[:scatter_axis] + (count, shape[scatter_axis] // count) + shape[scatter_axis + 1 :]
        )
        chunks = jnp.moveaxis(chunks, scatter_axis, 0)
        shapes.append(chunks.shape[1:])
        packed.append(chunks.reshape(count, -1))
    got = lax.all_to_all(jnp.concatenate(packed, axis=1), "dp", split_axis=0, concat_axis=0, tiled=True)
    results = []
    for piece, split_axis in zip(unpack(got, shapes), split_axes):
        piece = piece.reshape((count // 2, 2) + piece.shape[1:])
        even = jnp.sum(piece[:, 0], axis=0)
        odd = jnp.sum(piece[:, 1], axis=0)
        results.append(jnp.concatenate([even, odd], axis=split_axis))
    return results


def vector_step(params, gradients):
    return params - vector_rate * gradients * lax.rsqrt(
        jnp.mean(gradients * gradients, axis=-1, keepdims=True) + vector_eps
    )


def local(
    block_input,
    cotangent,
    segments,
    qkv_weight,
    proj_weight,
    up_weight,
    down_weight,
    norm_gains,
    biases,
    qkv_bias,
    up_bias,
    qkv_state,
    proj_state,
    up_state,
    down_state,
):
    tensor_rank = lax.axis_index("tensor")
    local_width = qkv_weight.shape[3]
    local_hidden = up_weight.shape[2]
    head_count = local_width // HD
    model_width = block_input.shape[1]
    segment_row = segments[0]
    cosine_table, sine_table = rotary_tables(segment_row)
    stream = block_input.astype(jnp.float32)
    saved_layers = []
    for layer_id in range(LAYERS):
        up_full = dp_gather(up_weight[layer_id], 0)
        qkv_full, proj_full, down_full = chip_gather_many(
            (qkv_weight[layer_id], proj_weight[layer_id], down_weight[layer_id]), (0, 1, 1), (2, 0, 0)
        )
        layer_weights = (qkv_full, proj_full, up_full, down_full)
        normed, inverse = normalize(stream)
        attn_rows = (normed * norm_gains[layer_id, 0] + biases[layer_id, 0]).astype(jnp.bfloat16)
        mlp_rows = (normed * norm_gains[layer_id, 1] + biases[layer_id, 1]).astype(jnp.bfloat16)
        both_in = tensor_gather(jnp.concatenate([attn_rows, mlp_rows], axis=1))
        attn_in, mlp_in = both_in[:, :model_width], both_in[:, model_width:]
        length = attn_in.shape[0]
        qkv_local_bias = lax.dynamic_slice_in_dim(
            qkv_bias[layer_id], tensor_rank * local_width, local_width, 1
        )
        qkv_pre = (
            jnp.einsum("ld,dcf->lcf", attn_in, qkv_full, preferred_element_type=jnp.float32)
            + qkv_local_bias
        )
        shaped = qkv_pre.reshape(length, 3, head_count, HD)
        queries = rotate(shaped[:, 0], cosine_table, sine_table).astype(jnp.bfloat16)
        key_rows = rotate(shaped[:, 1], cosine_table, sine_table).astype(jnp.bfloat16)
        values = shaped[:, 2].astype(jnp.bfloat16)
        heads_out, log_sums = attend(queries, key_rows, values, segment_row)
        heads_flat = heads_out.reshape(length, local_width)
        up_local_bias = lax.dynamic_slice_in_dim(
            up_bias[layer_id], tensor_rank * local_hidden, local_hidden, 0
        )
        up_pre = jnp.dot(mlp_in, up_full, preferred_element_type=jnp.float32) + up_local_bias
        act_low = gelu_exact(up_pre).astype(jnp.bfloat16)
        partial_sum = jnp.dot(heads_flat, proj_full, preferred_element_type=jnp.float32) + jnp.dot(
            act_low, down_full, preferred_element_type=jnp.float32
        )
        branch = tensor_scatter(partial_sum)
        saved_layers.append(
            (
                normed,
                inverse,
                attn_in,
                mlp_in,
                queries,
                key_rows,
                values,
                log_sums,
                heads_flat,
                up_pre,
                act_low,
                layer_weights,
            )
        )
        stream = stream + branch + biases[layer_id, 2] + biases[layer_id, 3]
    grad_stream = cotangent.astype(jnp.float32)
    gains_list = [None] * LAYERS
    biases_list = [None] * LAYERS
    qkv_bias_list = [None] * LAYERS
    up_bias_list = [None] * LAYERS
    weight_list = [None] * LAYERS
    for layer_id in reversed(range(LAYERS)):
        (
            normed,
            inverse,
            attn_in,
            mlp_in,
            queries,
            key_rows,
            values,
            log_sums,
            heads_flat,
            up_pre,
            act_low,
            layer_weights,
        ) = saved_layers[layer_id]
        qkv_full, proj_full, up_full, down_full = layer_weights
        length = attn_in.shape[0]
        out_bias_grad = jnp.sum(grad_stream, axis=0)
        branch_grad = tensor_gather(grad_stream.astype(jnp.bfloat16))
        down_part = jnp.einsum(
            "lf,ld->fd", act_low, branch_grad, preferred_element_type=jnp.float32
        )
        act_grad = jnp.einsum(
            "ld,fd->lf", branch_grad, down_full, preferred_element_type=jnp.float32
        )
        gelu_back = jax.vjp(gelu_exact, up_pre)[1]
        up_pre_grad = gelu_back(act_grad)[0].astype(jnp.bfloat16)
        up_bias_part = jnp.sum(up_pre_grad, axis=0, dtype=jnp.float32)
        up_part = jnp.einsum("ld,lf->df", mlp_in, up_pre_grad, preferred_element_type=jnp.float32)
        mlp_in_grad = jnp.einsum(
            "lf,df->ld", up_pre_grad, up_full, preferred_element_type=jnp.float32
        )
        proj_part = jnp.einsum(
            "lf,ld->fd", heads_flat, branch_grad, preferred_element_type=jnp.float32
        )
        heads_grad = (
            jnp.einsum("ld,fd->lf", branch_grad, proj_full, preferred_element_type=jnp.float32)
            .astype(jnp.bfloat16)
            .reshape(length, head_count, HD)
        )
        query_grad, key_grad, value_grad = attend_back(
            queries, key_rows, values, heads_grad, log_sums, segment_row
        )
        qkv_pre_grad = jnp.stack(
            [
                unrotate(query_grad, cosine_table, sine_table),
                unrotate(key_grad, cosine_table, sine_table),
                value_grad,
            ],
            axis=1,
        )
        qkv_pre_grad = qkv_pre_grad.reshape(length, 3, local_width).astype(jnp.bfloat16)
        qkv_bias_part = jnp.sum(qkv_pre_grad, axis=0, dtype=jnp.float32)
        qkv_part = jnp.einsum(
            "ld,lcf->dcf", attn_in, qkv_pre_grad, preferred_element_type=jnp.float32
        )
        attn_in_grad = jnp.einsum(
            "lcf,dcf->ld", qkv_pre_grad, qkv_full, preferred_element_type=jnp.float32
        )
        both_grad = tensor_scatter(jnp.concatenate([attn_in_grad, mlp_in_grad], axis=1))
        attn_rows_grad, mlp_rows_grad = both_grad[:, :model_width], both_grad[:, model_width:]
        gains_list[layer_id] = jnp.stack(
            [jnp.sum(attn_rows_grad * normed, axis=0), jnp.sum(mlp_rows_grad * normed, axis=0)]
        )
        biases_list[layer_id] = jnp.stack(
            [
                jnp.sum(attn_rows_grad, axis=0),
                jnp.sum(mlp_rows_grad, axis=0),
                out_bias_grad,
                out_bias_grad,
            ]
        )
        qkv_bias_list[layer_id] = lax.dynamic_update_slice_in_dim(
            jnp.zeros((3, model_width), jnp.float32), qkv_bias_part, tensor_rank * local_width, 1
        )
        up_bias_list[layer_id] = lax.dynamic_update_slice_in_dim(
            jnp.zeros((up_bias.shape[1],), jnp.float32), up_bias_part, tensor_rank * local_hidden, 0
        )
        normed_grad = (
            attn_rows_grad * norm_gains[layer_id, 0] + mlp_rows_grad * norm_gains[layer_id, 1]
        )
        normed_mean = jnp.mean(normed_grad, axis=-1, keepdims=True)
        product_mean = jnp.mean(normed_grad * normed, axis=-1, keepdims=True)
        grad_stream = grad_stream + inverse * (normed_grad - normed_mean - normed * product_mean)
        qkv_sum, proj_sum, down_sum = chip_scatter_many((qkv_part, proj_part, down_part), (0, 1, 1), (2, 0, 0))
        weight_list[layer_id] = (qkv_sum, proj_sum, dp_scatter(up_part, 0), down_sum)
    small_parts = (
        jnp.stack(gains_list),
        jnp.stack(biases_list),
        jnp.stack(qkv_bias_list),
        jnp.stack(up_bias_list),
    )
    flat = butterfly_sum(jnp.concatenate([part.reshape(-1) for part in small_parts]))
    small_sums = []
    offset = 0
    for part in small_parts:
        small_sums.append(flat[offset : offset + part.size].reshape(part.shape))
        offset += part.size
    gains_grad, biases_grad, qkv_bias_grad, up_bias_grad = small_sums
    qkv_grad = jnp.stack([weight_list[layer_id][0] for layer_id in range(LAYERS)])
    proj_grad = jnp.stack([weight_list[layer_id][1] for layer_id in range(LAYERS)])
    up_grad = jnp.stack([weight_list[layer_id][2] for layer_id in range(LAYERS)])
    down_grad = jnp.stack([weight_list[layer_id][3] for layer_id in range(LAYERS)])
    qkv_state_new = momentum * qkv_state + qkv_grad
    proj_state_new = momentum * proj_state + proj_grad
    up_state_new = momentum * up_state + up_grad
    down_state_new = momentum * down_state + down_grad
    rows_local = qkv_state.shape[1]
    dp_count = lax.axis_size("dp")
    dp_rank = lax.axis_index("dp")
    slot_count = 4 * LAYERS
    sub = dp_count // slot_count
    piece_width = up_state.shape[2] // sub
    slot_mats = []
    for layer_id in range(LAYERS):
        slot_mats.append(qkv_state_new[layer_id].reshape(rows_local, 3 * local_width))
        slot_mats.append(proj_state_new[layer_id].T)
        slot_mats.append(up_state_new[layer_id])
        slot_mats.append(down_state_new[layer_id].T)
    pieces = []
    for mat in slot_mats:
        width = mat.shape[1] // sub
        split = mat.reshape(rows_local, sub, width).transpose(1, 0, 2)
        pieces.append(jnp.pad(split, ((0, 0), (0, 0), (0, piece_width - width))))
    outgoing = jnp.concatenate(pieces, axis=0)
    owned = lax.all_to_all(outgoing, "dp", split_axis=0, concat_axis=0, tiled=True)
    owned = owned.reshape(dp_count * rows_local, piece_width)
    owned, flat, grad_stream = lax.optimization_barrier((owned, flat, grad_stream))
    gram = jnp.dot(owned, owned.T, precision=ns_precision)
    bit = 1
    while bit < sub:
        gram = gram + lax.ppermute(gram, "dp", swap_pairs(dp_count, bit))
        bit *= 2
    core_half = dp_rank % 2
    half_rows = gram.shape[0] // 2
    mine = lax.dynamic_slice_in_dim(gram, core_half * half_rows, half_rows, 0)
    mine = mine + lax.ppermute(mine, "tensor", [(0, 1), (1, 0)])
    other = lax.ppermute(mine, "dp", swap_pairs(dp_count, 1))
    gram = jnp.where(
        core_half == 0,
        jnp.concatenate([mine, other], axis=0),
        jnp.concatenate([other, mine], axis=0),
    )
    norm_sq = jnp.trace(gram)
    scale = 1.0 / (jnp.sqrt(norm_sq) + frobenius_eps)
    current_gram = gram * (scale * scale)
    identity = jnp.eye(current_gram.shape[0], dtype=jnp.float32)
    accumulated = None
    for iteration in range(NS_ITERS):
        squared = jnp.dot(current_gram, current_gram, precision=ns_precision)
        polynomial = coef_first * identity + coef_second * current_gram + coef_third * squared
        if accumulated is None:
            accumulated = polynomial
        else:
            accumulated = jnp.dot(polynomial, accumulated, precision=ns_precision)
        if iteration + 1 < NS_ITERS:
            current_gram = jnp.dot(
                polynomial,
                jnp.dot(current_gram, polynomial, precision=ns_precision),
                precision=ns_precision,
            )
    current = jnp.dot(accumulated, owned * scale, precision=ns_precision)
    returned = lax.all_to_all(
        current.astype(jnp.bfloat16).reshape(dp_count, rows_local, piece_width),
        "dp",
        split_axis=0,
        concat_axis=0,
        tiled=True,
    ).reshape(slot_count, sub, rows_local, piece_width)
    my_rows = []
    for slot_id, mat in enumerate(slot_mats):
        width = mat.shape[1] // sub
        my_rows.append(
            returned[slot_id, :, :, :width]
            .astype(jnp.float32)
            .transpose(1, 0, 2)
            .reshape(rows_local, sub * width)
        )
    muon_step = muon_rate * match_rms
    qkv_list, proj_list, up_list, down_list = ([], [], [], [])
    for layer_id in range(LAYERS):
        base_slot = 4 * layer_id
        qkv_ortho = my_rows[base_slot].reshape(rows_local, 3, local_width)
        proj_ortho = my_rows[base_slot + 1].T
        up_ortho = my_rows[base_slot + 2]
        down_ortho = my_rows[base_slot + 3].T
        qkv_list.append(
            qkv_weight[layer_id].astype(jnp.float32) - muon_step * math.sqrt(3 * D) * qkv_ortho
        )
        proj_list.append(
            proj_weight[layer_id].astype(jnp.float32) - muon_step * math.sqrt(D) * proj_ortho
        )
        up_list.append(
            up_weight[layer_id].astype(jnp.float32) - muon_step * math.sqrt(FF) * up_ortho
        )
        down_list.append(
            down_weight[layer_id].astype(jnp.float32) - muon_step * math.sqrt(FF) * down_ortho
        )
    qkv_new = jnp.stack(qkv_list)
    proj_new = jnp.stack(proj_list)
    up_new = jnp.stack(up_list)
    down_new = jnp.stack(down_list)
    gains_new = vector_step(norm_gains, gains_grad)
    biases_new = vector_step(biases, biases_grad)
    qkv_bias_new = vector_step(qkv_bias, qkv_bias_grad)
    up_bias_new = vector_step(up_bias, up_bias_grad)
    return (
        stream,
        grad_stream,
        qkv_grad,
        proj_grad,
        up_grad,
        down_grad,
        gains_grad,
        biases_grad,
        qkv_bias_grad,
        up_bias_grad,
        qkv_new,
        proj_new,
        up_new,
        down_new,
        gains_new,
        biases_new,
        qkv_bias_new,
        up_bias_new,
        qkv_state_new,
        proj_state_new,
        up_state_new,
        down_state_new,
    )


def solution(mesh):
    return jax.shard_map(
        local,
        mesh=mesh,
        in_specs=(
            P(("dp", "tensor"), None),
            P(("dp", "tensor"), None),
            P("dp", None),
            P(None, "dp", None, "tensor"),
            P(None, "tensor", "dp"),
            P(None, "dp", "tensor"),
            P(None, "tensor", "dp"),
            P(),
            P(),
            P(),
            P(),
            P(None, "dp", None, "tensor"),
            P(None, "tensor", "dp"),
            P(None, "dp", "tensor"),
            P(None, "tensor", "dp"),
        ),
        out_specs=(
            P(("dp", "tensor"), None),
            P(("dp", "tensor"), None),
            P(None, "dp", None, "tensor"),
            P(None, "tensor", "dp"),
            P(None, "dp", "tensor"),
            P(None, "tensor", "dp"),
            P(),
            P(),
            P(),
            P(),
            P(None, "dp", None, "tensor"),
            P(None, "tensor", "dp"),
            P(None, "dp", "tensor"),
            P(None, "tensor", "dp"),
            P(),
            P(),
            P(),
            P(),
            P(None, "dp", None, "tensor"),
            P(None, "tensor", "dp"),
            P(None, "dp", "tensor"),
            P(None, "tensor", "dp"),
        ),
        check_vma=False,
    )
```

```python
import math

import jax
import jax.numpy as jnp
from jax import lax
from jax.sharding import PartitionSpec as P

D = 768
HD = 64
FF = 3072
ROT = 16
LAYERS = 2
NS_ITERS = 5


highest = lax.Precision.HIGHEST
ns_precision = lax.Precision.HIGH
norm_eps = 1e-05
masked_score = -1e30
coef_first = 3.4445
coef_second = -4.775
coef_third = 2.0315
momentum = 0.9
muon_rate = 0.2
match_rms = 0.2
vector_rate = 0.2
vector_eps = 1e-06
frobenius_eps = 1e-07


def rotary_tables(segment_row):
    length = segment_row.shape[0]
    indices = jnp.arange(length, dtype=jnp.int32)
    change = jnp.concatenate([jnp.ones((1,), dtype=bool), segment_row[1:] != segment_row[:-1]])
    starts = lax.cummax(jnp.where(change, indices, jnp.zeros_like(indices)), axis=0)
    positions = (indices - starts).astype(jnp.float32)
    half_rot = ROT // 2
    frequency = 10000.0 ** (-2.0 * jnp.arange(half_rot, dtype=jnp.float32) / ROT)
    angles = positions[:, None] * frequency[None, :]
    return (jnp.cos(angles), jnp.sin(angles))


def rotate(values, cosine_table, sine_table):
    half_rot = ROT // 2
    first_half = values[..., :half_rot]
    second_half = values[..., half_rot:ROT]
    cos_b = cosine_table[:, None, :]
    sin_b = sine_table[:, None, :]
    return jnp.concatenate(
        [
            first_half * cos_b - second_half * sin_b,
            second_half * cos_b + first_half * sin_b,
            values[..., ROT:],
        ],
        axis=-1,
    )


def unrotate(gradient, cosine_table, sine_table):
    half_rot = ROT // 2
    first_half = gradient[..., :half_rot]
    second_half = gradient[..., half_rot:ROT]
    cos_b = cosine_table[:, None, :]
    sin_b = sine_table[:, None, :]
    return jnp.concatenate(
        [
            first_half * cos_b + second_half * sin_b,
            second_half * cos_b - first_half * sin_b,
            gradient[..., ROT:],
        ],
        axis=-1,
    )


def normalize(stream):
    centered = stream - jnp.mean(stream, axis=-1, keepdims=True)
    inverse = lax.rsqrt(jnp.mean(centered * centered, axis=-1, keepdims=True) + norm_eps)
    return (centered * inverse, inverse)


def gelu_exact(values):
    return jax.nn.gelu(values, approximate=False)


def block_mask(segment_row, block_rows):
    query_pos = jnp.arange(block_rows, dtype=jnp.int32)
    key_pos = jnp.arange(segment_row.shape[0], dtype=jnp.int32)
    return (segment_row[:, None] == segment_row[None, :]) & (query_pos[:, None] >= key_pos[None, :])


def block_scores(queries, key_rows, allowed):
    scores = jnp.einsum(
        "qhe,khe->hqk", queries, key_rows, preferred_element_type=jnp.float32
    ) * queries.shape[-1] ** (-0.5)
    return jnp.where(allowed[None], scores, masked_score)


def attend(queries, key_rows, values, segment_row):
    length = queries.shape[0]
    block_rows = min(512, length)
    allowed = block_mask(segment_row, block_rows)
    scores = block_scores(queries, key_rows, allowed)
    row_peak = jnp.max(scores, axis=-1, keepdims=True)
    exponent = jnp.exp(scores - row_peak)
    row_total = jnp.sum(exponent, axis=-1, keepdims=True)
    probs_low = (exponent / row_total).astype(jnp.bfloat16)
    outputs = jnp.einsum(
        "hqk,khe->qhe", probs_low, values, preferred_element_type=jnp.float32
    ).astype(jnp.bfloat16)
    log_sums = row_peak + jnp.log(row_total)
    return (outputs, log_sums)


def attend_back(queries, key_rows, values, heads_grad, log_sums, segment_row):
    length = queries.shape[0]
    block_rows = min(512, length)
    scale_factor = queries.shape[-1] ** (-0.5)
    allowed = block_mask(segment_row, block_rows)
    scores = block_scores(queries, key_rows, allowed)
    probs_full = jnp.exp(scores - log_sums)
    probs_grad = jnp.einsum("qhe,khe->hqk", heads_grad, values, preferred_element_type=jnp.float32)
    row_dot = jnp.sum(probs_full * probs_grad, axis=-1, keepdims=True)
    score_grad = (probs_full * (probs_grad - row_dot)).astype(jnp.bfloat16)
    value_grad = jnp.einsum(
        "hqk,qhe->khe",
        probs_full.astype(jnp.bfloat16),
        heads_grad,
        preferred_element_type=jnp.float32,
    )
    query_grads = (
        jnp.einsum("hqk,khe->qhe", score_grad, key_rows, preferred_element_type=jnp.float32)
        * scale_factor
    )
    key_grad = (
        jnp.einsum("hqk,qhe->khe", score_grad, queries, preferred_element_type=jnp.float32)
        * scale_factor
    )
    return (query_grads, key_grad, value_grad)


def dp_scatter(partial, dimension):
    return lax.psum_scatter(partial, "dp", scatter_dimension=dimension, tiled=True)


def dp_gather(block, axis):
    return lax.all_gather(block, "dp", axis=axis, tiled=True)


def swap_pairs(count, bit):
    return [(i, i ^ bit) for i in range(count)]


def butterfly_sum(flat):
    count = lax.axis_size("dp")
    bit = 1
    while bit < count:
        flat = flat + lax.ppermute(flat, "dp", swap_pairs(count, bit))
        bit *= 2
    return flat + lax.ppermute(flat, "tensor", [(0, 1), (1, 0)])


def tensor_swap(block):
    return lax.ppermute(block, "tensor", [(0, 1), (1, 0)])


def tensor_gather(block):
    other = tensor_swap(block)
    first = lax.axis_index("tensor") == 0
    return jnp.where(
        first, jnp.concatenate([block, other], axis=0), jnp.concatenate([other, block], axis=0)
    )


def tensor_scatter(partial):
    rank = lax.axis_index("tensor")
    half = partial.shape[0] // 2
    mine = lax.dynamic_slice_in_dim(partial, rank * half, half, 0)
    theirs = lax.dynamic_slice_in_dim(partial, (1 - rank) * half, half, 0)
    return mine + tensor_swap(theirs)


def chip_gather(block, gather_axis, split_axis):
    count = lax.axis_size("dp")
    parity = lax.axis_index("dp") % 2
    width = block.shape[split_axis] // 2
    halves = jnp.stack(
        [lax.slice_in_dim(block, 0, width, axis=split_axis), lax.slice_in_dim(block, width, 2 * width, axis=split_axis)]
    )
    outgoing = jnp.tile(halves, (count // 2,) + (1,) * block.ndim)
    got = lax.all_to_all(outgoing, "dp", split_axis=0, concat_axis=0, tiled=True)
    got = jnp.moveaxis(got, 0, gather_axis)
    shape = got.shape
    mine = got.reshape(shape[:gather_axis] + (shape[gather_axis] * shape[gather_axis + 1],) + shape[gather_axis + 2 :])
    theirs = lax.ppermute(mine, "dp", swap_pairs(count, 1))
    return jnp.where(
        parity == 0,
        jnp.concatenate([mine, theirs], axis=split_axis),
        jnp.concatenate([theirs, mine], axis=split_axis),
    )


def chip_scatter(partial, scatter_axis, split_axis):
    count = lax.axis_size("dp")
    parity = lax.axis_index("dp") % 2
    width = partial.shape[split_axis] // 2
    keep = lax.dynamic_slice_in_dim(partial, parity * width, width, split_axis)
    send = lax.dynamic_slice_in_dim(partial, (1 - parity) * width, width, split_axis)
    chip_sum = keep + lax.ppermute(send, "dp", swap_pairs(count, 1))
    shape = chip_sum.shape
    chunks = chip_sum.reshape(
        shape[:scatter_axis] + (count, shape[scatter_axis] // count) + shape[scatter_axis + 1 :]
    )
    chunks = jnp.moveaxis(chunks, scatter_axis, 0)
    got = lax.all_to_all(chunks, "dp", split_axis=0, concat_axis=0, tiled=True)
    got = got.reshape((count // 2, 2) + got.shape[1:])
    even = jnp.sum(got[:, 0], axis=0)
    odd = jnp.sum(got[:, 1], axis=0)
    return jnp.concatenate([even, odd], axis=split_axis)


def vector_step(params, gradients):
    return params - vector_rate * gradients * lax.rsqrt(
        jnp.mean(gradients * gradients, axis=-1, keepdims=True) + vector_eps
    )


def local(
    block_input,
    cotangent,
    segments,
    qkv_weight,
    proj_weight,
    up_weight,
    down_weight,
    norm_gains,
    biases,
    qkv_bias,
    up_bias,
    qkv_state,
    proj_state,
    up_state,
    down_state,
):
    tensor_rank = lax.axis_index("tensor")
    local_width = qkv_weight.shape[3]
    local_hidden = up_weight.shape[2]
    head_count = local_width // HD
    model_width = block_input.shape[1]
    segment_row = segments[0]
    cosine_table, sine_table = rotary_tables(segment_row)
    stream = block_input.astype(jnp.float32)
    saved_layers = []
    for layer_id in range(LAYERS):
        layer_weights = (
            chip_gather(qkv_weight[layer_id], 0, 2),
            chip_gather(proj_weight[layer_id], 1, 0),
            dp_gather(up_weight[layer_id], 0),
            chip_gather(down_weight[layer_id], 1, 0),
        )
        qkv_full, proj_full, up_full, down_full = layer_weights
        normed, inverse = normalize(stream)
        attn_rows = (normed * norm_gains[layer_id, 0] + biases[layer_id, 0]).astype(jnp.bfloat16)
        mlp_rows = (normed * norm_gains[layer_id, 1] + biases[layer_id, 1]).astype(jnp.bfloat16)
        both_in = tensor_gather(jnp.concatenate([attn_rows, mlp_rows], axis=1))
        attn_in, mlp_in = both_in[:, :model_width], both_in[:, model_width:]
        length = attn_in.shape[0]
        qkv_local_bias = lax.dynamic_slice_in_dim(
            qkv_bias[layer_id], tensor_rank * local_width, local_width, 1
        )
        qkv_pre = (
            jnp.einsum("ld,dcf->lcf", attn_in, qkv_full, preferred_element_type=jnp.float32)
            + qkv_local_bias
        )
        shaped = qkv_pre.reshape(length, 3, head_count, HD)
        queries = rotate(shaped[:, 0], cosine_table, sine_table).astype(jnp.bfloat16)
        key_rows = rotate(shaped[:, 1], cosine_table, sine_table).astype(jnp.bfloat16)
        values = shaped[:, 2].astype(jnp.bfloat16)
        heads_out, log_sums = attend(queries, key_rows, values, segment_row)
        heads_flat = heads_out.reshape(length, local_width)
        up_local_bias = lax.dynamic_slice_in_dim(
            up_bias[layer_id], tensor_rank * local_hidden, local_hidden, 0
        )
        up_pre = jnp.dot(mlp_in, up_full, preferred_element_type=jnp.float32) + up_local_bias
        act_low = gelu_exact(up_pre).astype(jnp.bfloat16)
        partial_sum = jnp.dot(heads_flat, proj_full, preferred_element_type=jnp.float32) + jnp.dot(
            act_low, down_full, preferred_element_type=jnp.float32
        )
        branch = tensor_scatter(partial_sum)
        saved_layers.append(
            (
                normed,
                inverse,
                attn_in,
                mlp_in,
                queries,
                key_rows,
                values,
                log_sums,
                heads_flat,
                up_pre,
                act_low,
                layer_weights,
            )
        )
        stream = stream + branch + biases[layer_id, 2] + biases[layer_id, 3]
    grad_stream = cotangent.astype(jnp.float32)
    gains_list = [None] * LAYERS
    biases_list = [None] * LAYERS
    qkv_bias_list = [None] * LAYERS
    up_bias_list = [None] * LAYERS
    weight_list = [None] * LAYERS
    for layer_id in reversed(range(LAYERS)):
        (
            normed,
            inverse,
            attn_in,
            mlp_in,
            queries,
            key_rows,
            values,
            log_sums,
            heads_flat,
            up_pre,
            act_low,
            layer_weights,
        ) = saved_layers[layer_id]
        qkv_full, proj_full, up_full, down_full = layer_weights
        length = attn_in.shape[0]
        out_bias_grad = jnp.sum(grad_stream, axis=0)
        branch_grad = tensor_gather(grad_stream.astype(jnp.bfloat16))
        down_part = jnp.einsum(
            "lf,ld->fd", act_low, branch_grad, preferred_element_type=jnp.float32
        )
        act_grad = jnp.einsum(
            "ld,fd->lf", branch_grad, down_full, preferred_element_type=jnp.float32
        )
        gelu_back = jax.vjp(gelu_exact, up_pre)[1]
        up_pre_grad = gelu_back(act_grad)[0].astype(jnp.bfloat16)
        up_bias_part = jnp.sum(up_pre_grad, axis=0, dtype=jnp.float32)
        up_part = jnp.einsum("ld,lf->df", mlp_in, up_pre_grad, preferred_element_type=jnp.float32)
        mlp_in_grad = jnp.einsum(
            "lf,df->ld", up_pre_grad, up_full, preferred_element_type=jnp.float32
        )
        proj_part = jnp.einsum(
            "lf,ld->fd", heads_flat, branch_grad, preferred_element_type=jnp.float32
        )
        heads_grad = (
            jnp.einsum("ld,fd->lf", branch_grad, proj_full, preferred_element_type=jnp.float32)
            .astype(jnp.bfloat16)
            .reshape(length, head_count, HD)
        )
        query_grad, key_grad, value_grad = attend_back(
            queries, key_rows, values, heads_grad, log_sums, segment_row
        )
        qkv_pre_grad = jnp.stack(
            [
                unrotate(query_grad, cosine_table, sine_table),
                unrotate(key_grad, cosine_table, sine_table),
                value_grad,
            ],
            axis=1,
        )
        qkv_pre_grad = qkv_pre_grad.reshape(length, 3, local_width).astype(jnp.bfloat16)
        qkv_bias_part = jnp.sum(qkv_pre_grad, axis=0, dtype=jnp.float32)
        qkv_part = jnp.einsum(
            "ld,lcf->dcf", attn_in, qkv_pre_grad, preferred_element_type=jnp.float32
        )
        attn_in_grad = jnp.einsum(
            "lcf,dcf->ld", qkv_pre_grad, qkv_full, preferred_element_type=jnp.float32
        )
        both_grad = tensor_scatter(jnp.concatenate([attn_in_grad, mlp_in_grad], axis=1))
        attn_rows_grad, mlp_rows_grad = both_grad[:, :model_width], both_grad[:, model_width:]
        gains_list[layer_id] = jnp.stack(
            [jnp.sum(attn_rows_grad * normed, axis=0), jnp.sum(mlp_rows_grad * normed, axis=0)]
        )
        biases_list[layer_id] = jnp.stack(
            [
                jnp.sum(attn_rows_grad, axis=0),
                jnp.sum(mlp_rows_grad, axis=0),
                out_bias_grad,
                out_bias_grad,
            ]
        )
        qkv_bias_list[layer_id] = lax.dynamic_update_slice_in_dim(
            jnp.zeros((3, model_width), jnp.float32), qkv_bias_part, tensor_rank * local_width, 1
        )
        up_bias_list[layer_id] = lax.dynamic_update_slice_in_dim(
            jnp.zeros((up_bias.shape[1],), jnp.float32), up_bias_part, tensor_rank * local_hidden, 0
        )
        normed_grad = (
            attn_rows_grad * norm_gains[layer_id, 0] + mlp_rows_grad * norm_gains[layer_id, 1]
        )
        normed_mean = jnp.mean(normed_grad, axis=-1, keepdims=True)
        product_mean = jnp.mean(normed_grad * normed, axis=-1, keepdims=True)
        grad_stream = grad_stream + inverse * (normed_grad - normed_mean - normed * product_mean)
        weight_list[layer_id] = (
            chip_scatter(qkv_part, 0, 2),
            chip_scatter(proj_part, 1, 0),
            dp_scatter(up_part, 0),
            chip_scatter(down_part, 1, 0),
        )
    small_parts = (
        jnp.stack(gains_list),
        jnp.stack(biases_list),
        jnp.stack(qkv_bias_list),
        jnp.stack(up_bias_list),
    )
    flat = butterfly_sum(jnp.concatenate([part.reshape(-1) for part in small_parts]))
    small_sums = []
    offset = 0
    for part in small_parts:
        small_sums.append(flat[offset : offset + part.size].reshape(part.shape))
        offset += part.size
    gains_grad, biases_grad, qkv_bias_grad, up_bias_grad = small_sums
    qkv_grad = jnp.stack([weight_list[layer_id][0] for layer_id in range(LAYERS)])
    proj_grad = jnp.stack([weight_list[layer_id][1] for layer_id in range(LAYERS)])
    up_grad = jnp.stack([weight_list[layer_id][2] for layer_id in range(LAYERS)])
    down_grad = jnp.stack([weight_list[layer_id][3] for layer_id in range(LAYERS)])
    qkv_state_new = momentum * qkv_state + qkv_grad
    proj_state_new = momentum * proj_state + proj_grad
    up_state_new = momentum * up_state + up_grad
    down_state_new = momentum * down_state + down_grad
    rows_local = qkv_state.shape[1]
    dp_count = lax.axis_size("dp")
    dp_rank = lax.axis_index("dp")
    slot_count = 4 * LAYERS
    sub = dp_count // slot_count
    piece_width = up_state.shape[2] // sub
    slot_mats = []
    for layer_id in range(LAYERS):
        slot_mats.append(qkv_state_new[layer_id].reshape(rows_local, 3 * local_width))
        slot_mats.append(proj_state_new[layer_id].T)
        slot_mats.append(up_state_new[layer_id])
        slot_mats.append(down_state_new[layer_id].T)
    pieces = []
    for mat in slot_mats:
        width = mat.shape[1] // sub
        split = mat.reshape(rows_local, sub, width).transpose(1, 0, 2)
        pieces.append(jnp.pad(split, ((0, 0), (0, 0), (0, piece_width - width))))
    outgoing = jnp.concatenate(pieces, axis=0)
    owned = lax.all_to_all(outgoing, "dp", split_axis=0, concat_axis=0, tiled=True)
    owned = owned.reshape(dp_count * rows_local, piece_width)
    owned, flat, grad_stream = lax.optimization_barrier((owned, flat, grad_stream))
    gram = jnp.dot(owned, owned.T, precision=ns_precision)
    bit = 1
    while bit < sub:
        gram = gram + lax.ppermute(gram, "dp", swap_pairs(dp_count, bit))
        bit *= 2
    core_half = dp_rank % 2
    half_rows = gram.shape[0] // 2
    mine = lax.dynamic_slice_in_dim(gram, core_half * half_rows, half_rows, 0)
    mine = mine + lax.ppermute(mine, "tensor", [(0, 1), (1, 0)])
    other = lax.ppermute(mine, "dp", swap_pairs(dp_count, 1))
    gram = jnp.where(
        core_half == 0,
        jnp.concatenate([mine, other], axis=0),
        jnp.concatenate([other, mine], axis=0),
    )
    norm_sq = jnp.trace(gram)
    scale = 1.0 / (jnp.sqrt(norm_sq) + frobenius_eps)
    current_gram = gram * (scale * scale)
    identity = jnp.eye(current_gram.shape[0], dtype=jnp.float32)
    accumulated = None
    for iteration in range(NS_ITERS):
        squared = jnp.dot(current_gram, current_gram, precision=ns_precision)
        polynomial = coef_first * identity + coef_second * current_gram + coef_third * squared
        if accumulated is None:
            accumulated = polynomial
        else:
            accumulated = jnp.dot(polynomial, accumulated, precision=ns_precision)
        if iteration + 1 < NS_ITERS:
            current_gram = jnp.dot(
                polynomial,
                jnp.dot(current_gram, polynomial, precision=ns_precision),
                precision=ns_precision,
            )
    current = jnp.dot(accumulated, owned * scale, precision=ns_precision)
    returned = lax.all_to_all(
        current.astype(jnp.bfloat16).reshape(dp_count, rows_local, piece_width),
        "dp",
        split_axis=0,
        concat_axis=0,
        tiled=True,
    ).reshape(slot_count, sub, rows_local, piece_width)
    my_rows = []
    for slot_id, mat in enumerate(slot_mats):
        width = mat.shape[1] // sub
        my_rows.append(
            returned[slot_id, :, :, :width]
            .astype(jnp.float32)
            .transpose(1, 0, 2)
            .reshape(rows_local, sub * width)
        )
    muon_step = muon_rate * match_rms
    qkv_list, proj_list, up_list, down_list = ([], [], [], [])
    for layer_id in range(LAYERS):
        base_slot = 4 * layer_id
        qkv_ortho = my_rows[base_slot].reshape(rows_local, 3, local_width)
        proj_ortho = my_rows[base_slot + 1].T
        up_ortho = my_rows[base_slot + 2]
        down_ortho = my_rows[base_slot + 3].T
        qkv_list.append(
            qkv_weight[layer_id].astype(jnp.float32) - muon_step * math.sqrt(3 * D) * qkv_ortho
        )
        proj_list.append(
            proj_weight[layer_id].astype(jnp.float32) - muon_step * math.sqrt(D) * proj_ortho
        )
        up_list.append(
            up_weight[layer_id].astype(jnp.float32) - muon_step * math.sqrt(FF) * up_ortho
        )
        down_list.append(
            down_weight[layer_id].astype(jnp.float32) - muon_step * math.sqrt(FF) * down_ortho
        )
    qkv_new = jnp.stack(qkv_list)
    proj_new = jnp.stack(proj_list)
    up_new = jnp.stack(up_list)
    down_new = jnp.stack(down_list)
    gains_new = vector_step(norm_gains, gains_grad)
    biases_new = vector_step(biases, biases_grad)
    qkv_bias_new = vector_step(qkv_bias, qkv_bias_grad)
    up_bias_new = vector_step(up_bias, up_bias_grad)
    return (
        stream,
        grad_stream,
        qkv_grad,
        proj_grad,
        up_grad,
        down_grad,
        gains_grad,
        biases_grad,
        qkv_bias_grad,
        up_bias_grad,
        qkv_new,
        proj_new,
        up_new,
        down_new,
        gains_new,
        biases_new,
        qkv_bias_new,
        up_bias_new,
        qkv_state_new,
        proj_state_new,
        up_state_new,
        down_state_new,
    )


def solution(mesh):
    return jax.shard_map(
        local,
        mesh=mesh,
        in_specs=(
            P(("dp", "tensor"), None),
            P(("dp", "tensor"), None),
            P("dp", None),
            P(None, "dp", None, "tensor"),
            P(None, "tensor", "dp"),
            P(None, "dp", "tensor"),
            P(None, "tensor", "dp"),
            P(),
            P(),
            P(),
            P(),
            P(None, "dp", None, "tensor"),
            P(None, "tensor", "dp"),
            P(None, "dp", "tensor"),
            P(None, "tensor", "dp"),
        ),
        out_specs=(
            P(("dp", "tensor"), None),
            P(("dp", "tensor"), None),
            P(None, "dp", None, "tensor"),
            P(None, "tensor", "dp"),
            P(None, "dp", "tensor"),
            P(None, "tensor", "dp"),
            P(),
            P(),
            P(),
            P(),
            P(None, "dp", None, "tensor"),
            P(None, "tensor", "dp"),
            P(None, "dp", "tensor"),
            P(None, "tensor", "dp"),
            P(),
            P(),
            P(),
            P(),
            P(None, "dp", None, "tensor"),
            P(None, "tensor", "dp"),
            P(None, "dp", "tensor"),
            P(None, "tensor", "dp"),
        ),
        check_vma=False,
    )
```

```python
import math

import jax
import jax.numpy as jnp
from jax import lax
from jax.sharding import PartitionSpec as P

D = 768
HD = 64
FF = 3072
ROT = 16
LAYERS = 2
NS_ITERS = 5


highest = lax.Precision.HIGHEST
ns_precision = lax.Precision.HIGH
norm_eps = 1e-05
masked_score = -1e30
coef_first = 3.4445
coef_second = -4.775
coef_third = 2.0315
momentum = 0.9
muon_rate = 0.2
match_rms = 0.2
vector_rate = 0.2
vector_eps = 1e-06
frobenius_eps = 1e-07


def rotary_tables(segment_row):
    length = segment_row.shape[0]
    indices = jnp.arange(length, dtype=jnp.int32)
    change = jnp.concatenate([jnp.ones((1,), dtype=bool), segment_row[1:] != segment_row[:-1]])
    starts = lax.cummax(jnp.where(change, indices, jnp.zeros_like(indices)), axis=0)
    positions = (indices - starts).astype(jnp.float32)
    half_rot = ROT // 2
    frequency = 10000.0 ** (-2.0 * jnp.arange(half_rot, dtype=jnp.float32) / ROT)
    angles = positions[:, None] * frequency[None, :]
    return (jnp.cos(angles), jnp.sin(angles))


def rotate(values, cosine_table, sine_table):
    half_rot = ROT // 2
    first_half = values[..., :half_rot]
    second_half = values[..., half_rot:ROT]
    cos_b = cosine_table[:, None, :]
    sin_b = sine_table[:, None, :]
    return jnp.concatenate(
        [
            first_half * cos_b - second_half * sin_b,
            second_half * cos_b + first_half * sin_b,
            values[..., ROT:],
        ],
        axis=-1,
    )


def unrotate(gradient, cosine_table, sine_table):
    half_rot = ROT // 2
    first_half = gradient[..., :half_rot]
    second_half = gradient[..., half_rot:ROT]
    cos_b = cosine_table[:, None, :]
    sin_b = sine_table[:, None, :]
    return jnp.concatenate(
        [
            first_half * cos_b + second_half * sin_b,
            second_half * cos_b - first_half * sin_b,
            gradient[..., ROT:],
        ],
        axis=-1,
    )


def normalize(stream):
    centered = stream - jnp.mean(stream, axis=-1, keepdims=True)
    inverse = lax.rsqrt(jnp.mean(centered * centered, axis=-1, keepdims=True) + norm_eps)
    return (centered * inverse, inverse)


def gelu_exact(values):
    return jax.nn.gelu(values, approximate=False)


def block_mask(segment_row, block_rows):
    query_pos = jnp.arange(block_rows, dtype=jnp.int32)
    key_pos = jnp.arange(segment_row.shape[0], dtype=jnp.int32)
    return (segment_row[:, None] == segment_row[None, :]) & (query_pos[:, None] >= key_pos[None, :])


def block_scores(queries, key_rows, allowed):
    scores = jnp.einsum(
        "qhe,khe->hqk", queries, key_rows, preferred_element_type=jnp.float32
    ) * queries.shape[-1] ** (-0.5)
    return jnp.where(allowed[None], scores, masked_score)


def attend(queries, key_rows, values, segment_row):
    length = queries.shape[0]
    block_rows = min(512, length)
    allowed = block_mask(segment_row, block_rows)
    scores = block_scores(queries, key_rows, allowed)
    row_peak = jnp.max(scores, axis=-1, keepdims=True)
    exponent = jnp.exp(scores - row_peak)
    row_total = jnp.sum(exponent, axis=-1, keepdims=True)
    probs_low = (exponent / row_total).astype(jnp.bfloat16)
    outputs = jnp.einsum(
        "hqk,khe->qhe", probs_low, values, preferred_element_type=jnp.float32
    ).astype(jnp.bfloat16)
    log_sums = row_peak + jnp.log(row_total)
    return (outputs, log_sums)


def attend_back(queries, key_rows, values, heads_grad, log_sums, segment_row):
    length = queries.shape[0]
    block_rows = min(512, length)
    scale_factor = queries.shape[-1] ** (-0.5)
    allowed = block_mask(segment_row, block_rows)
    scores = block_scores(queries, key_rows, allowed)
    probs_full = jnp.exp(scores - log_sums)
    probs_grad = jnp.einsum("qhe,khe->hqk", heads_grad, values, preferred_element_type=jnp.float32)
    row_dot = jnp.sum(probs_full * probs_grad, axis=-1, keepdims=True)
    score_grad = (probs_full * (probs_grad - row_dot)).astype(jnp.bfloat16)
    value_grad = jnp.einsum(
        "hqk,qhe->khe",
        probs_full.astype(jnp.bfloat16),
        heads_grad,
        preferred_element_type=jnp.float32,
    )
    query_grads = (
        jnp.einsum("hqk,khe->qhe", score_grad, key_rows, preferred_element_type=jnp.float32)
        * scale_factor
    )
    key_grad = (
        jnp.einsum("hqk,qhe->khe", score_grad, queries, preferred_element_type=jnp.float32)
        * scale_factor
    )
    return (query_grads, key_grad, value_grad)


def dp_scatter(partial, dimension):
    return lax.psum_scatter(partial, "dp", scatter_dimension=dimension, tiled=True)


def dp_gather(block, axis):
    return lax.all_gather(block, "dp", axis=axis, tiled=True)


def swap_pairs(count, bit):
    return [(i, i ^ bit) for i in range(count)]


def butterfly_sum(flat):
    count = lax.axis_size("dp")
    bit = 1
    while bit < count:
        flat = flat + lax.ppermute(flat, "dp", swap_pairs(count, bit))
        bit *= 2
    return flat + lax.ppermute(flat, "tensor", [(0, 1), (1, 0)])


def tensor_swap(block):
    return lax.ppermute(block, "tensor", [(0, 1), (1, 0)])


def tensor_gather(block):
    other = tensor_swap(block)
    first = lax.axis_index("tensor") == 0
    return jnp.where(
        first, jnp.concatenate([block, other], axis=0), jnp.concatenate([other, block], axis=0)
    )


def tensor_scatter(partial):
    rank = lax.axis_index("tensor")
    half = partial.shape[0] // 2
    mine = lax.dynamic_slice_in_dim(partial, rank * half, half, 0)
    theirs = lax.dynamic_slice_in_dim(partial, (1 - rank) * half, half, 0)
    return mine + tensor_swap(theirs)


def chip_gather_rows(block):
    count = lax.axis_size("dp")
    parity = lax.axis_index("dp") % 2
    half = block.shape[0] // 2
    halves = block.reshape((2, half) + block.shape[1:])
    outgoing = jnp.tile(halves, (count // 2,) + (1,) * block.ndim)
    got = lax.all_to_all(outgoing, "dp", split_axis=0, concat_axis=0, tiled=True)
    theirs = lax.ppermute(got, "dp", swap_pairs(count, 1))
    pair = jnp.where(parity == 0, jnp.stack([got, theirs], axis=1), jnp.stack([theirs, got], axis=1))
    return pair.reshape((count * 2 * half,) + block.shape[1:])


def chip_scatter_rows(partial):
    count = lax.axis_size("dp")
    parity = lax.axis_index("dp") % 2
    half = partial.shape[0] // count // 2
    blocks = partial.reshape((count, 2, half) + partial.shape[1:])
    keep = lax.dynamic_index_in_dim(blocks, parity, axis=1, keepdims=False)
    send = lax.dynamic_index_in_dim(blocks, 1 - parity, axis=1, keepdims=False)
    chip_sum = keep + lax.ppermute(send, "dp", swap_pairs(count, 1))
    got = lax.all_to_all(chip_sum, "dp", split_axis=0, concat_axis=0, tiled=True)
    got = got.reshape((count // 2, 2) + got.shape[1:])
    even = jnp.sum(got[:, 0], axis=0)
    odd = jnp.sum(got[:, 1], axis=0)
    return jnp.concatenate([even, odd], axis=0)


def scatter_layer(parts):
    qkv_part, proj_part, up_part, down_part = parts
    return (
        chip_scatter_rows(qkv_part),
        chip_scatter_rows(proj_part).T,
        dp_scatter(up_part, 0),
        chip_scatter_rows(down_part).T,
    )


def vector_step(params, gradients):
    return params - vector_rate * gradients * lax.rsqrt(
        jnp.mean(gradients * gradients, axis=-1, keepdims=True) + vector_eps
    )


def local(
    block_input,
    cotangent,
    segments,
    qkv_weight,
    proj_weight,
    up_weight,
    down_weight,
    norm_gains,
    biases,
    qkv_bias,
    up_bias,
    qkv_state,
    proj_state,
    up_state,
    down_state,
):
    tensor_rank = lax.axis_index("tensor")
    local_width = qkv_weight.shape[3]
    local_hidden = up_weight.shape[2]
    head_count = local_width // HD
    model_width = block_input.shape[1]
    segment_row = segments[0]
    cosine_table, sine_table = rotary_tables(segment_row)
    stream = block_input.astype(jnp.float32)
    saved_layers = []
    for layer_id in range(LAYERS):
        layer_weights = (
            chip_gather_rows(qkv_weight[layer_id]),
            chip_gather_rows(proj_weight[layer_id].T),
            dp_gather(up_weight[layer_id], 0),
            chip_gather_rows(down_weight[layer_id].T),
        )
        qkv_full, proj_full, up_full, down_full = layer_weights
        normed, inverse = normalize(stream)
        attn_rows = (normed * norm_gains[layer_id, 0] + biases[layer_id, 0]).astype(jnp.bfloat16)
        mlp_rows = (normed * norm_gains[layer_id, 1] + biases[layer_id, 1]).astype(jnp.bfloat16)
        both_in = tensor_gather(jnp.concatenate([attn_rows, mlp_rows], axis=1))
        attn_in, mlp_in = both_in[:, :model_width], both_in[:, model_width:]
        length = attn_in.shape[0]
        qkv_local_bias = lax.dynamic_slice_in_dim(
            qkv_bias[layer_id], tensor_rank * local_width, local_width, 1
        )
        qkv_pre = (
            jnp.einsum("ld,dcf->lcf", attn_in, qkv_full, preferred_element_type=jnp.float32)
            + qkv_local_bias
        )
        shaped = qkv_pre.reshape(length, 3, head_count, HD)
        queries = rotate(shaped[:, 0], cosine_table, sine_table).astype(jnp.bfloat16)
        key_rows = rotate(shaped[:, 1], cosine_table, sine_table).astype(jnp.bfloat16)
        values = shaped[:, 2].astype(jnp.bfloat16)
        heads_out, log_sums = attend(queries, key_rows, values, segment_row)
        heads_flat = heads_out.reshape(length, local_width)
        up_local_bias = lax.dynamic_slice_in_dim(
            up_bias[layer_id], tensor_rank * local_hidden, local_hidden, 0
        )
        up_pre = jnp.dot(mlp_in, up_full, preferred_element_type=jnp.float32) + up_local_bias
        act_low = gelu_exact(up_pre).astype(jnp.bfloat16)
        partial_sum = jnp.einsum(
            "lf,df->ld", heads_flat, proj_full, preferred_element_type=jnp.float32
        ) + jnp.einsum("lf,df->ld", act_low, down_full, preferred_element_type=jnp.float32)
        branch = tensor_scatter(partial_sum)
        saved_layers.append(
            (
                normed,
                inverse,
                attn_in,
                mlp_in,
                queries,
                key_rows,
                values,
                log_sums,
                heads_flat,
                up_pre,
                act_low,
                layer_weights,
            )
        )
        stream = stream + branch + biases[layer_id, 2] + biases[layer_id, 3]
    grad_stream = cotangent.astype(jnp.float32)
    gains_list = [None] * LAYERS
    biases_list = [None] * LAYERS
    qkv_bias_list = [None] * LAYERS
    up_bias_list = [None] * LAYERS
    weight_list = [None] * LAYERS
    for layer_id in reversed(range(LAYERS)):
        (
            normed,
            inverse,
            attn_in,
            mlp_in,
            queries,
            key_rows,
            values,
            log_sums,
            heads_flat,
            up_pre,
            act_low,
            layer_weights,
        ) = saved_layers[layer_id]
        qkv_full, proj_full, up_full, down_full = layer_weights
        length = attn_in.shape[0]
        out_bias_grad = jnp.sum(grad_stream, axis=0)
        branch_grad = tensor_gather(grad_stream.astype(jnp.bfloat16))
        down_part = jnp.einsum(
            "lf,ld->df", act_low, branch_grad, preferred_element_type=jnp.float32
        )
        act_grad = jnp.einsum(
            "ld,df->lf", branch_grad, down_full, preferred_element_type=jnp.float32
        )
        gelu_back = jax.vjp(gelu_exact, up_pre)[1]
        up_pre_grad = gelu_back(act_grad)[0].astype(jnp.bfloat16)
        up_bias_part = jnp.sum(up_pre_grad, axis=0, dtype=jnp.float32)
        up_part = jnp.einsum("ld,lf->df", mlp_in, up_pre_grad, preferred_element_type=jnp.float32)
        mlp_in_grad = jnp.einsum(
            "lf,df->ld", up_pre_grad, up_full, preferred_element_type=jnp.float32
        )
        proj_part = jnp.einsum(
            "lf,ld->df", heads_flat, branch_grad, preferred_element_type=jnp.float32
        )
        heads_grad = (
            jnp.einsum("ld,df->lf", branch_grad, proj_full, preferred_element_type=jnp.float32)
            .astype(jnp.bfloat16)
            .reshape(length, head_count, HD)
        )
        query_grad, key_grad, value_grad = attend_back(
            queries, key_rows, values, heads_grad, log_sums, segment_row
        )
        qkv_pre_grad = jnp.stack(
            [
                unrotate(query_grad, cosine_table, sine_table),
                unrotate(key_grad, cosine_table, sine_table),
                value_grad,
            ],
            axis=1,
        )
        qkv_pre_grad = qkv_pre_grad.reshape(length, 3, local_width).astype(jnp.bfloat16)
        qkv_bias_part = jnp.sum(qkv_pre_grad, axis=0, dtype=jnp.float32)
        qkv_part = jnp.einsum(
            "ld,lcf->dcf", attn_in, qkv_pre_grad, preferred_element_type=jnp.float32
        )
        attn_in_grad = jnp.einsum(
            "lcf,dcf->ld", qkv_pre_grad, qkv_full, preferred_element_type=jnp.float32
        )
        both_grad = tensor_scatter(jnp.concatenate([attn_in_grad, mlp_in_grad], axis=1))
        attn_rows_grad, mlp_rows_grad = both_grad[:, :model_width], both_grad[:, model_width:]
        gains_list[layer_id] = jnp.stack(
            [jnp.sum(attn_rows_grad * normed, axis=0), jnp.sum(mlp_rows_grad * normed, axis=0)]
        )
        biases_list[layer_id] = jnp.stack(
            [
                jnp.sum(attn_rows_grad, axis=0),
                jnp.sum(mlp_rows_grad, axis=0),
                out_bias_grad,
                out_bias_grad,
            ]
        )
        qkv_bias_list[layer_id] = lax.dynamic_update_slice_in_dim(
            jnp.zeros((3, model_width), jnp.float32), qkv_bias_part, tensor_rank * local_width, 1
        )
        up_bias_list[layer_id] = lax.dynamic_update_slice_in_dim(
            jnp.zeros((up_bias.shape[1],), jnp.float32), up_bias_part, tensor_rank * local_hidden, 0
        )
        normed_grad = (
            attn_rows_grad * norm_gains[layer_id, 0] + mlp_rows_grad * norm_gains[layer_id, 1]
        )
        normed_mean = jnp.mean(normed_grad, axis=-1, keepdims=True)
        product_mean = jnp.mean(normed_grad * normed, axis=-1, keepdims=True)
        grad_stream = grad_stream + inverse * (normed_grad - normed_mean - normed * product_mean)
        weight_list[layer_id] = (qkv_part, proj_part, up_part, down_part)
        if layer_id > 0:
            weight_list[layer_id] = scatter_layer(weight_list[layer_id])
    small_parts = (
        jnp.stack(gains_list),
        jnp.stack(biases_list),
        jnp.stack(qkv_bias_list),
        jnp.stack(up_bias_list),
    )
    flat = butterfly_sum(jnp.concatenate([part.reshape(-1) for part in small_parts]))
    small_sums = []
    offset = 0
    for part in small_parts:
        small_sums.append(flat[offset : offset + part.size].reshape(part.shape))
        offset += part.size
    gains_grad, biases_grad, qkv_bias_grad, up_bias_grad = small_sums
    flat, first_parts = lax.optimization_barrier((flat, weight_list[0]))
    weight_list[0] = scatter_layer(first_parts)
    qkv_grad = jnp.stack([weight_list[layer_id][0] for layer_id in range(LAYERS)])
    proj_grad = jnp.stack([weight_list[layer_id][1] for layer_id in range(LAYERS)])
    up_grad = jnp.stack([weight_list[layer_id][2] for layer_id in range(LAYERS)])
    down_grad = jnp.stack([weight_list[layer_id][3] for layer_id in range(LAYERS)])
    qkv_state_new = momentum * qkv_state + qkv_grad
    proj_state_new = momentum * proj_state + proj_grad
    up_state_new = momentum * up_state + up_grad
    down_state_new = momentum * down_state + down_grad
    rows_local = qkv_state.shape[1]
    dp_count = lax.axis_size("dp")
    dp_rank = lax.axis_index("dp")
    slot_count = 4 * LAYERS
    sub = dp_count // slot_count
    piece_width = up_state.shape[2] // sub
    slot_mats = []
    for layer_id in range(LAYERS):
        slot_mats.append(qkv_state_new[layer_id].reshape(rows_local, 3 * local_width))
        slot_mats.append(proj_state_new[layer_id].T)
        slot_mats.append(up_state_new[layer_id])
        slot_mats.append(down_state_new[layer_id].T)
    pieces = []
    for mat in slot_mats:
        width = mat.shape[1] // sub
        split = mat.reshape(rows_local, sub, width).transpose(1, 0, 2)
        pieces.append(jnp.pad(split, ((0, 0), (0, 0), (0, piece_width - width))))
    outgoing = jnp.concatenate(pieces, axis=0)
    owned = lax.all_to_all(outgoing, "dp", split_axis=0, concat_axis=0, tiled=True)
    owned = owned.reshape(dp_count * rows_local, piece_width)
    owned, grad_stream = lax.optimization_barrier((owned, grad_stream))
    gram = jnp.dot(owned, owned.T, precision=ns_precision)
    bit = 1
    while bit < sub:
        gram = gram + lax.ppermute(gram, "dp", swap_pairs(dp_count, bit))
        bit *= 2
    core_half = dp_rank % 2
    half_rows = gram.shape[0] // 2
    mine = lax.dynamic_slice_in_dim(gram, core_half * half_rows, half_rows, 0)
    mine = mine + lax.ppermute(mine, "tensor", [(0, 1), (1, 0)])
    other = lax.ppermute(mine, "dp", swap_pairs(dp_count, 1))
    gram = jnp.where(
        core_half == 0,
        jnp.concatenate([mine, other], axis=0),
        jnp.concatenate([other, mine], axis=0),
    )
    norm_sq = jnp.trace(gram)
    scale = 1.0 / (jnp.sqrt(norm_sq) + frobenius_eps)
    current_gram = gram * (scale * scale)
    identity = jnp.eye(current_gram.shape[0], dtype=jnp.float32)
    accumulated = None
    for iteration in range(NS_ITERS):
        squared = jnp.dot(current_gram, current_gram, precision=ns_precision)
        polynomial = coef_first * identity + coef_second * current_gram + coef_third * squared
        if accumulated is None:
            accumulated = polynomial
        else:
            accumulated = jnp.dot(polynomial, accumulated, precision=ns_precision)
        if iteration + 1 < NS_ITERS:
            current_gram = jnp.dot(
                polynomial,
                jnp.dot(current_gram, polynomial, precision=ns_precision),
                precision=ns_precision,
            )
    current = jnp.dot(accumulated, owned * scale, precision=ns_precision)
    returned = lax.all_to_all(
        current.astype(jnp.bfloat16).reshape(dp_count, rows_local, piece_width),
        "dp",
        split_axis=0,
        concat_axis=0,
        tiled=True,
    ).reshape(slot_count, sub, rows_local, piece_width)
    my_rows = []
    for slot_id, mat in enumerate(slot_mats):
        width = mat.shape[1] // sub
        my_rows.append(
            returned[slot_id, :, :, :width]
            .astype(jnp.float32)
            .transpose(1, 0, 2)
            .reshape(rows_local, sub * width)
        )
    muon_step = muon_rate * match_rms
    qkv_list, proj_list, up_list, down_list = ([], [], [], [])
    for layer_id in range(LAYERS):
        base_slot = 4 * layer_id
        qkv_ortho = my_rows[base_slot].reshape(rows_local, 3, local_width)
        proj_ortho = my_rows[base_slot + 1].T
        up_ortho = my_rows[base_slot + 2]
        down_ortho = my_rows[base_slot + 3].T
        qkv_list.append(
            qkv_weight[layer_id].astype(jnp.float32) - muon_step * math.sqrt(3 * D) * qkv_ortho
        )
        proj_list.append(
            proj_weight[layer_id].astype(jnp.float32) - muon_step * math.sqrt(D) * proj_ortho
        )
        up_list.append(
            up_weight[layer_id].astype(jnp.float32) - muon_step * math.sqrt(FF) * up_ortho
        )
        down_list.append(
            down_weight[layer_id].astype(jnp.float32) - muon_step * math.sqrt(FF) * down_ortho
        )
    qkv_new = jnp.stack(qkv_list)
    proj_new = jnp.stack(proj_list)
    up_new = jnp.stack(up_list)
    down_new = jnp.stack(down_list)
    gains_new = vector_step(norm_gains, gains_grad)
    biases_new = vector_step(biases, biases_grad)
    qkv_bias_new = vector_step(qkv_bias, qkv_bias_grad)
    up_bias_new = vector_step(up_bias, up_bias_grad)
    return (
        stream,
        grad_stream,
        qkv_grad,
        proj_grad,
        up_grad,
        down_grad,
        gains_grad,
        biases_grad,
        qkv_bias_grad,
        up_bias_grad,
        qkv_new,
        proj_new,
        up_new,
        down_new,
        gains_new,
        biases_new,
        qkv_bias_new,
        up_bias_new,
        qkv_state_new,
        proj_state_new,
        up_state_new,
        down_state_new,
    )


def solution(mesh):
    return jax.shard_map(
        local,
        mesh=mesh,
        in_specs=(
            P(("dp", "tensor"), None),
            P(("dp", "tensor"), None),
            P("dp", None),
            P(None, "dp", None, "tensor"),
            P(None, "tensor", "dp"),
            P(None, "dp", "tensor"),
            P(None, "tensor", "dp"),
            P(),
            P(),
            P(),
            P(),
            P(None, "dp", None, "tensor"),
            P(None, "tensor", "dp"),
            P(None, "dp", "tensor"),
            P(None, "tensor", "dp"),
        ),
        out_specs=(
            P(("dp", "tensor"), None),
            P(("dp", "tensor"), None),
            P(None, "dp", None, "tensor"),
            P(None, "tensor", "dp"),
            P(None, "dp", "tensor"),
            P(None, "tensor", "dp"),
            P(),
            P(),
            P(),
            P(),
            P(None, "dp", None, "tensor"),
            P(None, "tensor", "dp"),
            P(None, "dp", "tensor"),
            P(None, "tensor", "dp"),
            P(),
            P(),
            P(),
            P(),
            P(None, "dp", None, "tensor"),
            P(None, "tensor", "dp"),
            P(None, "dp", "tensor"),
            P(None, "tensor", "dp"),
        ),
        check_vma=False,
    )
```

```python
import math

import jax
import jax.numpy as jnp
from jax import lax
from jax.sharding import PartitionSpec as P

D = 768
HD = 64
FF = 3072
ROT = 16
LAYERS = 2
NS_ITERS = 5


highest = lax.Precision.HIGHEST
ns_precision = lax.Precision.HIGH
norm_eps = 1e-05
masked_score = -1e30
coef_first = 3.4445
coef_second = -4.775
coef_third = 2.0315
momentum = 0.9
muon_rate = 0.2
match_rms = 0.2
vector_rate = 0.2
vector_eps = 1e-06
frobenius_eps = 1e-07


def rotary_tables(segment_row):
    length = segment_row.shape[0]
    indices = jnp.arange(length, dtype=jnp.int32)
    change = jnp.concatenate([jnp.ones((1,), dtype=bool), segment_row[1:] != segment_row[:-1]])
    starts = lax.cummax(jnp.where(change, indices, jnp.zeros_like(indices)), axis=0)
    positions = (indices - starts).astype(jnp.float32)
    half_rot = ROT // 2
    frequency = 10000.0 ** (-2.0 * jnp.arange(half_rot, dtype=jnp.float32) / ROT)
    angles = positions[:, None] * frequency[None, :]
    return (jnp.cos(angles), jnp.sin(angles))


def rotate(values, cosine_table, sine_table):
    half_rot = ROT // 2
    first_half = values[..., :half_rot]
    second_half = values[..., half_rot:ROT]
    cos_b = cosine_table[:, None, :]
    sin_b = sine_table[:, None, :]
    return jnp.concatenate(
        [
            first_half * cos_b - second_half * sin_b,
            second_half * cos_b + first_half * sin_b,
            values[..., ROT:],
        ],
        axis=-1,
    )


def unrotate(gradient, cosine_table, sine_table):
    half_rot = ROT // 2
    first_half = gradient[..., :half_rot]
    second_half = gradient[..., half_rot:ROT]
    cos_b = cosine_table[:, None, :]
    sin_b = sine_table[:, None, :]
    return jnp.concatenate(
        [
            first_half * cos_b + second_half * sin_b,
            second_half * cos_b - first_half * sin_b,
            gradient[..., ROT:],
        ],
        axis=-1,
    )


def normalize(stream):
    centered = stream - jnp.mean(stream, axis=-1, keepdims=True)
    inverse = lax.rsqrt(jnp.mean(centered * centered, axis=-1, keepdims=True) + norm_eps)
    return (centered * inverse, inverse)


def gelu_exact(values):
    return jax.nn.gelu(values, approximate=False)


def block_mask(segment_row, block_rows):
    query_pos = jnp.arange(block_rows, dtype=jnp.int32)
    key_pos = jnp.arange(segment_row.shape[0], dtype=jnp.int32)
    return (segment_row[:, None] == segment_row[None, :]) & (query_pos[:, None] >= key_pos[None, :])


def block_scores(queries, key_rows, allowed):
    scores = jnp.einsum(
        "qhe,khe->hqk", queries, key_rows, preferred_element_type=jnp.float32
    ) * queries.shape[-1] ** (-0.5)
    return jnp.where(allowed[None], scores, masked_score)


def attend(queries, key_rows, values, segment_row):
    length = queries.shape[0]
    block_rows = min(512, length)
    allowed = block_mask(segment_row, block_rows)
    scores = block_scores(queries, key_rows, allowed)
    row_peak = jnp.max(scores, axis=-1, keepdims=True)
    exponent = jnp.exp(scores - row_peak)
    row_total = jnp.sum(exponent, axis=-1, keepdims=True)
    probs_low = (exponent / row_total).astype(jnp.bfloat16)
    outputs = jnp.einsum(
        "hqk,khe->qhe", probs_low, values, preferred_element_type=jnp.float32
    ).astype(jnp.bfloat16)
    log_sums = row_peak + jnp.log(row_total)
    return (outputs, log_sums)


def attend_back(queries, key_rows, values, heads_grad, log_sums, segment_row):
    length = queries.shape[0]
    block_rows = min(512, length)
    scale_factor = queries.shape[-1] ** (-0.5)
    allowed = block_mask(segment_row, block_rows)
    scores = block_scores(queries, key_rows, allowed)
    probs_full = jnp.exp(scores - log_sums)
    probs_grad = jnp.einsum("qhe,khe->hqk", heads_grad, values, preferred_element_type=jnp.float32)
    row_dot = jnp.sum(probs_full * probs_grad, axis=-1, keepdims=True)
    score_grad = (probs_full * (probs_grad - row_dot)).astype(jnp.bfloat16)
    value_grad = jnp.einsum(
        "hqk,qhe->khe",
        probs_full.astype(jnp.bfloat16),
        heads_grad,
        preferred_element_type=jnp.float32,
    )
    query_grads = (
        jnp.einsum("hqk,khe->qhe", score_grad, key_rows, preferred_element_type=jnp.float32)
        * scale_factor
    )
    key_grad = (
        jnp.einsum("hqk,qhe->khe", score_grad, queries, preferred_element_type=jnp.float32)
        * scale_factor
    )
    return (query_grads, key_grad, value_grad)


def dp_scatter(partial, dimension):
    return lax.psum_scatter(partial, "dp", scatter_dimension=dimension, tiled=True)


def dp_gather(block, axis):
    return lax.all_gather(block, "dp", axis=axis, tiled=True)


def swap_pairs(count, bit):
    return [(i, i ^ bit) for i in range(count)]


def butterfly_sum(flat):
    count = lax.axis_size("dp")
    bit = 1
    while bit < count:
        flat = flat + lax.ppermute(flat, "dp", swap_pairs(count, bit))
        bit *= 2
    return flat + lax.ppermute(flat, "tensor", [(0, 1), (1, 0)])


def tensor_swap(block):
    return lax.ppermute(block, "tensor", [(0, 1), (1, 0)])


def tensor_gather(block):
    other = tensor_swap(block)
    first = lax.axis_index("tensor") == 0
    return jnp.where(
        first, jnp.concatenate([block, other], axis=0), jnp.concatenate([other, block], axis=0)
    )


def tensor_scatter(partial):
    rank = lax.axis_index("tensor")
    half = partial.shape[0] // 2
    mine = lax.dynamic_slice_in_dim(partial, rank * half, half, 0)
    theirs = lax.dynamic_slice_in_dim(partial, (1 - rank) * half, half, 0)
    return mine + tensor_swap(theirs)


def chip_gather_rows(block):
    count = lax.axis_size("dp")
    parity = lax.axis_index("dp") % 2
    half = block.shape[0] // 2
    halves = block.reshape((2, half) + block.shape[1:])
    outgoing = jnp.tile(halves, (count // 2,) + (1,) * block.ndim)
    got = lax.all_to_all(outgoing, "dp", split_axis=0, concat_axis=0, tiled=True)
    theirs = lax.ppermute(got, "dp", swap_pairs(count, 1))
    pair = jnp.where(parity == 0, jnp.stack([got, theirs], axis=1), jnp.stack([theirs, got], axis=1))
    return pair.reshape((count * 2 * half,) + block.shape[1:])


def chip_scatter_rows(partial):
    count = lax.axis_size("dp")
    parity = lax.axis_index("dp") % 2
    half = partial.shape[0] // count // 2
    blocks = partial.reshape((count, 2, half) + partial.shape[1:])
    keep = lax.dynamic_index_in_dim(blocks, parity, axis=1, keepdims=False)
    send = lax.dynamic_index_in_dim(blocks, 1 - parity, axis=1, keepdims=False)
    chip_sum = keep + lax.ppermute(send, "dp", swap_pairs(count, 1))
    got = lax.all_to_all(chip_sum, "dp", split_axis=0, concat_axis=0, tiled=True)
    got = got.reshape((count // 2, 2) + got.shape[1:])
    even = jnp.sum(got[:, 0], axis=0)
    odd = jnp.sum(got[:, 1], axis=0)
    return jnp.concatenate([even, odd], axis=0)


def scatter_layer(parts):
    qkv_part, proj_part, up_part, down_part = parts
    return (
        chip_scatter_rows(qkv_part),
        chip_scatter_rows(proj_part).T,
        dp_scatter(up_part, 0),
        chip_scatter_rows(down_part).T,
    )


def orthogonal_rows(slot_mats, rows_local, keep_with=None):
    dp_count = lax.axis_size("dp")
    dp_rank = lax.axis_index("dp")
    slot_count = len(slot_mats)
    sub = dp_count // slot_count
    piece_width = max(mat.shape[1] for mat in slot_mats) // sub
    pieces = []
    for mat in slot_mats:
        width = mat.shape[1] // sub
        split = mat.reshape(rows_local, sub, width).transpose(1, 0, 2)
        pieces.append(jnp.pad(split, ((0, 0), (0, 0), (0, piece_width - width))))
    outgoing = jnp.concatenate(pieces, axis=0)
    owned = lax.all_to_all(outgoing, "dp", split_axis=0, concat_axis=0, tiled=True)
    owned = owned.reshape(dp_count * rows_local, piece_width)
    if keep_with is not None:
        owned, keep_with = lax.optimization_barrier((owned, keep_with))
    gram = jnp.dot(owned, owned.T, precision=ns_precision)
    bit = 1
    while bit < sub:
        gram = gram + lax.ppermute(gram, "dp", swap_pairs(dp_count, bit))
        bit *= 2
    core_half = dp_rank % 2
    half_rows = gram.shape[0] // 2
    mine = lax.dynamic_slice_in_dim(gram, core_half * half_rows, half_rows, 0)
    mine = mine + lax.ppermute(mine, "tensor", [(0, 1), (1, 0)])
    other = lax.ppermute(mine, "dp", swap_pairs(dp_count, 1))
    gram = jnp.where(
        core_half == 0,
        jnp.concatenate([mine, other], axis=0),
        jnp.concatenate([other, mine], axis=0),
    )
    norm_sq = jnp.trace(gram)
    scale = 1.0 / (jnp.sqrt(norm_sq) + frobenius_eps)
    current_gram = gram * (scale * scale)
    identity = jnp.eye(current_gram.shape[0], dtype=jnp.float32)
    accumulated = None
    for iteration in range(NS_ITERS):
        squared = jnp.dot(current_gram, current_gram, precision=ns_precision)
        polynomial = coef_first * identity + coef_second * current_gram + coef_third * squared
        if accumulated is None:
            accumulated = polynomial
        else:
            accumulated = jnp.dot(polynomial, accumulated, precision=ns_precision)
        if iteration + 1 < NS_ITERS:
            current_gram = jnp.dot(
                polynomial,
                jnp.dot(current_gram, polynomial, precision=ns_precision),
                precision=ns_precision,
            )
    current = jnp.dot(accumulated, owned * scale, precision=ns_precision)
    returned = lax.all_to_all(
        current.astype(jnp.bfloat16).reshape(dp_count, rows_local, piece_width),
        "dp",
        split_axis=0,
        concat_axis=0,
        tiled=True,
    ).reshape(slot_count, sub, rows_local, piece_width)
    my_rows = []
    for slot_id, mat in enumerate(slot_mats):
        width = mat.shape[1] // sub
        my_rows.append(
            returned[slot_id, :, :, :width]
            .astype(jnp.float32)
            .transpose(1, 0, 2)
            .reshape(rows_local, sub * width)
        )
    return my_rows, keep_with


def vector_step(params, gradients):
    return params - vector_rate * gradients * lax.rsqrt(
        jnp.mean(gradients * gradients, axis=-1, keepdims=True) + vector_eps
    )


def local(
    block_input,
    cotangent,
    segments,
    qkv_weight,
    proj_weight,
    up_weight,
    down_weight,
    norm_gains,
    biases,
    qkv_bias,
    up_bias,
    qkv_state,
    proj_state,
    up_state,
    down_state,
):
    tensor_rank = lax.axis_index("tensor")
    local_width = qkv_weight.shape[3]
    local_hidden = up_weight.shape[2]
    head_count = local_width // HD
    model_width = block_input.shape[1]
    segment_row = segments[0]
    cosine_table, sine_table = rotary_tables(segment_row)
    stream = block_input.astype(jnp.float32)
    saved_layers = []
    for layer_id in range(LAYERS):
        layer_weights = (
            chip_gather_rows(qkv_weight[layer_id]),
            chip_gather_rows(proj_weight[layer_id].T),
            dp_gather(up_weight[layer_id], 0),
            chip_gather_rows(down_weight[layer_id].T),
        )
        qkv_full, proj_full, up_full, down_full = layer_weights
        normed, inverse = normalize(stream)
        attn_rows = (normed * norm_gains[layer_id, 0] + biases[layer_id, 0]).astype(jnp.bfloat16)
        mlp_rows = (normed * norm_gains[layer_id, 1] + biases[layer_id, 1]).astype(jnp.bfloat16)
        both_in = tensor_gather(jnp.concatenate([attn_rows, mlp_rows], axis=1))
        attn_in, mlp_in = both_in[:, :model_width], both_in[:, model_width:]
        length = attn_in.shape[0]
        qkv_local_bias = lax.dynamic_slice_in_dim(
            qkv_bias[layer_id], tensor_rank * local_width, local_width, 1
        )
        qkv_pre = (
            jnp.einsum("ld,dcf->lcf", attn_in, qkv_full, preferred_element_type=jnp.float32)
            + qkv_local_bias
        )
        shaped = qkv_pre.reshape(length, 3, head_count, HD)
        queries = rotate(shaped[:, 0], cosine_table, sine_table).astype(jnp.bfloat16)
        key_rows = rotate(shaped[:, 1], cosine_table, sine_table).astype(jnp.bfloat16)
        values = shaped[:, 2].astype(jnp.bfloat16)
        heads_out, log_sums = attend(queries, key_rows, values, segment_row)
        heads_flat = heads_out.reshape(length, local_width)
        up_local_bias = lax.dynamic_slice_in_dim(
            up_bias[layer_id], tensor_rank * local_hidden, local_hidden, 0
        )
        up_pre = jnp.dot(mlp_in, up_full, preferred_element_type=jnp.float32) + up_local_bias
        act_low = gelu_exact(up_pre).astype(jnp.bfloat16)
        partial_sum = jnp.einsum(
            "lf,df->ld", heads_flat, proj_full, preferred_element_type=jnp.float32
        ) + jnp.einsum("lf,df->ld", act_low, down_full, preferred_element_type=jnp.float32)
        branch = tensor_scatter(partial_sum)
        saved_layers.append(
            (
                normed,
                inverse,
                attn_in,
                mlp_in,
                queries,
                key_rows,
                values,
                log_sums,
                heads_flat,
                up_pre,
                act_low,
                layer_weights,
            )
        )
        stream = stream + branch + biases[layer_id, 2] + biases[layer_id, 3]
    grad_stream = cotangent.astype(jnp.float32)
    gains_list = [None] * LAYERS
    biases_list = [None] * LAYERS
    qkv_bias_list = [None] * LAYERS
    up_bias_list = [None] * LAYERS
    weight_list = [None] * LAYERS
    for layer_id in reversed(range(LAYERS)):
        (
            normed,
            inverse,
            attn_in,
            mlp_in,
            queries,
            key_rows,
            values,
            log_sums,
            heads_flat,
            up_pre,
            act_low,
            layer_weights,
        ) = saved_layers[layer_id]
        qkv_full, proj_full, up_full, down_full = layer_weights
        length = attn_in.shape[0]
        out_bias_grad = jnp.sum(grad_stream, axis=0)
        branch_grad = tensor_gather(grad_stream.astype(jnp.bfloat16))
        down_part = jnp.einsum(
            "lf,ld->df", act_low, branch_grad, preferred_element_type=jnp.float32
        )
        act_grad = jnp.einsum(
            "ld,df->lf", branch_grad, down_full, preferred_element_type=jnp.float32
        )
        gelu_back = jax.vjp(gelu_exact, up_pre)[1]
        up_pre_grad = gelu_back(act_grad)[0].astype(jnp.bfloat16)
        up_bias_part = jnp.sum(up_pre_grad, axis=0, dtype=jnp.float32)
        up_part = jnp.einsum("ld,lf->df", mlp_in, up_pre_grad, preferred_element_type=jnp.float32)
        mlp_in_grad = jnp.einsum(
            "lf,df->ld", up_pre_grad, up_full, preferred_element_type=jnp.float32
        )
        proj_part = jnp.einsum(
            "lf,ld->df", heads_flat, branch_grad, preferred_element_type=jnp.float32
        )
        heads_grad = (
            jnp.einsum("ld,df->lf", branch_grad, proj_full, preferred_element_type=jnp.float32)
            .astype(jnp.bfloat16)
            .reshape(length, head_count, HD)
        )
        query_grad, key_grad, value_grad = attend_back(
            queries, key_rows, values, heads_grad, log_sums, segment_row
        )
        qkv_pre_grad = jnp.stack(
            [
                unrotate(query_grad, cosine_table, sine_table),
                unrotate(key_grad, cosine_table, sine_table),
                value_grad,
            ],
            axis=1,
        )
        qkv_pre_grad = qkv_pre_grad.reshape(length, 3, local_width).astype(jnp.bfloat16)
        qkv_bias_part = jnp.sum(qkv_pre_grad, axis=0, dtype=jnp.float32)
        qkv_part = jnp.einsum(
            "ld,lcf->dcf", attn_in, qkv_pre_grad, preferred_element_type=jnp.float32
        )
        attn_in_grad = jnp.einsum(
            "lcf,dcf->ld", qkv_pre_grad, qkv_full, preferred_element_type=jnp.float32
        )
        both_grad = tensor_scatter(jnp.concatenate([attn_in_grad, mlp_in_grad], axis=1))
        attn_rows_grad, mlp_rows_grad = both_grad[:, :model_width], both_grad[:, model_width:]
        gains_list[layer_id] = jnp.stack(
            [jnp.sum(attn_rows_grad * normed, axis=0), jnp.sum(mlp_rows_grad * normed, axis=0)]
        )
        biases_list[layer_id] = jnp.stack(
            [
                jnp.sum(attn_rows_grad, axis=0),
                jnp.sum(mlp_rows_grad, axis=0),
                out_bias_grad,
                out_bias_grad,
            ]
        )
        qkv_bias_list[layer_id] = lax.dynamic_update_slice_in_dim(
            jnp.zeros((3, model_width), jnp.float32), qkv_bias_part, tensor_rank * local_width, 1
        )
        up_bias_list[layer_id] = lax.dynamic_update_slice_in_dim(
            jnp.zeros((up_bias.shape[1],), jnp.float32), up_bias_part, tensor_rank * local_hidden, 0
        )
        normed_grad = (
            attn_rows_grad * norm_gains[layer_id, 0] + mlp_rows_grad * norm_gains[layer_id, 1]
        )
        normed_mean = jnp.mean(normed_grad, axis=-1, keepdims=True)
        product_mean = jnp.mean(normed_grad * normed, axis=-1, keepdims=True)
        grad_stream = grad_stream + inverse * (normed_grad - normed_mean - normed * product_mean)
        weight_list[layer_id] = (qkv_part, proj_part, up_part, down_part)
        if layer_id > 0:
            weight_list[layer_id] = scatter_layer(weight_list[layer_id])
    small_parts = (
        jnp.stack(gains_list),
        jnp.stack(biases_list),
        jnp.stack(qkv_bias_list),
        jnp.stack(up_bias_list),
    )
    flat = butterfly_sum(jnp.concatenate([part.reshape(-1) for part in small_parts]))
    small_sums = []
    offset = 0
    for part in small_parts:
        small_sums.append(flat[offset : offset + part.size].reshape(part.shape))
        offset += part.size
    gains_grad, biases_grad, qkv_bias_grad, up_bias_grad = small_sums
    flat, first_parts = lax.optimization_barrier((flat, weight_list[0]))
    weight_list[0] = scatter_layer(first_parts)
    qkv_grad = jnp.stack([weight_list[layer_id][0] for layer_id in range(LAYERS)])
    proj_grad = jnp.stack([weight_list[layer_id][1] for layer_id in range(LAYERS)])
    up_grad = jnp.stack([weight_list[layer_id][2] for layer_id in range(LAYERS)])
    down_grad = jnp.stack([weight_list[layer_id][3] for layer_id in range(LAYERS)])
    qkv_states = [momentum * qkv_state[i] + weight_list[i][0] for i in range(LAYERS)]
    proj_states = [momentum * proj_state[i] + weight_list[i][1] for i in range(LAYERS)]
    up_states = [momentum * up_state[i] + weight_list[i][2] for i in range(LAYERS)]
    down_states = [momentum * down_state[i] + weight_list[i][3] for i in range(LAYERS)]
    qkv_state_new = jnp.stack(qkv_states)
    proj_state_new = jnp.stack(proj_states)
    up_state_new = jnp.stack(up_states)
    down_state_new = jnp.stack(down_states)
    rows_local = qkv_state.shape[1]
    my_rows = [None] * LAYERS
    for layer_id in reversed(range(LAYERS)):
        slot_mats = [
            qkv_states[layer_id].reshape(rows_local, 3 * local_width),
            proj_states[layer_id].T,
            up_states[layer_id],
            down_states[layer_id].T,
        ]
        keep_with = grad_stream if layer_id == 0 else None
        my_rows[layer_id], keep_with = orthogonal_rows(slot_mats, rows_local, keep_with)
        if layer_id == 0:
            grad_stream = keep_with
    muon_step = muon_rate * match_rms
    qkv_list, proj_list, up_list, down_list = ([], [], [], [])
    for layer_id in range(LAYERS):
        qkv_ortho = my_rows[layer_id][0].reshape(rows_local, 3, local_width)
        proj_ortho = my_rows[layer_id][1].T
        up_ortho = my_rows[layer_id][2]
        down_ortho = my_rows[layer_id][3].T
        qkv_list.append(
            qkv_weight[layer_id].astype(jnp.float32) - muon_step * math.sqrt(3 * D) * qkv_ortho
        )
        proj_list.append(
            proj_weight[layer_id].astype(jnp.float32) - muon_step * math.sqrt(D) * proj_ortho
        )
        up_list.append(
            up_weight[layer_id].astype(jnp.float32) - muon_step * math.sqrt(FF) * up_ortho
        )
        down_list.append(
            down_weight[layer_id].astype(jnp.float32) - muon_step * math.sqrt(FF) * down_ortho
        )
    qkv_new = jnp.stack(qkv_list)
    proj_new = jnp.stack(proj_list)
    up_new = jnp.stack(up_list)
    down_new = jnp.stack(down_list)
    gains_new = vector_step(norm_gains, gains_grad)
    biases_new = vector_step(biases, biases_grad)
    qkv_bias_new = vector_step(qkv_bias, qkv_bias_grad)
    up_bias_new = vector_step(up_bias, up_bias_grad)
    return (
        stream,
        grad_stream,
        qkv_grad,
        proj_grad,
        up_grad,
        down_grad,
        gains_grad,
        biases_grad,
        qkv_bias_grad,
        up_bias_grad,
        qkv_new,
        proj_new,
        up_new,
        down_new,
        gains_new,
        biases_new,
        qkv_bias_new,
        up_bias_new,
        qkv_state_new,
        proj_state_new,
        up_state_new,
        down_state_new,
    )


def solution(mesh):
    return jax.shard_map(
        local,
        mesh=mesh,
        in_specs=(
            P(("dp", "tensor"), None),
            P(("dp", "tensor"), None),
            P("dp", None),
            P(None, "dp", None, "tensor"),
            P(None, "tensor", "dp"),
            P(None, "dp", "tensor"),
            P(None, "tensor", "dp"),
            P(),
            P(),
            P(),
            P(),
            P(None, "dp", None, "tensor"),
            P(None, "tensor", "dp"),
            P(None, "dp", "tensor"),
            P(None, "tensor", "dp"),
        ),
        out_specs=(
            P(("dp", "tensor"), None),
            P(("dp", "tensor"), None),
            P(None, "dp", None, "tensor"),
            P(None, "tensor", "dp"),
            P(None, "dp", "tensor"),
            P(None, "tensor", "dp"),
            P(),
            P(),
            P(),
            P(),
            P(None, "dp", None, "tensor"),
            P(None, "tensor", "dp"),
            P(None, "dp", "tensor"),
            P(None, "tensor", "dp"),
            P(),
            P(),
            P(),
            P(),
            P(None, "dp", None, "tensor"),
            P(None, "tensor", "dp"),
            P(None, "dp", "tensor"),
            P(None, "tensor", "dp"),
        ),
        check_vma=False,
    )
```

```python
import math

import jax
import jax.numpy as jnp
from jax import lax
from jax.sharding import PartitionSpec as P

D = 768
HD = 64
FF = 3072
ROT = 16
LAYERS = 2
NS_ITERS = 5


highest = lax.Precision.HIGHEST
ns_precision = lax.Precision.HIGH
norm_eps = 1e-05
masked_score = -1e30
coef_first = 3.4445
coef_second = -4.775
coef_third = 2.0315
momentum = 0.9
muon_rate = 0.2
match_rms = 0.2
vector_rate = 0.2
vector_eps = 1e-06
frobenius_eps = 1e-07


def rotary_tables(segment_row):
    length = segment_row.shape[0]
    indices = jnp.arange(length, dtype=jnp.int32)
    change = jnp.concatenate([jnp.ones((1,), dtype=bool), segment_row[1:] != segment_row[:-1]])
    starts = lax.cummax(jnp.where(change, indices, jnp.zeros_like(indices)), axis=0)
    positions = (indices - starts).astype(jnp.float32)
    half_rot = ROT // 2
    frequency = 10000.0 ** (-2.0 * jnp.arange(half_rot, dtype=jnp.float32) / ROT)
    angles = positions[:, None] * frequency[None, :]
    return (jnp.cos(angles), jnp.sin(angles))


def rotate(values, cosine_table, sine_table):
    half_rot = ROT // 2
    first_half = values[..., :half_rot]
    second_half = values[..., half_rot:ROT]
    cos_b = cosine_table[:, None, :]
    sin_b = sine_table[:, None, :]
    return jnp.concatenate(
        [
            first_half * cos_b - second_half * sin_b,
            second_half * cos_b + first_half * sin_b,
            values[..., ROT:],
        ],
        axis=-1,
    )


def unrotate(gradient, cosine_table, sine_table):
    half_rot = ROT // 2
    first_half = gradient[..., :half_rot]
    second_half = gradient[..., half_rot:ROT]
    cos_b = cosine_table[:, None, :]
    sin_b = sine_table[:, None, :]
    return jnp.concatenate(
        [
            first_half * cos_b + second_half * sin_b,
            second_half * cos_b - first_half * sin_b,
            gradient[..., ROT:],
        ],
        axis=-1,
    )


def normalize(stream):
    centered = stream - jnp.mean(stream, axis=-1, keepdims=True)
    inverse = lax.rsqrt(jnp.mean(centered * centered, axis=-1, keepdims=True) + norm_eps)
    return (centered * inverse, inverse)


def gelu_exact(values):
    return jax.nn.gelu(values, approximate=False)


def block_mask(segment_row, block_rows):
    query_pos = jnp.arange(block_rows, dtype=jnp.int32)
    key_pos = jnp.arange(segment_row.shape[0], dtype=jnp.int32)
    return (segment_row[:, None] == segment_row[None, :]) & (query_pos[:, None] >= key_pos[None, :])


def block_scores(queries, key_rows, allowed):
    scores = jnp.einsum(
        "qhe,khe->hqk", queries, key_rows, preferred_element_type=jnp.float32
    ) * queries.shape[-1] ** (-0.5)
    return jnp.where(allowed[None], scores, masked_score)


def attend(queries, key_rows, values, segment_row):
    length = queries.shape[0]
    block_rows = min(512, length)
    allowed = block_mask(segment_row, block_rows)
    scores = block_scores(queries, key_rows, allowed)
    row_peak = jnp.max(scores, axis=-1, keepdims=True)
    exponent = jnp.exp(scores - row_peak)
    row_total = jnp.sum(exponent, axis=-1, keepdims=True)
    probs_low = (exponent / row_total).astype(jnp.bfloat16)
    outputs = jnp.einsum(
        "hqk,khe->qhe", probs_low, values, preferred_element_type=jnp.float32
    ).astype(jnp.bfloat16)
    log_sums = row_peak + jnp.log(row_total)
    return (outputs, log_sums)


def attend_back(queries, key_rows, values, heads_grad, log_sums, segment_row):
    length = queries.shape[0]
    block_rows = min(512, length)
    scale_factor = queries.shape[-1] ** (-0.5)
    allowed = block_mask(segment_row, block_rows)
    scores = block_scores(queries, key_rows, allowed)
    probs_full = jnp.exp(scores - log_sums)
    probs_grad = jnp.einsum("qhe,khe->hqk", heads_grad, values, preferred_element_type=jnp.float32)
    row_dot = jnp.sum(probs_full * probs_grad, axis=-1, keepdims=True)
    score_grad = (probs_full * (probs_grad - row_dot)).astype(jnp.bfloat16)
    value_grad = jnp.einsum(
        "hqk,qhe->khe",
        probs_full.astype(jnp.bfloat16),
        heads_grad,
        preferred_element_type=jnp.float32,
    )
    query_grads = (
        jnp.einsum("hqk,khe->qhe", score_grad, key_rows, preferred_element_type=jnp.float32)
        * scale_factor
    )
    key_grad = (
        jnp.einsum("hqk,qhe->khe", score_grad, queries, preferred_element_type=jnp.float32)
        * scale_factor
    )
    return (query_grads, key_grad, value_grad)


def dp_scatter(partial, dimension):
    return lax.psum_scatter(partial, "dp", scatter_dimension=dimension, tiled=True)


def dp_gather(block, axis):
    return lax.all_gather(block, "dp", axis=axis, tiled=True)


def swap_pairs(count, bit):
    return [(i, i ^ bit) for i in range(count)]


def butterfly_sum(flat):
    count = lax.axis_size("dp")
    bit = 1
    while bit < count:
        flat = flat + lax.ppermute(flat, "dp", swap_pairs(count, bit))
        bit *= 2
    return flat + lax.ppermute(flat, "tensor", [(0, 1), (1, 0)])


def tensor_swap(block):
    return lax.ppermute(block, "tensor", [(0, 1), (1, 0)])


def tensor_gather(block):
    other = tensor_swap(block)
    first = lax.axis_index("tensor") == 0
    return jnp.where(
        first, jnp.concatenate([block, other], axis=0), jnp.concatenate([other, block], axis=0)
    )


def tensor_scatter(partial):
    rank = lax.axis_index("tensor")
    half = partial.shape[0] // 2
    mine = lax.dynamic_slice_in_dim(partial, rank * half, half, 0)
    theirs = lax.dynamic_slice_in_dim(partial, (1 - rank) * half, half, 0)
    return mine + tensor_swap(theirs)


def chip_gather_rows(block):
    count = lax.axis_size("dp")
    parity = lax.axis_index("dp") % 2
    half = block.shape[0] // 2
    halves = block.reshape((2, half) + block.shape[1:])
    outgoing = jnp.tile(halves, (count // 2,) + (1,) * block.ndim)
    got = lax.all_to_all(outgoing, "dp", split_axis=0, concat_axis=0, tiled=True)
    theirs = lax.ppermute(got, "dp", swap_pairs(count, 1))
    pair = jnp.where(parity == 0, jnp.stack([got, theirs], axis=1), jnp.stack([theirs, got], axis=1))
    return pair.reshape((count * 2 * half,) + block.shape[1:])


def chip_scatter_rows(partial):
    count = lax.axis_size("dp")
    parity = lax.axis_index("dp") % 2
    half = partial.shape[0] // count // 2
    blocks = partial.reshape((count, 2, half) + partial.shape[1:])
    keep = lax.dynamic_index_in_dim(blocks, parity, axis=1, keepdims=False)
    send = lax.dynamic_index_in_dim(blocks, 1 - parity, axis=1, keepdims=False)
    chip_sum = keep + lax.ppermute(send, "dp", swap_pairs(count, 1))
    got = lax.all_to_all(chip_sum, "dp", split_axis=0, concat_axis=0, tiled=True)
    got = got.reshape((count // 2, 2) + got.shape[1:])
    even = jnp.sum(got[:, 0], axis=0)
    odd = jnp.sum(got[:, 1], axis=0)
    return jnp.concatenate([even, odd], axis=0)


def scatter_layer(parts):
    qkv_part, proj_part, up_part, down_part = parts
    return (
        chip_scatter_rows(qkv_part),
        chip_scatter_rows(proj_part).T,
        dp_scatter(up_part, 0),
        chip_scatter_rows(down_part).T,
    )


def vector_step(params, gradients):
    return params - vector_rate * gradients * lax.rsqrt(
        jnp.mean(gradients * gradients, axis=-1, keepdims=True) + vector_eps
    )


def local(
    block_input,
    cotangent,
    segments,
    qkv_weight,
    proj_weight,
    up_weight,
    down_weight,
    norm_gains,
    biases,
    qkv_bias,
    up_bias,
    qkv_state,
    proj_state,
    up_state,
    down_state,
):
    tensor_rank = lax.axis_index("tensor")
    local_width = qkv_weight.shape[3]
    local_hidden = up_weight.shape[2]
    head_count = local_width // HD
    model_width = block_input.shape[1]
    segment_row = segments[0]
    cosine_table, sine_table = rotary_tables(segment_row)
    stream = block_input.astype(jnp.float32)
    saved_layers = []
    for layer_id in range(LAYERS):
        layer_weights = (
            chip_gather_rows(qkv_weight[layer_id]),
            chip_gather_rows(proj_weight[layer_id].T),
            dp_gather(up_weight[layer_id], 0),
            chip_gather_rows(down_weight[layer_id].T),
        )
        qkv_full, proj_full, up_full, down_full = layer_weights
        normed, inverse = normalize(stream)
        attn_rows = (normed * norm_gains[layer_id, 0] + biases[layer_id, 0]).astype(jnp.bfloat16)
        mlp_rows = (normed * norm_gains[layer_id, 1] + biases[layer_id, 1]).astype(jnp.bfloat16)
        both_in = tensor_gather(jnp.concatenate([attn_rows, mlp_rows], axis=1))
        attn_in, mlp_in = both_in[:, :model_width], both_in[:, model_width:]
        length = attn_in.shape[0]
        qkv_local_bias = lax.dynamic_slice_in_dim(
            qkv_bias[layer_id], tensor_rank * local_width, local_width, 1
        )
        qkv_pre = (
            jnp.einsum("ld,dcf->lcf", attn_in, qkv_full, preferred_element_type=jnp.float32)
            + qkv_local_bias
        )
        shaped = qkv_pre.reshape(length, 3, head_count, HD)
        queries = rotate(shaped[:, 0], cosine_table, sine_table).astype(jnp.bfloat16)
        key_rows = rotate(shaped[:, 1], cosine_table, sine_table).astype(jnp.bfloat16)
        values = shaped[:, 2].astype(jnp.bfloat16)
        heads_out, log_sums = attend(queries, key_rows, values, segment_row)
        heads_flat = heads_out.reshape(length, local_width)
        up_local_bias = lax.dynamic_slice_in_dim(
            up_bias[layer_id], tensor_rank * local_hidden, local_hidden, 0
        )
        up_pre = jnp.dot(mlp_in, up_full, preferred_element_type=jnp.float32) + up_local_bias
        act_low = gelu_exact(up_pre).astype(jnp.bfloat16)
        partial_sum = jnp.einsum(
            "lf,df->ld", heads_flat, proj_full, preferred_element_type=jnp.float32
        ) + jnp.einsum("lf,df->ld", act_low, down_full, preferred_element_type=jnp.float32)
        branch = tensor_scatter(partial_sum)
        saved_layers.append(
            (
                normed,
                inverse,
                attn_in,
                mlp_in,
                queries,
                key_rows,
                values,
                log_sums,
                heads_flat,
                up_pre,
                act_low,
                layer_weights,
            )
        )
        stream = stream + branch + biases[layer_id, 2] + biases[layer_id, 3]
    grad_stream = cotangent.astype(jnp.float32)
    gains_list = [None] * LAYERS
    biases_list = [None] * LAYERS
    qkv_bias_list = [None] * LAYERS
    up_bias_list = [None] * LAYERS
    weight_list = [None] * LAYERS
    for layer_id in reversed(range(LAYERS)):
        (
            normed,
            inverse,
            attn_in,
            mlp_in,
            queries,
            key_rows,
            values,
            log_sums,
            heads_flat,
            up_pre,
            act_low,
            layer_weights,
        ) = saved_layers[layer_id]
        qkv_full, proj_full, up_full, down_full = layer_weights
        length = attn_in.shape[0]
        out_bias_grad = jnp.sum(grad_stream, axis=0)
        branch_grad = tensor_gather(grad_stream.astype(jnp.bfloat16))
        down_part = jnp.einsum(
            "lf,ld->df", act_low, branch_grad, preferred_element_type=jnp.float32
        )
        act_grad = jnp.einsum(
            "ld,df->lf", branch_grad, down_full, preferred_element_type=jnp.float32
        )
        gelu_back = jax.vjp(gelu_exact, up_pre)[1]
        up_pre_grad = gelu_back(act_grad)[0].astype(jnp.bfloat16)
        up_bias_part = jnp.sum(up_pre_grad, axis=0, dtype=jnp.float32)
        up_part = jnp.einsum("ld,lf->df", mlp_in, up_pre_grad, preferred_element_type=jnp.float32)
        mlp_in_grad = jnp.einsum(
            "lf,df->ld", up_pre_grad, up_full, preferred_element_type=jnp.float32
        )
        proj_part = jnp.einsum(
            "lf,ld->df", heads_flat, branch_grad, preferred_element_type=jnp.float32
        )
        heads_grad = (
            jnp.einsum("ld,df->lf", branch_grad, proj_full, preferred_element_type=jnp.float32)
            .astype(jnp.bfloat16)
            .reshape(length, head_count, HD)
        )
        query_grad, key_grad, value_grad = attend_back(
            queries, key_rows, values, heads_grad, log_sums, segment_row
        )
        qkv_pre_grad = jnp.stack(
            [
                unrotate(query_grad, cosine_table, sine_table),
                unrotate(key_grad, cosine_table, sine_table),
                value_grad,
            ],
            axis=1,
        )
        qkv_pre_grad = qkv_pre_grad.reshape(length, 3, local_width).astype(jnp.bfloat16)
        qkv_bias_part = jnp.sum(qkv_pre_grad, axis=0, dtype=jnp.float32)
        qkv_part = jnp.einsum(
            "ld,lcf->dcf", attn_in, qkv_pre_grad, preferred_element_type=jnp.float32
        )
        attn_in_grad = jnp.einsum(
            "lcf,dcf->ld", qkv_pre_grad, qkv_full, preferred_element_type=jnp.float32
        )
        both_grad = tensor_scatter(jnp.concatenate([attn_in_grad, mlp_in_grad], axis=1))
        attn_rows_grad, mlp_rows_grad = both_grad[:, :model_width], both_grad[:, model_width:]
        gains_list[layer_id] = jnp.stack(
            [jnp.sum(attn_rows_grad * normed, axis=0), jnp.sum(mlp_rows_grad * normed, axis=0)]
        )
        biases_list[layer_id] = jnp.stack(
            [
                jnp.sum(attn_rows_grad, axis=0),
                jnp.sum(mlp_rows_grad, axis=0),
                out_bias_grad,
                out_bias_grad,
            ]
        )
        qkv_bias_list[layer_id] = lax.dynamic_update_slice_in_dim(
            jnp.zeros((3, model_width), jnp.float32), qkv_bias_part, tensor_rank * local_width, 1
        )
        up_bias_list[layer_id] = lax.dynamic_update_slice_in_dim(
            jnp.zeros((up_bias.shape[1],), jnp.float32), up_bias_part, tensor_rank * local_hidden, 0
        )
        normed_grad = (
            attn_rows_grad * norm_gains[layer_id, 0] + mlp_rows_grad * norm_gains[layer_id, 1]
        )
        normed_mean = jnp.mean(normed_grad, axis=-1, keepdims=True)
        product_mean = jnp.mean(normed_grad * normed, axis=-1, keepdims=True)
        grad_stream = grad_stream + inverse * (normed_grad - normed_mean - normed * product_mean)
        weight_list[layer_id] = (qkv_part, proj_part, up_part, down_part)
        if layer_id > 0:
            weight_list[layer_id] = scatter_layer(weight_list[layer_id])
            first_sum, grad_stream = lax.optimization_barrier((weight_list[layer_id][0], grad_stream))
            weight_list[layer_id] = (first_sum,) + weight_list[layer_id][1:]
    small_parts = (
        jnp.stack(gains_list),
        jnp.stack(biases_list),
        jnp.stack(qkv_bias_list),
        jnp.stack(up_bias_list),
    )
    flat = butterfly_sum(jnp.concatenate([part.reshape(-1) for part in small_parts]))
    small_sums = []
    offset = 0
    for part in small_parts:
        small_sums.append(flat[offset : offset + part.size].reshape(part.shape))
        offset += part.size
    gains_grad, biases_grad, qkv_bias_grad, up_bias_grad = small_sums
    flat, first_parts = lax.optimization_barrier((flat, weight_list[0]))
    weight_list[0] = scatter_layer(first_parts)
    qkv_grad = jnp.stack([weight_list[layer_id][0] for layer_id in range(LAYERS)])
    proj_grad = jnp.stack([weight_list[layer_id][1] for layer_id in range(LAYERS)])
    up_grad = jnp.stack([weight_list[layer_id][2] for layer_id in range(LAYERS)])
    down_grad = jnp.stack([weight_list[layer_id][3] for layer_id in range(LAYERS)])
    qkv_state_new = momentum * qkv_state + qkv_grad
    proj_state_new = momentum * proj_state + proj_grad
    up_state_new = momentum * up_state + up_grad
    down_state_new = momentum * down_state + down_grad
    rows_local = qkv_state.shape[1]
    dp_count = lax.axis_size("dp")
    dp_rank = lax.axis_index("dp")
    slot_count = 4 * LAYERS
    sub = dp_count // slot_count
    piece_width = up_state.shape[2] // sub
    slot_mats = []
    for layer_id in range(LAYERS):
        slot_mats.append(qkv_state_new[layer_id].reshape(rows_local, 3 * local_width))
        slot_mats.append(proj_state_new[layer_id].T)
        slot_mats.append(up_state_new[layer_id])
        slot_mats.append(down_state_new[layer_id].T)
    pieces = []
    for mat in slot_mats:
        width = mat.shape[1] // sub
        split = mat.reshape(rows_local, sub, width).transpose(1, 0, 2)
        pieces.append(jnp.pad(split, ((0, 0), (0, 0), (0, piece_width - width))))
    outgoing = jnp.concatenate(pieces, axis=0)
    owned = lax.all_to_all(outgoing, "dp", split_axis=0, concat_axis=0, tiled=True)
    owned = owned.reshape(dp_count * rows_local, piece_width)
    owned, grad_stream = lax.optimization_barrier((owned, grad_stream))
    gram = jnp.dot(owned, owned.T, precision=ns_precision)
    bit = 1
    while bit < sub:
        gram = gram + lax.ppermute(gram, "dp", swap_pairs(dp_count, bit))
        bit *= 2
    core_half = dp_rank % 2
    half_rows = gram.shape[0] // 2
    mine = lax.dynamic_slice_in_dim(gram, core_half * half_rows, half_rows, 0)
    mine = mine + lax.ppermute(mine, "tensor", [(0, 1), (1, 0)])
    other = lax.ppermute(mine, "dp", swap_pairs(dp_count, 1))
    gram = jnp.where(
        core_half == 0,
        jnp.concatenate([mine, other], axis=0),
        jnp.concatenate([other, mine], axis=0),
    )
    norm_sq = jnp.trace(gram)
    scale = 1.0 / (jnp.sqrt(norm_sq) + frobenius_eps)
    current_gram = gram * (scale * scale)
    identity = jnp.eye(current_gram.shape[0], dtype=jnp.float32)
    accumulated = None
    for iteration in range(NS_ITERS):
        squared = jnp.dot(current_gram, current_gram, precision=ns_precision)
        polynomial = coef_first * identity + coef_second * current_gram + coef_third * squared
        if accumulated is None:
            accumulated = polynomial
        else:
            accumulated = jnp.dot(polynomial, accumulated, precision=ns_precision)
        if iteration + 1 < NS_ITERS:
            current_gram = jnp.dot(
                polynomial,
                jnp.dot(current_gram, polynomial, precision=ns_precision),
                precision=ns_precision,
            )
    current = jnp.dot(accumulated, owned * scale, precision=ns_precision)
    returned = lax.all_to_all(
        current.astype(jnp.bfloat16).reshape(dp_count, rows_local, piece_width),
        "dp",
        split_axis=0,
        concat_axis=0,
        tiled=True,
    ).reshape(slot_count, sub, rows_local, piece_width)
    my_rows = []
    for slot_id, mat in enumerate(slot_mats):
        width = mat.shape[1] // sub
        my_rows.append(
            returned[slot_id, :, :, :width]
            .astype(jnp.float32)
            .transpose(1, 0, 2)
            .reshape(rows_local, sub * width)
        )
    muon_step = muon_rate * match_rms
    qkv_list, proj_list, up_list, down_list = ([], [], [], [])
    for layer_id in range(LAYERS):
        base_slot = 4 * layer_id
        qkv_ortho = my_rows[base_slot].reshape(rows_local, 3, local_width)
        proj_ortho = my_rows[base_slot + 1].T
        up_ortho = my_rows[base_slot + 2]
        down_ortho = my_rows[base_slot + 3].T
        qkv_list.append(
            qkv_weight[layer_id].astype(jnp.float32) - muon_step * math.sqrt(3 * D) * qkv_ortho
        )
        proj_list.append(
            proj_weight[layer_id].astype(jnp.float32) - muon_step * math.sqrt(D) * proj_ortho
        )
        up_list.append(
            up_weight[layer_id].astype(jnp.float32) - muon_step * math.sqrt(FF) * up_ortho
        )
        down_list.append(
            down_weight[layer_id].astype(jnp.float32) - muon_step * math.sqrt(FF) * down_ortho
        )
    qkv_new = jnp.stack(qkv_list)
    proj_new = jnp.stack(proj_list)
    up_new = jnp.stack(up_list)
    down_new = jnp.stack(down_list)
    gains_new = vector_step(norm_gains, gains_grad)
    biases_new = vector_step(biases, biases_grad)
    qkv_bias_new = vector_step(qkv_bias, qkv_bias_grad)
    up_bias_new = vector_step(up_bias, up_bias_grad)
    return (
        stream,
        grad_stream,
        qkv_grad,
        proj_grad,
        up_grad,
        down_grad,
        gains_grad,
        biases_grad,
        qkv_bias_grad,
        up_bias_grad,
        qkv_new,
        proj_new,
        up_new,
        down_new,
        gains_new,
        biases_new,
        qkv_bias_new,
        up_bias_new,
        qkv_state_new,
        proj_state_new,
        up_state_new,
        down_state_new,
    )


def solution(mesh):
    return jax.shard_map(
        local,
        mesh=mesh,
        in_specs=(
            P(("dp", "tensor"), None),
            P(("dp", "tensor"), None),
            P("dp", None),
            P(None, "dp", None, "tensor"),
            P(None, "tensor", "dp"),
            P(None, "dp", "tensor"),
            P(None, "tensor", "dp"),
            P(),
            P(),
            P(),
            P(),
            P(None, "dp", None, "tensor"),
            P(None, "tensor", "dp"),
            P(None, "dp", "tensor"),
            P(None, "tensor", "dp"),
        ),
        out_specs=(
            P(("dp", "tensor"), None),
            P(("dp", "tensor"), None),
            P(None, "dp", None, "tensor"),
            P(None, "tensor", "dp"),
            P(None, "dp", "tensor"),
            P(None, "tensor", "dp"),
            P(),
            P(),
            P(),
            P(),
            P(None, "dp", None, "tensor"),
            P(None, "tensor", "dp"),
            P(None, "dp", "tensor"),
            P(None, "tensor", "dp"),
            P(),
            P(),
            P(),
            P(),
            P(None, "dp", None, "tensor"),
            P(None, "tensor", "dp"),
            P(None, "dp", "tensor"),
            P(None, "tensor", "dp"),
        ),
        check_vma=False,
    )
```

```python
import math

import jax
import jax.numpy as jnp
from jax import lax
from jax.sharding import PartitionSpec as P

D = 768
HD = 64
FF = 3072
ROT = 16
LAYERS = 2
NS_ITERS = 5


highest = lax.Precision.HIGHEST
ns_precision = lax.Precision.HIGH
norm_eps = 1e-05
masked_score = -1e30
coef_first = 3.4445
coef_second = -4.775
coef_third = 2.0315
momentum = 0.9
muon_rate = 0.2
match_rms = 0.2
vector_rate = 0.2
vector_eps = 1e-06
frobenius_eps = 1e-07


def rotary_tables(segment_row):
    length = segment_row.shape[0]
    indices = jnp.arange(length, dtype=jnp.int32)
    change = jnp.concatenate([jnp.ones((1,), dtype=bool), segment_row[1:] != segment_row[:-1]])
    starts = lax.cummax(jnp.where(change, indices, jnp.zeros_like(indices)), axis=0)
    positions = (indices - starts).astype(jnp.float32)
    half_rot = ROT // 2
    frequency = 10000.0 ** (-2.0 * jnp.arange(half_rot, dtype=jnp.float32) / ROT)
    angles = positions[:, None] * frequency[None, :]
    return (jnp.cos(angles), jnp.sin(angles))


def rotate(values, cosine_table, sine_table):
    half_rot = ROT // 2
    first_half = values[..., :half_rot]
    second_half = values[..., half_rot:ROT]
    cos_b = cosine_table[:, None, :]
    sin_b = sine_table[:, None, :]
    return jnp.concatenate(
        [
            first_half * cos_b - second_half * sin_b,
            second_half * cos_b + first_half * sin_b,
            values[..., ROT:],
        ],
        axis=-1,
    )


def unrotate(gradient, cosine_table, sine_table):
    half_rot = ROT // 2
    first_half = gradient[..., :half_rot]
    second_half = gradient[..., half_rot:ROT]
    cos_b = cosine_table[:, None, :]
    sin_b = sine_table[:, None, :]
    return jnp.concatenate(
        [
            first_half * cos_b + second_half * sin_b,
            second_half * cos_b - first_half * sin_b,
            gradient[..., ROT:],
        ],
        axis=-1,
    )


def normalize(stream):
    centered = stream - jnp.mean(stream, axis=-1, keepdims=True)
    inverse = lax.rsqrt(jnp.mean(centered * centered, axis=-1, keepdims=True) + norm_eps)
    return (centered * inverse, inverse)


def gelu_exact(values):
    return jax.nn.gelu(values, approximate=False)


def block_mask(segment_row, block_rows):
    query_pos = jnp.arange(block_rows, dtype=jnp.int32)
    key_pos = jnp.arange(segment_row.shape[0], dtype=jnp.int32)
    return (segment_row[:, None] == segment_row[None, :]) & (query_pos[:, None] >= key_pos[None, :])


def block_scores(queries, key_rows, allowed):
    scores = jnp.einsum(
        "qhe,khe->hqk", queries, key_rows, preferred_element_type=jnp.float32
    ) * queries.shape[-1] ** (-0.5)
    return jnp.where(allowed[None], scores, masked_score)


def attend(queries, key_rows, values, segment_row):
    length = queries.shape[0]
    block_rows = min(512, length)
    allowed = block_mask(segment_row, block_rows)
    scores = block_scores(queries, key_rows, allowed)
    row_peak = jnp.max(scores, axis=-1, keepdims=True)
    exponent = jnp.exp(scores - row_peak)
    row_total = jnp.sum(exponent, axis=-1, keepdims=True)
    probs_low = (exponent / row_total).astype(jnp.bfloat16)
    outputs = jnp.einsum(
        "hqk,khe->qhe", probs_low, values, preferred_element_type=jnp.float32
    ).astype(jnp.bfloat16)
    log_sums = row_peak + jnp.log(row_total)
    return (outputs, log_sums)


def attend_back(queries, key_rows, values, heads_grad, log_sums, segment_row):
    length = queries.shape[0]
    block_rows = min(512, length)
    scale_factor = queries.shape[-1] ** (-0.5)
    allowed = block_mask(segment_row, block_rows)
    scores = block_scores(queries, key_rows, allowed)
    probs_full = jnp.exp(scores - log_sums)
    probs_grad = jnp.einsum("qhe,khe->hqk", heads_grad, values, preferred_element_type=jnp.float32)
    row_dot = jnp.sum(probs_full * probs_grad, axis=-1, keepdims=True)
    score_grad = (probs_full * (probs_grad - row_dot)).astype(jnp.bfloat16)
    value_grad = jnp.einsum(
        "hqk,qhe->khe",
        probs_full.astype(jnp.bfloat16),
        heads_grad,
        preferred_element_type=jnp.float32,
    )
    query_grads = (
        jnp.einsum("hqk,khe->qhe", score_grad, key_rows, preferred_element_type=jnp.float32)
        * scale_factor
    )
    key_grad = (
        jnp.einsum("hqk,qhe->khe", score_grad, queries, preferred_element_type=jnp.float32)
        * scale_factor
    )
    return (query_grads, key_grad, value_grad)


def dp_scatter(partial, dimension):
    return lax.psum_scatter(partial, "dp", scatter_dimension=dimension, tiled=True)


def dp_gather(block, axis):
    return lax.all_gather(block, "dp", axis=axis, tiled=True)


def swap_pairs(count, bit):
    return [(i, i ^ bit) for i in range(count)]


def butterfly_sum(flat):
    count = lax.axis_size("dp")
    bit = 1
    while bit < count:
        flat = flat + lax.ppermute(flat, "dp", swap_pairs(count, bit))
        bit *= 2
    return flat + lax.ppermute(flat, "tensor", [(0, 1), (1, 0)])


def tensor_swap(block):
    return lax.ppermute(block, "tensor", [(0, 1), (1, 0)])


def tensor_gather(block):
    other = tensor_swap(block)
    first = lax.axis_index("tensor") == 0
    return jnp.where(
        first, jnp.concatenate([block, other], axis=0), jnp.concatenate([other, block], axis=0)
    )


def tensor_scatter(partial):
    rank = lax.axis_index("tensor")
    half = partial.shape[0] // 2
    mine = lax.dynamic_slice_in_dim(partial, rank * half, half, 0)
    theirs = lax.dynamic_slice_in_dim(partial, (1 - rank) * half, half, 0)
    return mine + tensor_swap(theirs)


def chip_gather_rows(block):
    count = lax.axis_size("dp")
    parity = lax.axis_index("dp") % 2
    half = block.shape[0] // 2
    halves = block.reshape((2, half) + block.shape[1:])
    outgoing = jnp.tile(halves, (count // 2,) + (1,) * block.ndim)
    got = lax.all_to_all(outgoing, "dp", split_axis=0, concat_axis=0, tiled=True)
    theirs = lax.ppermute(got, "dp", swap_pairs(count, 1))
    pair = jnp.where(parity == 0, jnp.stack([got, theirs], axis=1), jnp.stack([theirs, got], axis=1))
    return pair.reshape((count * 2 * half,) + block.shape[1:])


def chip_scatter_rows(partial):
    count = lax.axis_size("dp")
    parity = lax.axis_index("dp") % 2
    half = partial.shape[0] // count // 2
    blocks = partial.reshape((count, 2, half) + partial.shape[1:])
    keep = lax.dynamic_index_in_dim(blocks, parity, axis=1, keepdims=False)
    send = lax.dynamic_index_in_dim(blocks, 1 - parity, axis=1, keepdims=False)
    chip_sum = keep + lax.ppermute(send, "dp", swap_pairs(count, 1))
    got = lax.all_to_all(chip_sum, "dp", split_axis=0, concat_axis=0, tiled=True)
    got = got.reshape((count // 2, 2) + got.shape[1:])
    even = jnp.sum(got[:, 0], axis=0)
    odd = jnp.sum(got[:, 1], axis=0)
    return jnp.concatenate([even, odd], axis=0)


def scatter_layer(parts):
    qkv_part, proj_part, up_part, down_part = parts
    return (
        chip_scatter_rows(qkv_part),
        chip_scatter_rows(proj_part).T,
        dp_scatter(up_part, 0),
        chip_scatter_rows(down_part).T,
    )


def vector_step(params, gradients):
    return params - vector_rate * gradients * lax.rsqrt(
        jnp.mean(gradients * gradients, axis=-1, keepdims=True) + vector_eps
    )


def local(
    block_input,
    cotangent,
    segments,
    qkv_weight,
    proj_weight,
    up_weight,
    down_weight,
    norm_gains,
    biases,
    qkv_bias,
    up_bias,
    qkv_state,
    proj_state,
    up_state,
    down_state,
):
    tensor_rank = lax.axis_index("tensor")
    local_width = qkv_weight.shape[3]
    local_hidden = up_weight.shape[2]
    head_count = local_width // HD
    model_width = block_input.shape[1]
    segment_row = segments[0]
    cosine_table, sine_table = rotary_tables(segment_row)
    stream = block_input.astype(jnp.float32)
    saved_layers = []
    for layer_id in range(LAYERS):
        layer_weights = (
            chip_gather_rows(qkv_weight[layer_id]),
            dp_gather(proj_weight[layer_id].T, 0),
            dp_gather(up_weight[layer_id], 0),
            chip_gather_rows(down_weight[layer_id].T),
        )
        qkv_full, proj_full, up_full, down_full = layer_weights
        normed, inverse = normalize(stream)
        attn_rows = (normed * norm_gains[layer_id, 0] + biases[layer_id, 0]).astype(jnp.bfloat16)
        mlp_rows = (normed * norm_gains[layer_id, 1] + biases[layer_id, 1]).astype(jnp.bfloat16)
        both_in = tensor_gather(jnp.concatenate([attn_rows, mlp_rows], axis=1))
        attn_in, mlp_in = both_in[:, :model_width], both_in[:, model_width:]
        length = attn_in.shape[0]
        qkv_local_bias = lax.dynamic_slice_in_dim(
            qkv_bias[layer_id], tensor_rank * local_width, local_width, 1
        )
        qkv_pre = (
            jnp.einsum("ld,dcf->lcf", attn_in, qkv_full, preferred_element_type=jnp.float32)
            + qkv_local_bias
        )
        shaped = qkv_pre.reshape(length, 3, head_count, HD)
        queries = rotate(shaped[:, 0], cosine_table, sine_table).astype(jnp.bfloat16)
        key_rows = rotate(shaped[:, 1], cosine_table, sine_table).astype(jnp.bfloat16)
        values = shaped[:, 2].astype(jnp.bfloat16)
        heads_out, log_sums = attend(queries, key_rows, values, segment_row)
        heads_flat = heads_out.reshape(length, local_width)
        up_local_bias = lax.dynamic_slice_in_dim(
            up_bias[layer_id], tensor_rank * local_hidden, local_hidden, 0
        )
        up_pre = jnp.dot(mlp_in, up_full, preferred_element_type=jnp.float32) + up_local_bias
        act_low = gelu_exact(up_pre).astype(jnp.bfloat16)
        partial_sum = jnp.einsum(
            "lf,df->ld", heads_flat, proj_full, preferred_element_type=jnp.float32
        ) + jnp.einsum("lf,df->ld", act_low, down_full, preferred_element_type=jnp.float32)
        branch = tensor_scatter(partial_sum)
        saved_layers.append(
            (
                normed,
                inverse,
                attn_in,
                mlp_in,
                queries,
                key_rows,
                values,
                log_sums,
                heads_flat,
                up_pre,
                act_low,
                layer_weights,
            )
        )
        stream = stream + branch + biases[layer_id, 2] + biases[layer_id, 3]
    grad_stream = cotangent.astype(jnp.float32)
    gains_list = [None] * LAYERS
    biases_list = [None] * LAYERS
    qkv_bias_list = [None] * LAYERS
    up_bias_list = [None] * LAYERS
    weight_list = [None] * LAYERS
    for layer_id in reversed(range(LAYERS)):
        (
            normed,
            inverse,
            attn_in,
            mlp_in,
            queries,
            key_rows,
            values,
            log_sums,
            heads_flat,
            up_pre,
            act_low,
            layer_weights,
        ) = saved_layers[layer_id]
        qkv_full, proj_full, up_full, down_full = layer_weights
        length = attn_in.shape[0]
        out_bias_grad = jnp.sum(grad_stream, axis=0)
        branch_grad = tensor_gather(grad_stream.astype(jnp.bfloat16))
        down_part = jnp.einsum(
            "lf,ld->df", act_low, branch_grad, preferred_element_type=jnp.float32
        )
        act_grad = jnp.einsum(
            "ld,df->lf", branch_grad, down_full, preferred_element_type=jnp.float32
        )
        gelu_back = jax.vjp(gelu_exact, up_pre)[1]
        up_pre_grad = gelu_back(act_grad)[0].astype(jnp.bfloat16)
        up_bias_part = jnp.sum(up_pre_grad, axis=0, dtype=jnp.float32)
        up_part = jnp.einsum("ld,lf->df", mlp_in, up_pre_grad, preferred_element_type=jnp.float32)
        mlp_in_grad = jnp.einsum(
            "lf,df->ld", up_pre_grad, up_full, preferred_element_type=jnp.float32
        )
        proj_part = jnp.einsum(
            "lf,ld->df", heads_flat, branch_grad, preferred_element_type=jnp.float32
        )
        heads_grad = (
            jnp.einsum("ld,df->lf", branch_grad, proj_full, preferred_element_type=jnp.float32)
            .astype(jnp.bfloat16)
            .reshape(length, head_count, HD)
        )
        query_grad, key_grad, value_grad = attend_back(
            queries, key_rows, values, heads_grad, log_sums, segment_row
        )
        qkv_pre_grad = jnp.stack(
            [
                unrotate(query_grad, cosine_table, sine_table),
                unrotate(key_grad, cosine_table, sine_table),
                value_grad,
            ],
            axis=1,
        )
        qkv_pre_grad = qkv_pre_grad.reshape(length, 3, local_width).astype(jnp.bfloat16)
        qkv_bias_part = jnp.sum(qkv_pre_grad, axis=0, dtype=jnp.float32)
        qkv_part = jnp.einsum(
            "ld,lcf->dcf", attn_in, qkv_pre_grad, preferred_element_type=jnp.float32
        )
        attn_in_grad = jnp.einsum(
            "lcf,dcf->ld", qkv_pre_grad, qkv_full, preferred_element_type=jnp.float32
        )
        both_grad = tensor_scatter(jnp.concatenate([attn_in_grad, mlp_in_grad], axis=1))
        attn_rows_grad, mlp_rows_grad = both_grad[:, :model_width], both_grad[:, model_width:]
        gains_list[layer_id] = jnp.stack(
            [jnp.sum(attn_rows_grad * normed, axis=0), jnp.sum(mlp_rows_grad * normed, axis=0)]
        )
        biases_list[layer_id] = jnp.stack(
            [
                jnp.sum(attn_rows_grad, axis=0),
                jnp.sum(mlp_rows_grad, axis=0),
                out_bias_grad,
                out_bias_grad,
            ]
        )
        qkv_bias_list[layer_id] = lax.dynamic_update_slice_in_dim(
            jnp.zeros((3, model_width), jnp.float32), qkv_bias_part, tensor_rank * local_width, 1
        )
        up_bias_list[layer_id] = lax.dynamic_update_slice_in_dim(
            jnp.zeros((up_bias.shape[1],), jnp.float32), up_bias_part, tensor_rank * local_hidden, 0
        )
        normed_grad = (
            attn_rows_grad * norm_gains[layer_id, 0] + mlp_rows_grad * norm_gains[layer_id, 1]
        )
        normed_mean = jnp.mean(normed_grad, axis=-1, keepdims=True)
        product_mean = jnp.mean(normed_grad * normed, axis=-1, keepdims=True)
        grad_stream = grad_stream + inverse * (normed_grad - normed_mean - normed * product_mean)
        weight_list[layer_id] = (qkv_part, proj_part, up_part, down_part)
        if layer_id > 0:
            weight_list[layer_id] = scatter_layer(weight_list[layer_id])
            first_sum, grad_stream = lax.optimization_barrier((weight_list[layer_id][0], grad_stream))
            weight_list[layer_id] = (first_sum,) + weight_list[layer_id][1:]
    small_parts = (
        jnp.stack(gains_list),
        jnp.stack(biases_list),
        jnp.stack(qkv_bias_list),
        jnp.stack(up_bias_list),
    )
    flat = butterfly_sum(jnp.concatenate([part.reshape(-1) for part in small_parts]))
    small_sums = []
    offset = 0
    for part in small_parts:
        small_sums.append(flat[offset : offset + part.size].reshape(part.shape))
        offset += part.size
    gains_grad, biases_grad, qkv_bias_grad, up_bias_grad = small_sums
    flat, first_parts = lax.optimization_barrier((flat, weight_list[0]))
    weight_list[0] = scatter_layer(first_parts)
    qkv_grad = jnp.stack([weight_list[layer_id][0] for layer_id in range(LAYERS)])
    proj_grad = jnp.stack([weight_list[layer_id][1] for layer_id in range(LAYERS)])
    up_grad = jnp.stack([weight_list[layer_id][2] for layer_id in range(LAYERS)])
    down_grad = jnp.stack([weight_list[layer_id][3] for layer_id in range(LAYERS)])
    qkv_state_new = momentum * qkv_state + qkv_grad
    proj_state_new = momentum * proj_state + proj_grad
    up_state_new = momentum * up_state + up_grad
    down_state_new = momentum * down_state + down_grad
    rows_local = qkv_state.shape[1]
    dp_count = lax.axis_size("dp")
    dp_rank = lax.axis_index("dp")
    slot_count = 4 * LAYERS
    sub = dp_count // slot_count
    piece_width = up_state.shape[2] // sub
    slot_mats = []
    for layer_id in range(LAYERS):
        slot_mats.append(qkv_state_new[layer_id].reshape(rows_local, 3 * local_width))
        slot_mats.append(proj_state_new[layer_id].T)
        slot_mats.append(up_state_new[layer_id])
        slot_mats.append(down_state_new[layer_id].T)
    pieces = []
    for mat in slot_mats:
        width = mat.shape[1] // sub
        split = mat.reshape(rows_local, sub, width).transpose(1, 0, 2)
        pieces.append(jnp.pad(split, ((0, 0), (0, 0), (0, piece_width - width))))
    outgoing = jnp.concatenate(pieces, axis=0)
    owned = lax.all_to_all(outgoing, "dp", split_axis=0, concat_axis=0, tiled=True)
    owned = owned.reshape(dp_count * rows_local, piece_width)
    owned, grad_stream = lax.optimization_barrier((owned, grad_stream))
    gram = jnp.dot(owned, owned.T, precision=ns_precision)
    bit = 1
    while bit < sub:
        gram = gram + lax.ppermute(gram, "dp", swap_pairs(dp_count, bit))
        bit *= 2
    core_half = dp_rank % 2
    half_rows = gram.shape[0] // 2
    mine = lax.dynamic_slice_in_dim(gram, core_half * half_rows, half_rows, 0)
    mine = mine + lax.ppermute(mine, "tensor", [(0, 1), (1, 0)])
    other = lax.ppermute(mine, "dp", swap_pairs(dp_count, 1))
    gram = jnp.where(
        core_half == 0,
        jnp.concatenate([mine, other], axis=0),
        jnp.concatenate([other, mine], axis=0),
    )
    norm_sq = jnp.trace(gram)
    scale = 1.0 / (jnp.sqrt(norm_sq) + frobenius_eps)
    current_gram = gram * (scale * scale)
    identity = jnp.eye(current_gram.shape[0], dtype=jnp.float32)
    accumulated = None
    for iteration in range(NS_ITERS):
        squared = jnp.dot(current_gram, current_gram, precision=ns_precision)
        polynomial = coef_first * identity + coef_second * current_gram + coef_third * squared
        if accumulated is None:
            accumulated = polynomial
        else:
            accumulated = jnp.dot(polynomial, accumulated, precision=ns_precision)
        if iteration + 1 < NS_ITERS:
            current_gram = jnp.dot(
                polynomial,
                jnp.dot(current_gram, polynomial, precision=ns_precision),
                precision=ns_precision,
            )
    current = jnp.dot(accumulated, owned * scale, precision=ns_precision)
    returned = lax.all_to_all(
        current.astype(jnp.bfloat16).reshape(dp_count, rows_local, piece_width),
        "dp",
        split_axis=0,
        concat_axis=0,
        tiled=True,
    ).reshape(slot_count, sub, rows_local, piece_width)
    my_rows = []
    for slot_id, mat in enumerate(slot_mats):
        width = mat.shape[1] // sub
        my_rows.append(
            returned[slot_id, :, :, :width]
            .astype(jnp.float32)
            .transpose(1, 0, 2)
            .reshape(rows_local, sub * width)
        )
    muon_step = muon_rate * match_rms
    qkv_list, proj_list, up_list, down_list = ([], [], [], [])
    for layer_id in range(LAYERS):
        base_slot = 4 * layer_id
        qkv_ortho = my_rows[base_slot].reshape(rows_local, 3, local_width)
        proj_ortho = my_rows[base_slot + 1].T
        up_ortho = my_rows[base_slot + 2]
        down_ortho = my_rows[base_slot + 3].T
        qkv_list.append(
            qkv_weight[layer_id].astype(jnp.float32) - muon_step * math.sqrt(3 * D) * qkv_ortho
        )
        proj_list.append(
            proj_weight[layer_id].astype(jnp.float32) - muon_step * math.sqrt(D) * proj_ortho
        )
        up_list.append(
            up_weight[layer_id].astype(jnp.float32) - muon_step * math.sqrt(FF) * up_ortho
        )
        down_list.append(
            down_weight[layer_id].astype(jnp.float32) - muon_step * math.sqrt(FF) * down_ortho
        )
    qkv_new = jnp.stack(qkv_list)
    proj_new = jnp.stack(proj_list)
    up_new = jnp.stack(up_list)
    down_new = jnp.stack(down_list)
    gains_new = vector_step(norm_gains, gains_grad)
    biases_new = vector_step(biases, biases_grad)
    qkv_bias_new = vector_step(qkv_bias, qkv_bias_grad)
    up_bias_new = vector_step(up_bias, up_bias_grad)
    return (
        stream,
        grad_stream,
        qkv_grad,
        proj_grad,
        up_grad,
        down_grad,
        gains_grad,
        biases_grad,
        qkv_bias_grad,
        up_bias_grad,
        qkv_new,
        proj_new,
        up_new,
        down_new,
        gains_new,
        biases_new,
        qkv_bias_new,
        up_bias_new,
        qkv_state_new,
        proj_state_new,
        up_state_new,
        down_state_new,
    )


def solution(mesh):
    return jax.shard_map(
        local,
        mesh=mesh,
        in_specs=(
            P(("dp", "tensor"), None),
            P(("dp", "tensor"), None),
            P("dp", None),
            P(None, "dp", None, "tensor"),
            P(None, "tensor", "dp"),
            P(None, "dp", "tensor"),
            P(None, "tensor", "dp"),
            P(),
            P(),
            P(),
            P(),
            P(None, "dp", None, "tensor"),
            P(None, "tensor", "dp"),
            P(None, "dp", "tensor"),
            P(None, "tensor", "dp"),
        ),
        out_specs=(
            P(("dp", "tensor"), None),
            P(("dp", "tensor"), None),
            P(None, "dp", None, "tensor"),
            P(None, "tensor", "dp"),
            P(None, "dp", "tensor"),
            P(None, "tensor", "dp"),
            P(),
            P(),
            P(),
            P(),
            P(None, "dp", None, "tensor"),
            P(None, "tensor", "dp"),
            P(None, "dp", "tensor"),
            P(None, "tensor", "dp"),
            P(),
            P(),
            P(),
            P(),
            P(None, "dp", None, "tensor"),
            P(None, "tensor", "dp"),
            P(None, "dp", "tensor"),
            P(None, "tensor", "dp"),
        ),
        check_vma=False,
    )
```

```python
import math

import jax
import jax.numpy as jnp
from jax import lax
from jax.sharding import PartitionSpec as P

D = 768
HD = 64
FF = 3072
ROT = 16
LAYERS = 2
NS_ITERS = 5


highest = lax.Precision.HIGHEST
ns_precision = lax.Precision.HIGH
norm_eps = 1e-05
masked_score = -1e30
coef_first = 3.4445
coef_second = -4.775
coef_third = 2.0315
momentum = 0.9
muon_rate = 0.2
match_rms = 0.2
vector_rate = 0.2
vector_eps = 1e-06
frobenius_eps = 1e-07


def rotary_tables(segment_row):
    length = segment_row.shape[0]
    indices = jnp.arange(length, dtype=jnp.int32)
    change = jnp.concatenate([jnp.ones((1,), dtype=bool), segment_row[1:] != segment_row[:-1]])
    starts = lax.cummax(jnp.where(change, indices, jnp.zeros_like(indices)), axis=0)
    positions = (indices - starts).astype(jnp.float32)
    half_rot = ROT // 2
    frequency = 10000.0 ** (-2.0 * jnp.arange(half_rot, dtype=jnp.float32) / ROT)
    angles = positions[:, None] * frequency[None, :]
    return (jnp.cos(angles), jnp.sin(angles))


def rotate(values, cosine_table, sine_table):
    half_rot = ROT // 2
    first_half = values[..., :half_rot]
    second_half = values[..., half_rot:ROT]
    cos_b = cosine_table[:, None, :]
    sin_b = sine_table[:, None, :]
    return jnp.concatenate(
        [
            first_half * cos_b - second_half * sin_b,
            second_half * cos_b + first_half * sin_b,
            values[..., ROT:],
        ],
        axis=-1,
    )


def unrotate(gradient, cosine_table, sine_table):
    half_rot = ROT // 2
    first_half = gradient[..., :half_rot]
    second_half = gradient[..., half_rot:ROT]
    cos_b = cosine_table[:, None, :]
    sin_b = sine_table[:, None, :]
    return jnp.concatenate(
        [
            first_half * cos_b + second_half * sin_b,
            second_half * cos_b - first_half * sin_b,
            gradient[..., ROT:],
        ],
        axis=-1,
    )


def normalize(stream):
    centered = stream - jnp.mean(stream, axis=-1, keepdims=True)
    inverse = lax.rsqrt(jnp.mean(centered * centered, axis=-1, keepdims=True) + norm_eps)
    return (centered * inverse, inverse)


def gelu_exact(values):
    return jax.nn.gelu(values, approximate=False)


def block_mask(segment_row, block_rows):
    query_pos = jnp.arange(block_rows, dtype=jnp.int32)
    key_pos = jnp.arange(segment_row.shape[0], dtype=jnp.int32)
    return (segment_row[:, None] == segment_row[None, :]) & (query_pos[:, None] >= key_pos[None, :])


def block_scores(queries, key_rows, allowed):
    scores = jnp.einsum(
        "qhe,khe->hqk", queries, key_rows, preferred_element_type=jnp.float32
    ) * queries.shape[-1] ** (-0.5)
    return jnp.where(allowed[None], scores, masked_score)


def attend(queries, key_rows, values, segment_row):
    length = queries.shape[0]
    block_rows = min(512, length)
    allowed = block_mask(segment_row, block_rows)
    scores = block_scores(queries, key_rows, allowed)
    row_peak = jnp.max(scores, axis=-1, keepdims=True)
    exponent = jnp.exp(scores - row_peak)
    row_total = jnp.sum(exponent, axis=-1, keepdims=True)
    probs_low = (exponent / row_total).astype(jnp.bfloat16)
    outputs = jnp.einsum(
        "hqk,khe->qhe", probs_low, values, preferred_element_type=jnp.float32
    ).astype(jnp.bfloat16)
    log_sums = row_peak + jnp.log(row_total)
    return (outputs, log_sums)


def attend_back(queries, key_rows, values, heads_grad, log_sums, segment_row):
    length = queries.shape[0]
    block_rows = min(512, length)
    scale_factor = queries.shape[-1] ** (-0.5)
    allowed = block_mask(segment_row, block_rows)
    scores = block_scores(queries, key_rows, allowed)
    probs_full = jnp.exp(scores - log_sums)
    probs_grad = jnp.einsum("qhe,khe->hqk", heads_grad, values, preferred_element_type=jnp.float32)
    row_dot = jnp.sum(probs_full * probs_grad, axis=-1, keepdims=True)
    score_grad = (probs_full * (probs_grad - row_dot)).astype(jnp.bfloat16)
    value_grad = jnp.einsum(
        "hqk,qhe->khe",
        probs_full.astype(jnp.bfloat16),
        heads_grad,
        preferred_element_type=jnp.float32,
    )
    query_grads = (
        jnp.einsum("hqk,khe->qhe", score_grad, key_rows, preferred_element_type=jnp.float32)
        * scale_factor
    )
    key_grad = (
        jnp.einsum("hqk,qhe->khe", score_grad, queries, preferred_element_type=jnp.float32)
        * scale_factor
    )
    return (query_grads, key_grad, value_grad)


def dp_scatter(partial, dimension):
    return lax.psum_scatter(partial, "dp", scatter_dimension=dimension, tiled=True)


def dp_gather(block, axis):
    return lax.all_gather(block, "dp", axis=axis, tiled=True)


def swap_pairs(count, bit):
    return [(i, i ^ bit) for i in range(count)]


def butterfly_sum(flat):
    count = lax.axis_size("dp")
    bit = 1
    while bit < count:
        flat = flat + lax.ppermute(flat, "dp", swap_pairs(count, bit))
        bit *= 2
    return flat + lax.ppermute(flat, "tensor", [(0, 1), (1, 0)])


def tensor_swap(block):
    return lax.ppermute(block, "tensor", [(0, 1), (1, 0)])


def tensor_gather(block):
    other = tensor_swap(block)
    first = lax.axis_index("tensor") == 0
    return jnp.where(
        first, jnp.concatenate([block, other], axis=0), jnp.concatenate([other, block], axis=0)
    )


def tensor_scatter(partial):
    rank = lax.axis_index("tensor")
    half = partial.shape[0] // 2
    mine = lax.dynamic_slice_in_dim(partial, rank * half, half, 0)
    theirs = lax.dynamic_slice_in_dim(partial, (1 - rank) * half, half, 0)
    return mine + tensor_swap(theirs)


def chip_gather_rows(block):
    count = lax.axis_size("dp")
    parity = lax.axis_index("dp") % 2
    half = block.shape[0] // 2
    halves = block.reshape((2, half) + block.shape[1:])
    outgoing = jnp.tile(halves, (count // 2,) + (1,) * block.ndim)
    got = lax.all_to_all(outgoing, "dp", split_axis=0, concat_axis=0, tiled=True)
    theirs = lax.ppermute(got, "dp", swap_pairs(count, 1))
    pair = jnp.where(parity == 0, jnp.stack([got, theirs], axis=1), jnp.stack([theirs, got], axis=1))
    return pair.reshape((count * 2 * half,) + block.shape[1:])


def chip_scatter_rows(partial):
    count = lax.axis_size("dp")
    parity = lax.axis_index("dp") % 2
    half = partial.shape[0] // count // 2
    blocks = partial.reshape((count, 2, half) + partial.shape[1:])
    keep = lax.dynamic_index_in_dim(blocks, parity, axis=1, keepdims=False)
    send = lax.dynamic_index_in_dim(blocks, 1 - parity, axis=1, keepdims=False)
    chip_sum = keep + lax.ppermute(send, "dp", swap_pairs(count, 1))
    got = lax.all_to_all(chip_sum, "dp", split_axis=0, concat_axis=0, tiled=True)
    got = got.reshape((count // 2, 2) + got.shape[1:])
    even = jnp.sum(got[:, 0], axis=0)
    odd = jnp.sum(got[:, 1], axis=0)
    return jnp.concatenate([even, odd], axis=0)


def scatter_layer(parts):
    qkv_part, proj_part, up_part, down_part = parts
    return (
        chip_scatter_rows(qkv_part),
        chip_scatter_rows(proj_part).T,
        dp_scatter(up_part, 0),
        chip_scatter_rows(down_part).T,
    )


def vector_step(params, gradients):
    return params - vector_rate * gradients * lax.rsqrt(
        jnp.mean(gradients * gradients, axis=-1, keepdims=True) + vector_eps
    )


def local(
    block_input,
    cotangent,
    segments,
    qkv_weight,
    proj_weight,
    up_weight,
    down_weight,
    norm_gains,
    biases,
    qkv_bias,
    up_bias,
    qkv_state,
    proj_state,
    up_state,
    down_state,
):
    tensor_rank = lax.axis_index("tensor")
    local_width = qkv_weight.shape[3]
    local_hidden = up_weight.shape[2]
    head_count = local_width // HD
    model_width = block_input.shape[1]
    segment_row = segments[0]
    cosine_table, sine_table = rotary_tables(segment_row)
    stream = block_input.astype(jnp.float32)
    saved_layers = []
    for layer_id in range(LAYERS):
        layer_weights = (
            chip_gather_rows(qkv_weight[layer_id]),
            chip_gather_rows(proj_weight[layer_id].T),
            dp_gather(up_weight[layer_id], 0),
            chip_gather_rows(down_weight[layer_id].T),
        )
        qkv_full, proj_full, up_full, down_full = layer_weights
        normed, inverse = normalize(stream)
        attn_rows = (normed * norm_gains[layer_id, 0] + biases[layer_id, 0]).astype(jnp.bfloat16)
        mlp_rows = (normed * norm_gains[layer_id, 1] + biases[layer_id, 1]).astype(jnp.bfloat16)
        both_in = tensor_gather(jnp.concatenate([attn_rows, mlp_rows], axis=1))
        attn_in, mlp_in = both_in[:, :model_width], both_in[:, model_width:]
        length = attn_in.shape[0]
        qkv_local_bias = lax.dynamic_slice_in_dim(
            qkv_bias[layer_id], tensor_rank * local_width, local_width, 1
        )
        qkv_pre = (
            jnp.einsum("ld,dcf->lcf", attn_in, qkv_full, preferred_element_type=jnp.float32)
            + qkv_local_bias
        )
        shaped = qkv_pre.reshape(length, 3, head_count, HD)
        queries = rotate(shaped[:, 0], cosine_table, sine_table).astype(jnp.bfloat16)
        key_rows = rotate(shaped[:, 1], cosine_table, sine_table).astype(jnp.bfloat16)
        values = shaped[:, 2].astype(jnp.bfloat16)
        heads_out, log_sums = attend(queries, key_rows, values, segment_row)
        heads_flat = heads_out.reshape(length, local_width)
        up_local_bias = lax.dynamic_slice_in_dim(
            up_bias[layer_id], tensor_rank * local_hidden, local_hidden, 0
        )
        up_pre = jnp.dot(mlp_in, up_full, preferred_element_type=jnp.float32) + up_local_bias
        act_low = gelu_exact(up_pre).astype(jnp.bfloat16)
        partial_sum = jnp.einsum(
            "lf,df->ld", heads_flat, proj_full, preferred_element_type=jnp.float32
        ) + jnp.einsum("lf,df->ld", act_low, down_full, preferred_element_type=jnp.float32)
        branch = tensor_scatter(partial_sum)
        saved_layers.append(
            (
                normed,
                inverse,
                attn_in,
                mlp_in,
                queries,
                key_rows,
                values,
                log_sums,
                heads_flat,
                up_pre,
                act_low,
                layer_weights,
            )
        )
        stream = stream + branch + biases[layer_id, 2] + biases[layer_id, 3]
    grad_stream = cotangent.astype(jnp.float32)
    gains_list = [None] * LAYERS
    biases_list = [None] * LAYERS
    qkv_bias_list = [None] * LAYERS
    up_bias_list = [None] * LAYERS
    weight_list = [None] * LAYERS
    for layer_id in reversed(range(LAYERS)):
        (
            normed,
            inverse,
            attn_in,
            mlp_in,
            queries,
            key_rows,
            values,
            log_sums,
            heads_flat,
            up_pre,
            act_low,
            layer_weights,
        ) = saved_layers[layer_id]
        qkv_full, proj_full, up_full, down_full = layer_weights
        length = attn_in.shape[0]
        out_bias_grad = jnp.sum(grad_stream, axis=0)
        branch_grad = tensor_gather(grad_stream.astype(jnp.bfloat16))
        down_part = jnp.einsum(
            "lf,ld->df", act_low, branch_grad, preferred_element_type=jnp.float32
        )
        act_grad = jnp.einsum(
            "ld,df->lf", branch_grad, down_full, preferred_element_type=jnp.float32
        )
        gelu_back = jax.vjp(gelu_exact, up_pre)[1]
        up_pre_grad = gelu_back(act_grad)[0].astype(jnp.bfloat16)
        up_bias_part = jnp.sum(up_pre_grad, axis=0, dtype=jnp.float32)
        up_part = jnp.einsum("ld,lf->df", mlp_in, up_pre_grad, preferred_element_type=jnp.float32)
        mlp_in_grad = jnp.einsum(
            "lf,df->ld", up_pre_grad, up_full, preferred_element_type=jnp.float32
        )
        proj_part = jnp.einsum(
            "lf,ld->df", heads_flat, branch_grad, preferred_element_type=jnp.float32
        )
        heads_grad = (
            jnp.einsum("ld,df->lf", branch_grad, proj_full, preferred_element_type=jnp.float32)
            .astype(jnp.bfloat16)
            .reshape(length, head_count, HD)
        )
        query_grad, key_grad, value_grad = attend_back(
            queries, key_rows, values, heads_grad, log_sums, segment_row
        )
        qkv_pre_grad = jnp.stack(
            [
                unrotate(query_grad, cosine_table, sine_table),
                unrotate(key_grad, cosine_table, sine_table),
                value_grad,
            ],
            axis=1,
        )
        qkv_pre_grad = qkv_pre_grad.reshape(length, 3, local_width).astype(jnp.bfloat16)
        qkv_bias_part = jnp.sum(qkv_pre_grad, axis=0, dtype=jnp.float32)
        qkv_part = jnp.einsum(
            "ld,lcf->dcf", attn_in, qkv_pre_grad, preferred_element_type=jnp.float32
        )
        attn_in_grad = jnp.einsum(
            "lcf,dcf->ld", qkv_pre_grad, qkv_full, preferred_element_type=jnp.float32
        )
        both_grad = tensor_scatter(jnp.concatenate([attn_in_grad, mlp_in_grad], axis=1))
        attn_rows_grad, mlp_rows_grad = both_grad[:, :model_width], both_grad[:, model_width:]
        gains_list[layer_id] = jnp.stack(
            [jnp.sum(attn_rows_grad * normed, axis=0), jnp.sum(mlp_rows_grad * normed, axis=0)]
        )
        biases_list[layer_id] = jnp.stack(
            [
                jnp.sum(attn_rows_grad, axis=0),
                jnp.sum(mlp_rows_grad, axis=0),
                out_bias_grad,
                out_bias_grad,
            ]
        )
        qkv_bias_list[layer_id] = lax.dynamic_update_slice_in_dim(
            jnp.zeros((3, model_width), jnp.float32), qkv_bias_part, tensor_rank * local_width, 1
        )
        up_bias_list[layer_id] = lax.dynamic_update_slice_in_dim(
            jnp.zeros((up_bias.shape[1],), jnp.float32), up_bias_part, tensor_rank * local_hidden, 0
        )
        normed_grad = (
            attn_rows_grad * norm_gains[layer_id, 0] + mlp_rows_grad * norm_gains[layer_id, 1]
        )
        normed_mean = jnp.mean(normed_grad, axis=-1, keepdims=True)
        product_mean = jnp.mean(normed_grad * normed, axis=-1, keepdims=True)
        grad_stream = grad_stream + inverse * (normed_grad - normed_mean - normed * product_mean)
        weight_list[layer_id] = (qkv_part, proj_part, up_part, down_part)
        if layer_id > 0:
            weight_list[layer_id] = scatter_layer(weight_list[layer_id])
            first_sum, grad_stream = lax.optimization_barrier((weight_list[layer_id][0], grad_stream))
            weight_list[layer_id] = (first_sum,) + weight_list[layer_id][1:]
    small_parts = (
        jnp.stack(gains_list),
        jnp.stack(biases_list),
        jnp.stack(qkv_bias_list),
        jnp.stack(up_bias_list),
    )
    flat = butterfly_sum(jnp.concatenate([part.reshape(-1) for part in small_parts]))
    small_sums = []
    offset = 0
    for part in small_parts:
        small_sums.append(flat[offset : offset + part.size].reshape(part.shape))
        offset += part.size
    gains_grad, biases_grad, qkv_bias_grad, up_bias_grad = small_sums
    flat, first_down = lax.optimization_barrier((flat, weight_list[0][3]))
    weight_list[0] = scatter_layer(weight_list[0][:3] + (first_down,))
    qkv_grad = jnp.stack([weight_list[layer_id][0] for layer_id in range(LAYERS)])
    proj_grad = jnp.stack([weight_list[layer_id][1] for layer_id in range(LAYERS)])
    up_grad = jnp.stack([weight_list[layer_id][2] for layer_id in range(LAYERS)])
    down_grad = jnp.stack([weight_list[layer_id][3] for layer_id in range(LAYERS)])
    qkv_state_new = momentum * qkv_state + qkv_grad
    proj_state_new = momentum * proj_state + proj_grad
    up_state_new = momentum * up_state + up_grad
    down_state_new = momentum * down_state + down_grad
    rows_local = qkv_state.shape[1]
    dp_count = lax.axis_size("dp")
    dp_rank = lax.axis_index("dp")
    slot_count = 4 * LAYERS
    sub = dp_count // slot_count
    piece_width = up_state.shape[2] // sub
    slot_mats = []
    for layer_id in range(LAYERS):
        slot_mats.append(qkv_state_new[layer_id].reshape(rows_local, 3 * local_width))
        slot_mats.append(proj_state_new[layer_id].T)
        slot_mats.append(up_state_new[layer_id])
        slot_mats.append(down_state_new[layer_id].T)
    pieces = []
    for mat in slot_mats:
        width = mat.shape[1] // sub
        split = mat.reshape(rows_local, sub, width).transpose(1, 0, 2)
        pieces.append(jnp.pad(split, ((0, 0), (0, 0), (0, piece_width - width))))
    outgoing = jnp.concatenate(pieces, axis=0)
    owned = lax.all_to_all(outgoing, "dp", split_axis=0, concat_axis=0, tiled=True)
    owned = owned.reshape(dp_count * rows_local, piece_width)
    owned, grad_stream = lax.optimization_barrier((owned, grad_stream))
    gram = jnp.dot(owned, owned.T, precision=ns_precision)
    bit = 1
    while bit < sub:
        gram = gram + lax.ppermute(gram, "dp", swap_pairs(dp_count, bit))
        bit *= 2
    core_half = dp_rank % 2
    half_rows = gram.shape[0] // 2
    mine = lax.dynamic_slice_in_dim(gram, core_half * half_rows, half_rows, 0)
    mine = mine + lax.ppermute(mine, "tensor", [(0, 1), (1, 0)])
    other = lax.ppermute(mine, "dp", swap_pairs(dp_count, 1))
    gram = jnp.where(
        core_half == 0,
        jnp.concatenate([mine, other], axis=0),
        jnp.concatenate([other, mine], axis=0),
    )
    norm_sq = jnp.trace(gram)
    scale = 1.0 / (jnp.sqrt(norm_sq) + frobenius_eps)
    current_gram = gram * (scale * scale)
    identity = jnp.eye(current_gram.shape[0], dtype=jnp.float32)
    accumulated = None
    for iteration in range(NS_ITERS):
        squared = jnp.dot(current_gram, current_gram, precision=ns_precision)
        polynomial = coef_first * identity + coef_second * current_gram + coef_third * squared
        if accumulated is None:
            accumulated = polynomial
        else:
            accumulated = jnp.dot(polynomial, accumulated, precision=ns_precision)
        if iteration + 1 < NS_ITERS:
            current_gram = jnp.dot(
                polynomial,
                jnp.dot(current_gram, polynomial, precision=ns_precision),
                precision=ns_precision,
            )
    current = jnp.dot(accumulated, owned * scale, precision=ns_precision)
    returned = lax.all_to_all(
        current.astype(jnp.bfloat16).reshape(dp_count, rows_local, piece_width),
        "dp",
        split_axis=0,
        concat_axis=0,
        tiled=True,
    ).reshape(slot_count, sub, rows_local, piece_width)
    my_rows = []
    for slot_id, mat in enumerate(slot_mats):
        width = mat.shape[1] // sub
        my_rows.append(
            returned[slot_id, :, :, :width]
            .astype(jnp.float32)
            .transpose(1, 0, 2)
            .reshape(rows_local, sub * width)
        )
    muon_step = muon_rate * match_rms
    qkv_list, proj_list, up_list, down_list = ([], [], [], [])
    for layer_id in range(LAYERS):
        base_slot = 4 * layer_id
        qkv_ortho = my_rows[base_slot].reshape(rows_local, 3, local_width)
        proj_ortho = my_rows[base_slot + 1].T
        up_ortho = my_rows[base_slot + 2]
        down_ortho = my_rows[base_slot + 3].T
        qkv_list.append(
            qkv_weight[layer_id].astype(jnp.float32) - muon_step * math.sqrt(3 * D) * qkv_ortho
        )
        proj_list.append(
            proj_weight[layer_id].astype(jnp.float32) - muon_step * math.sqrt(D) * proj_ortho
        )
        up_list.append(
            up_weight[layer_id].astype(jnp.float32) - muon_step * math.sqrt(FF) * up_ortho
        )
        down_list.append(
            down_weight[layer_id].astype(jnp.float32) - muon_step * math.sqrt(FF) * down_ortho
        )
    qkv_new = jnp.stack(qkv_list)
    proj_new = jnp.stack(proj_list)
    up_new = jnp.stack(up_list)
    down_new = jnp.stack(down_list)
    gains_new = vector_step(norm_gains, gains_grad)
    biases_new = vector_step(biases, biases_grad)
    qkv_bias_new = vector_step(qkv_bias, qkv_bias_grad)
    up_bias_new = vector_step(up_bias, up_bias_grad)
    return (
        stream,
        grad_stream,
        qkv_grad,
        proj_grad,
        up_grad,
        down_grad,
        gains_grad,
        biases_grad,
        qkv_bias_grad,
        up_bias_grad,
        qkv_new,
        proj_new,
        up_new,
        down_new,
        gains_new,
        biases_new,
        qkv_bias_new,
        up_bias_new,
        qkv_state_new,
        proj_state_new,
        up_state_new,
        down_state_new,
    )


def solution(mesh):
    return jax.shard_map(
        local,
        mesh=mesh,
        in_specs=(
            P(("dp", "tensor"), None),
            P(("dp", "tensor"), None),
            P("dp", None),
            P(None, "dp", None, "tensor"),
            P(None, "tensor", "dp"),
            P(None, "dp", "tensor"),
            P(None, "tensor", "dp"),
            P(),
            P(),
            P(),
            P(),
            P(None, "dp", None, "tensor"),
            P(None, "tensor", "dp"),
            P(None, "dp", "tensor"),
            P(None, "tensor", "dp"),
        ),
        out_specs=(
            P(("dp", "tensor"), None),
            P(("dp", "tensor"), None),
            P(None, "dp", None, "tensor"),
            P(None, "tensor", "dp"),
            P(None, "dp", "tensor"),
            P(None, "tensor", "dp"),
            P(),
            P(),
            P(),
            P(),
            P(None, "dp", None, "tensor"),
            P(None, "tensor", "dp"),
            P(None, "dp", "tensor"),
            P(None, "tensor", "dp"),
            P(),
            P(),
            P(),
            P(),
            P(None, "dp", None, "tensor"),
            P(None, "tensor", "dp"),
            P(None, "dp", "tensor"),
            P(None, "tensor", "dp"),
        ),
        check_vma=False,
    )
```

```python
import math

import jax
import jax.numpy as jnp
from jax import lax
from jax.sharding import PartitionSpec as P

D = 768
HD = 64
FF = 3072
ROT = 16
LAYERS = 2
NS_ITERS = 5


highest = lax.Precision.HIGHEST
ns_precision = lax.Precision.HIGH
norm_eps = 1e-05
masked_score = -1e30
coef_first = 3.4445
coef_second = -4.775
coef_third = 2.0315
momentum = 0.9
muon_rate = 0.2
match_rms = 0.2
vector_rate = 0.2
vector_eps = 1e-06
frobenius_eps = 1e-07


def rotary_tables(segment_row):
    length = segment_row.shape[0]
    indices = jnp.arange(length, dtype=jnp.int32)
    change = jnp.concatenate([jnp.ones((1,), dtype=bool), segment_row[1:] != segment_row[:-1]])
    starts = lax.cummax(jnp.where(change, indices, jnp.zeros_like(indices)), axis=0)
    positions = (indices - starts).astype(jnp.float32)
    half_rot = ROT // 2
    frequency = 10000.0 ** (-2.0 * jnp.arange(half_rot, dtype=jnp.float32) / ROT)
    angles = positions[:, None] * frequency[None, :]
    return (jnp.cos(angles), jnp.sin(angles))


def rotate(values, cosine_table, sine_table):
    half_rot = ROT // 2
    first_half = values[..., :half_rot]
    second_half = values[..., half_rot:ROT]
    cos_b = cosine_table[:, None, :]
    sin_b = sine_table[:, None, :]
    return jnp.concatenate(
        [
            first_half * cos_b - second_half * sin_b,
            second_half * cos_b + first_half * sin_b,
            values[..., ROT:],
        ],
        axis=-1,
    )


def unrotate(gradient, cosine_table, sine_table):
    half_rot = ROT // 2
    first_half = gradient[..., :half_rot]
    second_half = gradient[..., half_rot:ROT]
    cos_b = cosine_table[:, None, :]
    sin_b = sine_table[:, None, :]
    return jnp.concatenate(
        [
            first_half * cos_b + second_half * sin_b,
            second_half * cos_b - first_half * sin_b,
            gradient[..., ROT:],
        ],
        axis=-1,
    )


def normalize(stream):
    centered = stream - jnp.mean(stream, axis=-1, keepdims=True)
    inverse = lax.rsqrt(jnp.mean(centered * centered, axis=-1, keepdims=True) + norm_eps)
    return (centered * inverse, inverse)


def gelu_exact(values):
    return jax.nn.gelu(values, approximate=False)


def block_mask(segment_row, block_rows):
    query_pos = jnp.arange(block_rows, dtype=jnp.int32)
    key_pos = jnp.arange(segment_row.shape[0], dtype=jnp.int32)
    return (segment_row[:, None] == segment_row[None, :]) & (query_pos[:, None] >= key_pos[None, :])


def block_scores(queries, key_rows, allowed):
    scores = jnp.einsum(
        "qhe,khe->hqk", queries, key_rows, preferred_element_type=jnp.float32
    ) * queries.shape[-1] ** (-0.5)
    return jnp.where(allowed[None], scores, masked_score)


def attend(queries, key_rows, values, segment_row):
    length = queries.shape[0]
    block_rows = min(512, length)
    allowed = block_mask(segment_row, block_rows)
    scores = block_scores(queries, key_rows, allowed)
    row_peak = jnp.max(scores, axis=-1, keepdims=True)
    exponent = jnp.exp(scores - row_peak)
    row_total = jnp.sum(exponent, axis=-1, keepdims=True)
    probs_low = (exponent / row_total).astype(jnp.bfloat16)
    outputs = jnp.einsum(
        "hqk,khe->qhe", probs_low, values, preferred_element_type=jnp.float32
    ).astype(jnp.bfloat16)
    log_sums = row_peak + jnp.log(row_total)
    return (outputs, log_sums)


def attend_back(queries, key_rows, values, heads_grad, log_sums, segment_row):
    length = queries.shape[0]
    block_rows = min(512, length)
    scale_factor = queries.shape[-1] ** (-0.5)
    allowed = block_mask(segment_row, block_rows)
    scores = block_scores(queries, key_rows, allowed)
    probs_full = jnp.exp(scores - log_sums)
    probs_grad = jnp.einsum("qhe,khe->hqk", heads_grad, values, preferred_element_type=jnp.float32)
    row_dot = jnp.sum(probs_full * probs_grad, axis=-1, keepdims=True)
    score_grad = (probs_full * (probs_grad - row_dot)).astype(jnp.bfloat16)
    value_grad = jnp.einsum(
        "hqk,qhe->khe",
        probs_full.astype(jnp.bfloat16),
        heads_grad,
        preferred_element_type=jnp.float32,
    )
    query_grads = (
        jnp.einsum("hqk,khe->qhe", score_grad, key_rows, preferred_element_type=jnp.float32)
        * scale_factor
    )
    key_grad = (
        jnp.einsum("hqk,qhe->khe", score_grad, queries, preferred_element_type=jnp.float32)
        * scale_factor
    )
    return (query_grads, key_grad, value_grad)


def dp_scatter(partial, dimension):
    return lax.psum_scatter(partial, "dp", scatter_dimension=dimension, tiled=True)


def dp_gather(block, axis):
    return lax.all_gather(block, "dp", axis=axis, tiled=True)


def swap_pairs(count, bit):
    return [(i, i ^ bit) for i in range(count)]


def butterfly_sum(flat):
    count = lax.axis_size("dp")
    bit = 1
    while bit < count:
        flat = flat + lax.ppermute(flat, "dp", swap_pairs(count, bit))
        bit *= 2
    return flat + lax.ppermute(flat, "tensor", [(0, 1), (1, 0)])


def tensor_swap(block):
    return lax.ppermute(block, "tensor", [(0, 1), (1, 0)])


def tensor_gather(block):
    other = tensor_swap(block)
    first = lax.axis_index("tensor") == 0
    return jnp.where(
        first, jnp.concatenate([block, other], axis=0), jnp.concatenate([other, block], axis=0)
    )


def tensor_scatter(partial):
    rank = lax.axis_index("tensor")
    half = partial.shape[0] // 2
    mine = lax.dynamic_slice_in_dim(partial, rank * half, half, 0)
    theirs = lax.dynamic_slice_in_dim(partial, (1 - rank) * half, half, 0)
    return mine + tensor_swap(theirs)


def chip_gather_rows(block):
    count = lax.axis_size("dp")
    parity = lax.axis_index("dp") % 2
    half = block.shape[0] // 2
    halves = block.reshape((2, half) + block.shape[1:])
    outgoing = jnp.tile(halves, (count // 2,) + (1,) * block.ndim)
    got = lax.all_to_all(outgoing, "dp", split_axis=0, concat_axis=0, tiled=True)
    theirs = lax.ppermute(got, "dp", swap_pairs(count, 1))
    pair = jnp.where(parity == 0, jnp.stack([got, theirs], axis=1), jnp.stack([theirs, got], axis=1))
    return pair.reshape((count * 2 * half,) + block.shape[1:])


def chip_scatter_rows(partial):
    count = lax.axis_size("dp")
    parity = lax.axis_index("dp") % 2
    half = partial.shape[0] // count // 2
    blocks = partial.reshape((count, 2, half) + partial.shape[1:])
    keep = lax.dynamic_index_in_dim(blocks, parity, axis=1, keepdims=False)
    send = lax.dynamic_index_in_dim(blocks, 1 - parity, axis=1, keepdims=False)
    chip_sum = keep + lax.ppermute(send, "dp", swap_pairs(count, 1))
    got = lax.all_to_all(chip_sum, "dp", split_axis=0, concat_axis=0, tiled=True)
    got = got.reshape((count // 2, 2) + got.shape[1:])
    even = jnp.sum(got[:, 0], axis=0)
    odd = jnp.sum(got[:, 1], axis=0)
    return jnp.concatenate([even, odd], axis=0)


def scatter_layer(parts):
    qkv_part, proj_part, up_part, down_part = parts
    return (
        chip_scatter_rows(qkv_part),
        chip_scatter_rows(proj_part).T,
        dp_scatter(up_part, 0),
        chip_scatter_rows(down_part).T,
    )


def vector_step(params, gradients):
    return params - vector_rate * gradients * lax.rsqrt(
        jnp.mean(gradients * gradients, axis=-1, keepdims=True) + vector_eps
    )


def local(
    block_input,
    cotangent,
    segments,
    qkv_weight,
    proj_weight,
    up_weight,
    down_weight,
    norm_gains,
    biases,
    qkv_bias,
    up_bias,
    qkv_state,
    proj_state,
    up_state,
    down_state,
):
    tensor_rank = lax.axis_index("tensor")
    local_width = qkv_weight.shape[3]
    local_hidden = up_weight.shape[2]
    head_count = local_width // HD
    model_width = block_input.shape[1]
    segment_row = segments[0]
    cosine_table, sine_table = rotary_tables(segment_row)
    stream = block_input.astype(jnp.float32)
    saved_layers = []
    for layer_id in range(LAYERS):
        layer_weights = (
            dp_gather(qkv_weight[layer_id], 0)
            if layer_id == LAYERS - 1
            else chip_gather_rows(qkv_weight[layer_id]),
            chip_gather_rows(proj_weight[layer_id].T),
            dp_gather(up_weight[layer_id], 0),
            chip_gather_rows(down_weight[layer_id].T),
        )
        qkv_full, proj_full, up_full, down_full = layer_weights
        normed, inverse = normalize(stream)
        attn_rows = (normed * norm_gains[layer_id, 0] + biases[layer_id, 0]).astype(jnp.bfloat16)
        mlp_rows = (normed * norm_gains[layer_id, 1] + biases[layer_id, 1]).astype(jnp.bfloat16)
        both_in = tensor_gather(jnp.concatenate([attn_rows, mlp_rows], axis=1))
        attn_in, mlp_in = both_in[:, :model_width], both_in[:, model_width:]
        length = attn_in.shape[0]
        qkv_local_bias = lax.dynamic_slice_in_dim(
            qkv_bias[layer_id], tensor_rank * local_width, local_width, 1
        )
        qkv_pre = (
            jnp.einsum("ld,dcf->lcf", attn_in, qkv_full, preferred_element_type=jnp.float32)
            + qkv_local_bias
        )
        shaped = qkv_pre.reshape(length, 3, head_count, HD)
        queries = rotate(shaped[:, 0], cosine_table, sine_table).astype(jnp.bfloat16)
        key_rows = rotate(shaped[:, 1], cosine_table, sine_table).astype(jnp.bfloat16)
        values = shaped[:, 2].astype(jnp.bfloat16)
        heads_out, log_sums = attend(queries, key_rows, values, segment_row)
        heads_flat = heads_out.reshape(length, local_width)
        up_local_bias = lax.dynamic_slice_in_dim(
            up_bias[layer_id], tensor_rank * local_hidden, local_hidden, 0
        )
        up_pre = jnp.dot(mlp_in, up_full, preferred_element_type=jnp.float32) + up_local_bias
        act_low = gelu_exact(up_pre).astype(jnp.bfloat16)
        partial_sum = jnp.einsum(
            "lf,df->ld", heads_flat, proj_full, preferred_element_type=jnp.float32
        ) + jnp.einsum("lf,df->ld", act_low, down_full, preferred_element_type=jnp.float32)
        branch = tensor_scatter(partial_sum)
        saved_layers.append(
            (
                normed,
                inverse,
                attn_in,
                mlp_in,
                queries,
                key_rows,
                values,
                log_sums,
                heads_flat,
                up_pre,
                act_low,
                layer_weights,
            )
        )
        stream = stream + branch + biases[layer_id, 2] + biases[layer_id, 3]
    grad_stream = cotangent.astype(jnp.float32)
    gains_list = [None] * LAYERS
    biases_list = [None] * LAYERS
    qkv_bias_list = [None] * LAYERS
    up_bias_list = [None] * LAYERS
    weight_list = [None] * LAYERS
    for layer_id in reversed(range(LAYERS)):
        (
            normed,
            inverse,
            attn_in,
            mlp_in,
            queries,
            key_rows,
            values,
            log_sums,
            heads_flat,
            up_pre,
            act_low,
            layer_weights,
        ) = saved_layers[layer_id]
        qkv_full, proj_full, up_full, down_full = layer_weights
        length = attn_in.shape[0]
        out_bias_grad = jnp.sum(grad_stream, axis=0)
        branch_grad = tensor_gather(grad_stream.astype(jnp.bfloat16))
        down_part = jnp.einsum(
            "lf,ld->df", act_low, branch_grad, preferred_element_type=jnp.float32
        )
        act_grad = jnp.einsum(
            "ld,df->lf", branch_grad, down_full, preferred_element_type=jnp.float32
        )
        gelu_back = jax.vjp(gelu_exact, up_pre)[1]
        up_pre_grad = gelu_back(act_grad)[0].astype(jnp.bfloat16)
        up_bias_part = jnp.sum(up_pre_grad, axis=0, dtype=jnp.float32)
        up_part = jnp.einsum("ld,lf->df", mlp_in, up_pre_grad, preferred_element_type=jnp.float32)
        mlp_in_grad = jnp.einsum(
            "lf,df->ld", up_pre_grad, up_full, preferred_element_type=jnp.float32
        )
        proj_part = jnp.einsum(
            "lf,ld->df", heads_flat, branch_grad, preferred_element_type=jnp.float32
        )
        heads_grad = (
            jnp.einsum("ld,df->lf", branch_grad, proj_full, preferred_element_type=jnp.float32)
            .astype(jnp.bfloat16)
            .reshape(length, head_count, HD)
        )
        query_grad, key_grad, value_grad = attend_back(
            queries, key_rows, values, heads_grad, log_sums, segment_row
        )
        qkv_pre_grad = jnp.stack(
            [
                unrotate(query_grad, cosine_table, sine_table),
                unrotate(key_grad, cosine_table, sine_table),
                value_grad,
            ],
            axis=1,
        )
        qkv_pre_grad = qkv_pre_grad.reshape(length, 3, local_width).astype(jnp.bfloat16)
        qkv_bias_part = jnp.sum(qkv_pre_grad, axis=0, dtype=jnp.float32)
        qkv_part = jnp.einsum(
            "ld,lcf->dcf", attn_in, qkv_pre_grad, preferred_element_type=jnp.float32
        )
        attn_in_grad = jnp.einsum(
            "lcf,dcf->ld", qkv_pre_grad, qkv_full, preferred_element_type=jnp.float32
        )
        both_grad = tensor_scatter(jnp.concatenate([attn_in_grad, mlp_in_grad], axis=1))
        attn_rows_grad, mlp_rows_grad = both_grad[:, :model_width], both_grad[:, model_width:]
        gains_list[layer_id] = jnp.stack(
            [jnp.sum(attn_rows_grad * normed, axis=0), jnp.sum(mlp_rows_grad * normed, axis=0)]
        )
        biases_list[layer_id] = jnp.stack(
            [
                jnp.sum(attn_rows_grad, axis=0),
                jnp.sum(mlp_rows_grad, axis=0),
                out_bias_grad,
                out_bias_grad,
            ]
        )
        qkv_bias_list[layer_id] = lax.dynamic_update_slice_in_dim(
            jnp.zeros((3, model_width), jnp.float32), qkv_bias_part, tensor_rank * local_width, 1
        )
        up_bias_list[layer_id] = lax.dynamic_update_slice_in_dim(
            jnp.zeros((up_bias.shape[1],), jnp.float32), up_bias_part, tensor_rank * local_hidden, 0
        )
        normed_grad = (
            attn_rows_grad * norm_gains[layer_id, 0] + mlp_rows_grad * norm_gains[layer_id, 1]
        )
        normed_mean = jnp.mean(normed_grad, axis=-1, keepdims=True)
        product_mean = jnp.mean(normed_grad * normed, axis=-1, keepdims=True)
        grad_stream = grad_stream + inverse * (normed_grad - normed_mean - normed * product_mean)
        weight_list[layer_id] = (qkv_part, proj_part, up_part, down_part)
        if layer_id > 0:
            weight_list[layer_id] = scatter_layer(weight_list[layer_id])
            first_sum, grad_stream = lax.optimization_barrier((weight_list[layer_id][0], grad_stream))
            weight_list[layer_id] = (first_sum,) + weight_list[layer_id][1:]
    small_parts = (
        jnp.stack(gains_list),
        jnp.stack(biases_list),
        jnp.stack(qkv_bias_list),
        jnp.stack(up_bias_list),
    )
    flat = butterfly_sum(jnp.concatenate([part.reshape(-1) for part in small_parts]))
    small_sums = []
    offset = 0
    for part in small_parts:
        small_sums.append(flat[offset : offset + part.size].reshape(part.shape))
        offset += part.size
    gains_grad, biases_grad, qkv_bias_grad, up_bias_grad = small_sums
    flat, first_down = lax.optimization_barrier((flat, weight_list[0][3]))
    weight_list[0] = scatter_layer(weight_list[0][:3] + (first_down,))
    qkv_grad = jnp.stack([weight_list[layer_id][0] for layer_id in range(LAYERS)])
    proj_grad = jnp.stack([weight_list[layer_id][1] for layer_id in range(LAYERS)])
    up_grad = jnp.stack([weight_list[layer_id][2] for layer_id in range(LAYERS)])
    down_grad = jnp.stack([weight_list[layer_id][3] for layer_id in range(LAYERS)])
    qkv_state_new = momentum * qkv_state + qkv_grad
    proj_state_new = momentum * proj_state + proj_grad
    up_state_new = momentum * up_state + up_grad
    down_state_new = momentum * down_state + down_grad
    rows_local = qkv_state.shape[1]
    dp_count = lax.axis_size("dp")
    dp_rank = lax.axis_index("dp")
    slot_count = 4 * LAYERS
    sub = dp_count // slot_count
    piece_width = up_state.shape[2] // sub
    slot_mats = []
    for layer_id in range(LAYERS):
        slot_mats.append(qkv_state_new[layer_id].reshape(rows_local, 3 * local_width))
        slot_mats.append(proj_state_new[layer_id].T)
        slot_mats.append(up_state_new[layer_id])
        slot_mats.append(down_state_new[layer_id].T)
    pieces = []
    for mat in slot_mats:
        width = mat.shape[1] // sub
        split = mat.reshape(rows_local, sub, width).transpose(1, 0, 2)
        pieces.append(jnp.pad(split, ((0, 0), (0, 0), (0, piece_width - width))))
    outgoing = jnp.concatenate(pieces, axis=0)
    owned = lax.all_to_all(outgoing, "dp", split_axis=0, concat_axis=0, tiled=True)
    owned = owned.reshape(dp_count * rows_local, piece_width)
    owned, grad_stream = lax.optimization_barrier((owned, grad_stream))
    gram = jnp.dot(owned, owned.T, precision=ns_precision)
    bit = 1
    while bit < sub:
        gram = gram + lax.ppermute(gram, "dp", swap_pairs(dp_count, bit))
        bit *= 2
    core_half = dp_rank % 2
    half_rows = gram.shape[0] // 2
    mine = lax.dynamic_slice_in_dim(gram, core_half * half_rows, half_rows, 0)
    mine = mine + lax.ppermute(mine, "tensor", [(0, 1), (1, 0)])
    other = lax.ppermute(mine, "dp", swap_pairs(dp_count, 1))
    gram = jnp.where(
        core_half == 0,
        jnp.concatenate([mine, other], axis=0),
        jnp.concatenate([other, mine], axis=0),
    )
    norm_sq = jnp.trace(gram)
    scale = 1.0 / (jnp.sqrt(norm_sq) + frobenius_eps)
    current_gram = gram * (scale * scale)
    identity = jnp.eye(current_gram.shape[0], dtype=jnp.float32)
    accumulated = None
    for iteration in range(NS_ITERS):
        squared = jnp.dot(current_gram, current_gram, precision=ns_precision)
        polynomial = coef_first * identity + coef_second * current_gram + coef_third * squared
        if accumulated is None:
            accumulated = polynomial
        else:
            accumulated = jnp.dot(polynomial, accumulated, precision=ns_precision)
        if iteration + 1 < NS_ITERS:
            current_gram = jnp.dot(
                polynomial,
                jnp.dot(current_gram, polynomial, precision=ns_precision),
                precision=ns_precision,
            )
    current = jnp.dot(accumulated, owned * scale, precision=ns_precision)
    returned = lax.all_to_all(
        current.astype(jnp.bfloat16).reshape(dp_count, rows_local, piece_width),
        "dp",
        split_axis=0,
        concat_axis=0,
        tiled=True,
    ).reshape(slot_count, sub, rows_local, piece_width)
    my_rows = []
    for slot_id, mat in enumerate(slot_mats):
        width = mat.shape[1] // sub
        my_rows.append(
            returned[slot_id, :, :, :width]
            .astype(jnp.float32)
            .transpose(1, 0, 2)
            .reshape(rows_local, sub * width)
        )
    muon_step = muon_rate * match_rms
    qkv_list, proj_list, up_list, down_list = ([], [], [], [])
    for layer_id in range(LAYERS):
        base_slot = 4 * layer_id
        qkv_ortho = my_rows[base_slot].reshape(rows_local, 3, local_width)
        proj_ortho = my_rows[base_slot + 1].T
        up_ortho = my_rows[base_slot + 2]
        down_ortho = my_rows[base_slot + 3].T
        qkv_list.append(
            qkv_weight[layer_id].astype(jnp.float32) - muon_step * math.sqrt(3 * D) * qkv_ortho
        )
        proj_list.append(
            proj_weight[layer_id].astype(jnp.float32) - muon_step * math.sqrt(D) * proj_ortho
        )
        up_list.append(
            up_weight[layer_id].astype(jnp.float32) - muon_step * math.sqrt(FF) * up_ortho
        )
        down_list.append(
            down_weight[layer_id].astype(jnp.float32) - muon_step * math.sqrt(FF) * down_ortho
        )
    qkv_new = jnp.stack(qkv_list)
    proj_new = jnp.stack(proj_list)
    up_new = jnp.stack(up_list)
    down_new = jnp.stack(down_list)
    gains_new = vector_step(norm_gains, gains_grad)
    biases_new = vector_step(biases, biases_grad)
    qkv_bias_new = vector_step(qkv_bias, qkv_bias_grad)
    up_bias_new = vector_step(up_bias, up_bias_grad)
    return (
        stream,
        grad_stream,
        qkv_grad,
        proj_grad,
        up_grad,
        down_grad,
        gains_grad,
        biases_grad,
        qkv_bias_grad,
        up_bias_grad,
        qkv_new,
        proj_new,
        up_new,
        down_new,
        gains_new,
        biases_new,
        qkv_bias_new,
        up_bias_new,
        qkv_state_new,
        proj_state_new,
        up_state_new,
        down_state_new,
    )


def solution(mesh):
    return jax.shard_map(
        local,
        mesh=mesh,
        in_specs=(
            P(("dp", "tensor"), None),
            P(("dp", "tensor"), None),
            P("dp", None),
            P(None, "dp", None, "tensor"),
            P(None, "tensor", "dp"),
            P(None, "dp", "tensor"),
            P(None, "tensor", "dp"),
            P(),
            P(),
            P(),
            P(),
            P(None, "dp", None, "tensor"),
            P(None, "tensor", "dp"),
            P(None, "dp", "tensor"),
            P(None, "tensor", "dp"),
        ),
        out_specs=(
            P(("dp", "tensor"), None),
            P(("dp", "tensor"), None),
            P(None, "dp", None, "tensor"),
            P(None, "tensor", "dp"),
            P(None, "dp", "tensor"),
            P(None, "tensor", "dp"),
            P(),
            P(),
            P(),
            P(),
            P(None, "dp", None, "tensor"),
            P(None, "tensor", "dp"),
            P(None, "dp", "tensor"),
            P(None, "tensor", "dp"),
            P(),
            P(),
            P(),
            P(),
            P(None, "dp", None, "tensor"),
            P(None, "tensor", "dp"),
            P(None, "dp", "tensor"),
            P(None, "tensor", "dp"),
        ),
        check_vma=False,
    )
```

```python
import math

import jax
import jax.numpy as jnp
from jax import lax
from jax.sharding import PartitionSpec as P

D = 768
HD = 64
FF = 3072
ROT = 16
LAYERS = 2
NS_ITERS = 5


highest = lax.Precision.HIGHEST
ns_precision = lax.Precision.HIGH
norm_eps = 1e-05
masked_score = -1e30
coef_first = 3.4445
coef_second = -4.775
coef_third = 2.0315
momentum = 0.9
muon_rate = 0.2
match_rms = 0.2
vector_rate = 0.2
vector_eps = 1e-06
frobenius_eps = 1e-07


def rotary_tables(segment_row):
    length = segment_row.shape[0]
    indices = jnp.arange(length, dtype=jnp.int32)
    change = jnp.concatenate([jnp.ones((1,), dtype=bool), segment_row[1:] != segment_row[:-1]])
    starts = lax.cummax(jnp.where(change, indices, jnp.zeros_like(indices)), axis=0)
    positions = (indices - starts).astype(jnp.float32)
    half_rot = ROT // 2
    frequency = 10000.0 ** (-2.0 * jnp.arange(half_rot, dtype=jnp.float32) / ROT)
    angles = positions[:, None] * frequency[None, :]
    return (jnp.cos(angles), jnp.sin(angles))


def rotate(values, cosine_table, sine_table):
    half_rot = ROT // 2
    first_half = values[..., :half_rot]
    second_half = values[..., half_rot:ROT]
    cos_b = cosine_table[:, None, :]
    sin_b = sine_table[:, None, :]
    return jnp.concatenate(
        [
            first_half * cos_b - second_half * sin_b,
            second_half * cos_b + first_half * sin_b,
            values[..., ROT:],
        ],
        axis=-1,
    )


def unrotate(gradient, cosine_table, sine_table):
    half_rot = ROT // 2
    first_half = gradient[..., :half_rot]
    second_half = gradient[..., half_rot:ROT]
    cos_b = cosine_table[:, None, :]
    sin_b = sine_table[:, None, :]
    return jnp.concatenate(
        [
            first_half * cos_b + second_half * sin_b,
            second_half * cos_b - first_half * sin_b,
            gradient[..., ROT:],
        ],
        axis=-1,
    )


def normalize(stream):
    centered = stream - jnp.mean(stream, axis=-1, keepdims=True)
    inverse = lax.rsqrt(jnp.mean(centered * centered, axis=-1, keepdims=True) + norm_eps)
    return (centered * inverse, inverse)


def gelu_exact(values):
    return jax.nn.gelu(values, approximate=False)


def block_mask(segment_row, block_rows):
    query_pos = jnp.arange(block_rows, dtype=jnp.int32)
    key_pos = jnp.arange(segment_row.shape[0], dtype=jnp.int32)
    return (segment_row[:, None] == segment_row[None, :]) & (query_pos[:, None] >= key_pos[None, :])


def block_scores(queries, key_rows, allowed):
    scores = jnp.einsum(
        "qhe,khe->hqk", queries, key_rows, preferred_element_type=jnp.float32
    ) * queries.shape[-1] ** (-0.5)
    return jnp.where(allowed[None], scores, masked_score)


def attend(queries, key_rows, values, segment_row):
    length = queries.shape[0]
    block_rows = min(512, length)
    allowed = block_mask(segment_row, block_rows)
    scores = block_scores(queries, key_rows, allowed)
    row_peak = jnp.max(scores, axis=-1, keepdims=True)
    exponent = jnp.exp(scores - row_peak)
    row_total = jnp.sum(exponent, axis=-1, keepdims=True)
    probs_low = (exponent / row_total).astype(jnp.bfloat16)
    outputs = jnp.einsum(
        "hqk,khe->qhe", probs_low, values, preferred_element_type=jnp.float32
    ).astype(jnp.bfloat16)
    log_sums = row_peak + jnp.log(row_total)
    return (outputs, log_sums)


def attend_back(queries, key_rows, values, heads_grad, log_sums, segment_row):
    length = queries.shape[0]
    block_rows = min(512, length)
    scale_factor = queries.shape[-1] ** (-0.5)
    allowed = block_mask(segment_row, block_rows)
    scores = block_scores(queries, key_rows, allowed)
    probs_full = jnp.exp(scores - log_sums)
    probs_grad = jnp.einsum("qhe,khe->hqk", heads_grad, values, preferred_element_type=jnp.float32)
    row_dot = jnp.sum(probs_full * probs_grad, axis=-1, keepdims=True)
    score_grad = (probs_full * (probs_grad - row_dot)).astype(jnp.bfloat16)
    value_grad = jnp.einsum(
        "hqk,qhe->khe",
        probs_full.astype(jnp.bfloat16),
        heads_grad,
        preferred_element_type=jnp.float32,
    )
    query_grads = (
        jnp.einsum("hqk,khe->qhe", score_grad, key_rows, preferred_element_type=jnp.float32)
        * scale_factor
    )
    key_grad = (
        jnp.einsum("hqk,qhe->khe", score_grad, queries, preferred_element_type=jnp.float32)
        * scale_factor
    )
    return (query_grads, key_grad, value_grad)


def dp_scatter(partial, dimension):
    return lax.psum_scatter(partial, "dp", scatter_dimension=dimension, tiled=True)


def dp_gather(block, axis):
    return lax.all_gather(block, "dp", axis=axis, tiled=True)


def swap_pairs(count, bit):
    return [(i, i ^ bit) for i in range(count)]


def butterfly_sum(flat):
    count = lax.axis_size("dp")
    bit = 1
    while bit < count:
        flat = flat + lax.ppermute(flat, "dp", swap_pairs(count, bit))
        bit *= 2
    return flat + lax.ppermute(flat, "tensor", [(0, 1), (1, 0)])


def tensor_swap(block):
    return lax.ppermute(block, "tensor", [(0, 1), (1, 0)])


def tensor_gather(block):
    other = tensor_swap(block)
    first = lax.axis_index("tensor") == 0
    return jnp.where(
        first, jnp.concatenate([block, other], axis=0), jnp.concatenate([other, block], axis=0)
    )


def tensor_scatter(partial):
    rank = lax.axis_index("tensor")
    half = partial.shape[0] // 2
    mine = lax.dynamic_slice_in_dim(partial, rank * half, half, 0)
    theirs = lax.dynamic_slice_in_dim(partial, (1 - rank) * half, half, 0)
    return mine + tensor_swap(theirs)


def chip_gather_rows(block):
    count = lax.axis_size("dp")
    parity = lax.axis_index("dp") % 2
    half = block.shape[0] // 2
    halves = block.reshape((2, half) + block.shape[1:])
    outgoing = jnp.tile(halves, (count // 2,) + (1,) * block.ndim)
    got = lax.all_to_all(outgoing, "dp", split_axis=0, concat_axis=0, tiled=True)
    theirs = lax.ppermute(got, "dp", swap_pairs(count, 1))
    pair = jnp.where(parity == 0, jnp.stack([got, theirs], axis=1), jnp.stack([theirs, got], axis=1))
    return pair.reshape((count * 2 * half,) + block.shape[1:])


def chip_scatter_rows(partial):
    count = lax.axis_size("dp")
    parity = lax.axis_index("dp") % 2
    half = partial.shape[0] // count // 2
    blocks = partial.reshape((count, 2, half) + partial.shape[1:])
    keep = lax.dynamic_index_in_dim(blocks, parity, axis=1, keepdims=False)
    send = lax.dynamic_index_in_dim(blocks, 1 - parity, axis=1, keepdims=False)
    chip_sum = keep + lax.ppermute(send, "dp", swap_pairs(count, 1))
    got = lax.all_to_all(chip_sum, "dp", split_axis=0, concat_axis=0, tiled=True)
    got = got.reshape((count // 2, 2) + got.shape[1:])
    even = jnp.sum(got[:, 0], axis=0)
    odd = jnp.sum(got[:, 1], axis=0)
    return jnp.concatenate([even, odd], axis=0)


def scatter_layer(parts, proj_whole=False):
    qkv_part, proj_part, up_part, down_part = parts
    return (
        chip_scatter_rows(qkv_part),
        (dp_scatter(proj_part, 0) if proj_whole else chip_scatter_rows(proj_part)).T,
        dp_scatter(up_part, 0),
        chip_scatter_rows(down_part).T,
    )


def vector_step(params, gradients):
    return params - vector_rate * gradients * lax.rsqrt(
        jnp.mean(gradients * gradients, axis=-1, keepdims=True) + vector_eps
    )


def local(
    block_input,
    cotangent,
    segments,
    qkv_weight,
    proj_weight,
    up_weight,
    down_weight,
    norm_gains,
    biases,
    qkv_bias,
    up_bias,
    qkv_state,
    proj_state,
    up_state,
    down_state,
):
    tensor_rank = lax.axis_index("tensor")
    local_width = qkv_weight.shape[3]
    local_hidden = up_weight.shape[2]
    head_count = local_width // HD
    model_width = block_input.shape[1]
    segment_row = segments[0]
    cosine_table, sine_table = rotary_tables(segment_row)
    stream = block_input.astype(jnp.float32)
    saved_layers = []
    for layer_id in range(LAYERS):
        layer_weights = (
            dp_gather(qkv_weight[layer_id], 0)
            if layer_id == LAYERS - 1
            else chip_gather_rows(qkv_weight[layer_id]),
            chip_gather_rows(proj_weight[layer_id].T),
            dp_gather(up_weight[layer_id], 0),
            chip_gather_rows(down_weight[layer_id].T),
        )
        qkv_full, proj_full, up_full, down_full = layer_weights
        normed, inverse = normalize(stream)
        attn_rows = (normed * norm_gains[layer_id, 0] + biases[layer_id, 0]).astype(jnp.bfloat16)
        mlp_rows = (normed * norm_gains[layer_id, 1] + biases[layer_id, 1]).astype(jnp.bfloat16)
        both_in = tensor_gather(jnp.concatenate([attn_rows, mlp_rows], axis=1))
        attn_in, mlp_in = both_in[:, :model_width], both_in[:, model_width:]
        length = attn_in.shape[0]
        qkv_local_bias = lax.dynamic_slice_in_dim(
            qkv_bias[layer_id], tensor_rank * local_width, local_width, 1
        )
        qkv_pre = (
            jnp.einsum("ld,dcf->lcf", attn_in, qkv_full, preferred_element_type=jnp.float32)
            + qkv_local_bias
        )
        shaped = qkv_pre.reshape(length, 3, head_count, HD)
        queries = rotate(shaped[:, 0], cosine_table, sine_table).astype(jnp.bfloat16)
        key_rows = rotate(shaped[:, 1], cosine_table, sine_table).astype(jnp.bfloat16)
        values = shaped[:, 2].astype(jnp.bfloat16)
        heads_out, log_sums = attend(queries, key_rows, values, segment_row)
        heads_flat = heads_out.reshape(length, local_width)
        up_local_bias = lax.dynamic_slice_in_dim(
            up_bias[layer_id], tensor_rank * local_hidden, local_hidden, 0
        )
        up_pre = jnp.dot(mlp_in, up_full, preferred_element_type=jnp.float32) + up_local_bias
        act_low = gelu_exact(up_pre).astype(jnp.bfloat16)
        partial_sum = jnp.einsum(
            "lf,df->ld", heads_flat, proj_full, preferred_element_type=jnp.float32
        ) + jnp.einsum("lf,df->ld", act_low, down_full, preferred_element_type=jnp.float32)
        branch = tensor_scatter(partial_sum)
        saved_layers.append(
            (
                normed,
                inverse,
                attn_in,
                mlp_in,
                queries,
                key_rows,
                values,
                log_sums,
                heads_flat,
                up_pre,
                act_low,
                layer_weights,
            )
        )
        stream = stream + branch + biases[layer_id, 2] + biases[layer_id, 3]
    grad_stream = cotangent.astype(jnp.float32)
    gains_list = [None] * LAYERS
    biases_list = [None] * LAYERS
    qkv_bias_list = [None] * LAYERS
    up_bias_list = [None] * LAYERS
    weight_list = [None] * LAYERS
    for layer_id in reversed(range(LAYERS)):
        (
            normed,
            inverse,
            attn_in,
            mlp_in,
            queries,
            key_rows,
            values,
            log_sums,
            heads_flat,
            up_pre,
            act_low,
            layer_weights,
        ) = saved_layers[layer_id]
        qkv_full, proj_full, up_full, down_full = layer_weights
        length = attn_in.shape[0]
        out_bias_grad = jnp.sum(grad_stream, axis=0)
        branch_grad = tensor_gather(grad_stream.astype(jnp.bfloat16))
        down_part = jnp.einsum(
            "lf,ld->df", act_low, branch_grad, preferred_element_type=jnp.float32
        )
        act_grad = jnp.einsum(
            "ld,df->lf", branch_grad, down_full, preferred_element_type=jnp.float32
        )
        gelu_back = jax.vjp(gelu_exact, up_pre)[1]
        up_pre_grad = gelu_back(act_grad)[0].astype(jnp.bfloat16)
        up_bias_part = jnp.sum(up_pre_grad, axis=0, dtype=jnp.float32)
        up_part = jnp.einsum("ld,lf->df", mlp_in, up_pre_grad, preferred_element_type=jnp.float32)
        mlp_in_grad = jnp.einsum(
            "lf,df->ld", up_pre_grad, up_full, preferred_element_type=jnp.float32
        )
        proj_part = jnp.einsum(
            "lf,ld->df", heads_flat, branch_grad, preferred_element_type=jnp.float32
        )
        heads_grad = (
            jnp.einsum("ld,df->lf", branch_grad, proj_full, preferred_element_type=jnp.float32)
            .astype(jnp.bfloat16)
            .reshape(length, head_count, HD)
        )
        query_grad, key_grad, value_grad = attend_back(
            queries, key_rows, values, heads_grad, log_sums, segment_row
        )
        qkv_pre_grad = jnp.stack(
            [
                unrotate(query_grad, cosine_table, sine_table),
                unrotate(key_grad, cosine_table, sine_table),
                value_grad,
            ],
            axis=1,
        )
        qkv_pre_grad = qkv_pre_grad.reshape(length, 3, local_width).astype(jnp.bfloat16)
        qkv_bias_part = jnp.sum(qkv_pre_grad, axis=0, dtype=jnp.float32)
        qkv_part = jnp.einsum(
            "ld,lcf->dcf", attn_in, qkv_pre_grad, preferred_element_type=jnp.float32
        )
        attn_in_grad = jnp.einsum(
            "lcf,dcf->ld", qkv_pre_grad, qkv_full, preferred_element_type=jnp.float32
        )
        both_grad = tensor_scatter(jnp.concatenate([attn_in_grad, mlp_in_grad], axis=1))
        attn_rows_grad, mlp_rows_grad = both_grad[:, :model_width], both_grad[:, model_width:]
        gains_list[layer_id] = jnp.stack(
            [jnp.sum(attn_rows_grad * normed, axis=0), jnp.sum(mlp_rows_grad * normed, axis=0)]
        )
        biases_list[layer_id] = jnp.stack(
            [
                jnp.sum(attn_rows_grad, axis=0),
                jnp.sum(mlp_rows_grad, axis=0),
                out_bias_grad,
                out_bias_grad,
            ]
        )
        qkv_bias_list[layer_id] = lax.dynamic_update_slice_in_dim(
            jnp.zeros((3, model_width), jnp.float32), qkv_bias_part, tensor_rank * local_width, 1
        )
        up_bias_list[layer_id] = lax.dynamic_update_slice_in_dim(
            jnp.zeros((up_bias.shape[1],), jnp.float32), up_bias_part, tensor_rank * local_hidden, 0
        )
        normed_grad = (
            attn_rows_grad * norm_gains[layer_id, 0] + mlp_rows_grad * norm_gains[layer_id, 1]
        )
        normed_mean = jnp.mean(normed_grad, axis=-1, keepdims=True)
        product_mean = jnp.mean(normed_grad * normed, axis=-1, keepdims=True)
        grad_stream = grad_stream + inverse * (normed_grad - normed_mean - normed * product_mean)
        weight_list[layer_id] = (qkv_part, proj_part, up_part, down_part)
        if layer_id > 0:
            weight_list[layer_id] = scatter_layer(weight_list[layer_id], proj_whole=True)
            first_sum, grad_stream = lax.optimization_barrier((weight_list[layer_id][0], grad_stream))
            weight_list[layer_id] = (first_sum,) + weight_list[layer_id][1:]
    small_parts = (
        jnp.stack(gains_list),
        jnp.stack(biases_list),
        jnp.stack(qkv_bias_list),
        jnp.stack(up_bias_list),
    )
    flat = butterfly_sum(jnp.concatenate([part.reshape(-1) for part in small_parts]))
    small_sums = []
    offset = 0
    for part in small_parts:
        small_sums.append(flat[offset : offset + part.size].reshape(part.shape))
        offset += part.size
    gains_grad, biases_grad, qkv_bias_grad, up_bias_grad = small_sums
    flat, first_down = lax.optimization_barrier((flat, weight_list[0][3]))
    weight_list[0] = scatter_layer(weight_list[0][:3] + (first_down,))
    qkv_grad = jnp.stack([weight_list[layer_id][0] for layer_id in range(LAYERS)])
    proj_grad = jnp.stack([weight_list[layer_id][1] for layer_id in range(LAYERS)])
    up_grad = jnp.stack([weight_list[layer_id][2] for layer_id in range(LAYERS)])
    down_grad = jnp.stack([weight_list[layer_id][3] for layer_id in range(LAYERS)])
    qkv_state_new = momentum * qkv_state + qkv_grad
    proj_state_new = momentum * proj_state + proj_grad
    up_state_new = momentum * up_state + up_grad
    down_state_new = momentum * down_state + down_grad
    rows_local = qkv_state.shape[1]
    dp_count = lax.axis_size("dp")
    dp_rank = lax.axis_index("dp")
    slot_count = 4 * LAYERS
    sub = dp_count // slot_count
    piece_width = up_state.shape[2] // sub
    slot_mats = []
    for layer_id in range(LAYERS):
        slot_mats.append(qkv_state_new[layer_id].reshape(rows_local, 3 * local_width))
        slot_mats.append(proj_state_new[layer_id].T)
        slot_mats.append(up_state_new[layer_id])
        slot_mats.append(down_state_new[layer_id].T)
    pieces = []
    for mat in slot_mats:
        width = mat.shape[1] // sub
        split = mat.reshape(rows_local, sub, width).transpose(1, 0, 2)
        pieces.append(jnp.pad(split, ((0, 0), (0, 0), (0, piece_width - width))))
    outgoing = jnp.concatenate(pieces, axis=0)
    owned = lax.all_to_all(outgoing, "dp", split_axis=0, concat_axis=0, tiled=True)
    owned = owned.reshape(dp_count * rows_local, piece_width)
    owned, grad_stream = lax.optimization_barrier((owned, grad_stream))
    gram = jnp.dot(owned, owned.T, precision=ns_precision)
    bit = 1
    while bit < sub:
        gram = gram + lax.ppermute(gram, "dp", swap_pairs(dp_count, bit))
        bit *= 2
    core_half = dp_rank % 2
    half_rows = gram.shape[0] // 2
    mine = lax.dynamic_slice_in_dim(gram, core_half * half_rows, half_rows, 0)
    mine = mine + lax.ppermute(mine, "tensor", [(0, 1), (1, 0)])
    other = lax.ppermute(mine, "dp", swap_pairs(dp_count, 1))
    gram = jnp.where(
        core_half == 0,
        jnp.concatenate([mine, other], axis=0),
        jnp.concatenate([other, mine], axis=0),
    )
    norm_sq = jnp.trace(gram)
    scale = 1.0 / (jnp.sqrt(norm_sq) + frobenius_eps)
    current_gram = gram * (scale * scale)
    identity = jnp.eye(current_gram.shape[0], dtype=jnp.float32)
    accumulated = None
    for iteration in range(NS_ITERS):
        squared = jnp.dot(current_gram, current_gram, precision=ns_precision)
        polynomial = coef_first * identity + coef_second * current_gram + coef_third * squared
        if accumulated is None:
            accumulated = polynomial
        else:
            accumulated = jnp.dot(polynomial, accumulated, precision=ns_precision)
        if iteration + 1 < NS_ITERS:
            current_gram = jnp.dot(
                polynomial,
                jnp.dot(current_gram, polynomial, precision=ns_precision),
                precision=ns_precision,
            )
    current = jnp.dot(accumulated, owned * scale, precision=ns_precision)
    returned = lax.all_to_all(
        current.astype(jnp.bfloat16).reshape(dp_count, rows_local, piece_width),
        "dp",
        split_axis=0,
        concat_axis=0,
        tiled=True,
    ).reshape(slot_count, sub, rows_local, piece_width)
    my_rows = []
    for slot_id, mat in enumerate(slot_mats):
        width = mat.shape[1] // sub
        my_rows.append(
            returned[slot_id, :, :, :width]
            .astype(jnp.float32)
            .transpose(1, 0, 2)
            .reshape(rows_local, sub * width)
        )
    muon_step = muon_rate * match_rms
    qkv_list, proj_list, up_list, down_list = ([], [], [], [])
    for layer_id in range(LAYERS):
        base_slot = 4 * layer_id
        qkv_ortho = my_rows[base_slot].reshape(rows_local, 3, local_width)
        proj_ortho = my_rows[base_slot + 1].T
        up_ortho = my_rows[base_slot + 2]
        down_ortho = my_rows[base_slot + 3].T
        qkv_list.append(
            qkv_weight[layer_id].astype(jnp.float32) - muon_step * math.sqrt(3 * D) * qkv_ortho
        )
        proj_list.append(
            proj_weight[layer_id].astype(jnp.float32) - muon_step * math.sqrt(D) * proj_ortho
        )
        up_list.append(
            up_weight[layer_id].astype(jnp.float32) - muon_step * math.sqrt(FF) * up_ortho
        )
        down_list.append(
            down_weight[layer_id].astype(jnp.float32) - muon_step * math.sqrt(FF) * down_ortho
        )
    qkv_new = jnp.stack(qkv_list)
    proj_new = jnp.stack(proj_list)
    up_new = jnp.stack(up_list)
    down_new = jnp.stack(down_list)
    gains_new = vector_step(norm_gains, gains_grad)
    biases_new = vector_step(biases, biases_grad)
    qkv_bias_new = vector_step(qkv_bias, qkv_bias_grad)
    up_bias_new = vector_step(up_bias, up_bias_grad)
    return (
        stream,
        grad_stream,
        qkv_grad,
        proj_grad,
        up_grad,
        down_grad,
        gains_grad,
        biases_grad,
        qkv_bias_grad,
        up_bias_grad,
        qkv_new,
        proj_new,
        up_new,
        down_new,
        gains_new,
        biases_new,
        qkv_bias_new,
        up_bias_new,
        qkv_state_new,
        proj_state_new,
        up_state_new,
        down_state_new,
    )


def solution(mesh):
    return jax.shard_map(
        local,
        mesh=mesh,
        in_specs=(
            P(("dp", "tensor"), None),
            P(("dp", "tensor"), None),
            P("dp", None),
            P(None, "dp", None, "tensor"),
            P(None, "tensor", "dp"),
            P(None, "dp", "tensor"),
            P(None, "tensor", "dp"),
            P(),
            P(),
            P(),
            P(),
            P(None, "dp", None, "tensor"),
            P(None, "tensor", "dp"),
            P(None, "dp", "tensor"),
            P(None, "tensor", "dp"),
        ),
        out_specs=(
            P(("dp", "tensor"), None),
            P(("dp", "tensor"), None),
            P(None, "dp", None, "tensor"),
            P(None, "tensor", "dp"),
            P(None, "dp", "tensor"),
            P(None, "tensor", "dp"),
            P(),
            P(),
            P(),
            P(),
            P(None, "dp", None, "tensor"),
            P(None, "tensor", "dp"),
            P(None, "dp", "tensor"),
            P(None, "tensor", "dp"),
            P(),
            P(),
            P(),
            P(),
            P(None, "dp", None, "tensor"),
            P(None, "tensor", "dp"),
            P(None, "dp", "tensor"),
            P(None, "tensor", "dp"),
        ),
        check_vma=False,
    )
```

```python
import math

import jax
import jax.numpy as jnp
from jax import lax
from jax.sharding import PartitionSpec as P

D = 768
HD = 64
FF = 3072
ROT = 16
LAYERS = 2
NS_ITERS = 5


highest = lax.Precision.HIGHEST
ns_precision = lax.Precision.HIGH
norm_eps = 1e-05
masked_score = -1e30
coef_first = 3.4445
coef_second = -4.775
coef_third = 2.0315
momentum = 0.9
muon_rate = 0.2
match_rms = 0.2
vector_rate = 0.2
vector_eps = 1e-06
frobenius_eps = 1e-07


def rotary_tables(segment_row):
    length = segment_row.shape[0]
    indices = jnp.arange(length, dtype=jnp.int32)
    change = jnp.concatenate([jnp.ones((1,), dtype=bool), segment_row[1:] != segment_row[:-1]])
    starts = lax.cummax(jnp.where(change, indices, jnp.zeros_like(indices)), axis=0)
    positions = (indices - starts).astype(jnp.float32)
    half_rot = ROT // 2
    frequency = 10000.0 ** (-2.0 * jnp.arange(half_rot, dtype=jnp.float32) / ROT)
    angles = positions[:, None] * frequency[None, :]
    return (jnp.cos(angles), jnp.sin(angles))


def rotate(values, cosine_table, sine_table):
    half_rot = ROT // 2
    first_half = values[..., :half_rot]
    second_half = values[..., half_rot:ROT]
    cos_b = cosine_table[:, None, :]
    sin_b = sine_table[:, None, :]
    return jnp.concatenate(
        [
            first_half * cos_b - second_half * sin_b,
            second_half * cos_b + first_half * sin_b,
            values[..., ROT:],
        ],
        axis=-1,
    )


def unrotate(gradient, cosine_table, sine_table):
    half_rot = ROT // 2
    first_half = gradient[..., :half_rot]
    second_half = gradient[..., half_rot:ROT]
    cos_b = cosine_table[:, None, :]
    sin_b = sine_table[:, None, :]
    return jnp.concatenate(
        [
            first_half * cos_b + second_half * sin_b,
            second_half * cos_b - first_half * sin_b,
            gradient[..., ROT:],
        ],
        axis=-1,
    )


def normalize(stream):
    centered = stream - jnp.mean(stream, axis=-1, keepdims=True)
    inverse = lax.rsqrt(jnp.mean(centered * centered, axis=-1, keepdims=True) + norm_eps)
    return (centered * inverse, inverse)


def gelu_exact(values):
    return jax.nn.gelu(values, approximate=False)


def block_mask(segment_row, block_rows):
    query_pos = jnp.arange(block_rows, dtype=jnp.int32)
    key_pos = jnp.arange(segment_row.shape[0], dtype=jnp.int32)
    return (segment_row[:, None] == segment_row[None, :]) & (query_pos[:, None] >= key_pos[None, :])


def block_scores(queries, key_rows, allowed):
    scores = jnp.einsum(
        "qhe,khe->hqk", queries, key_rows, preferred_element_type=jnp.float32
    ) * queries.shape[-1] ** (-0.5)
    return jnp.where(allowed[None], scores, masked_score)


def attend(queries, key_rows, values, segment_row):
    length = queries.shape[0]
    block_rows = min(512, length)
    allowed = block_mask(segment_row, block_rows)
    scores = block_scores(queries, key_rows, allowed)
    row_peak = jnp.max(scores, axis=-1, keepdims=True)
    exponent = jnp.exp(scores - row_peak)
    row_total = jnp.sum(exponent, axis=-1, keepdims=True)
    probs_low = (exponent / row_total).astype(jnp.bfloat16)
    outputs = jnp.einsum(
        "hqk,khe->qhe", probs_low, values, preferred_element_type=jnp.float32
    ).astype(jnp.bfloat16)
    log_sums = row_peak + jnp.log(row_total)
    return (outputs, log_sums)


def attend_back(queries, key_rows, values, heads_grad, log_sums, segment_row):
    length = queries.shape[0]
    block_rows = min(512, length)
    scale_factor = queries.shape[-1] ** (-0.5)
    allowed = block_mask(segment_row, block_rows)
    scores = block_scores(queries, key_rows, allowed)
    probs_full = jnp.exp(scores - log_sums)
    probs_grad = jnp.einsum("qhe,khe->hqk", heads_grad, values, preferred_element_type=jnp.float32)
    row_dot = jnp.sum(probs_full * probs_grad, axis=-1, keepdims=True)
    score_grad = (probs_full * (probs_grad - row_dot)).astype(jnp.bfloat16)
    value_grad = jnp.einsum(
        "hqk,qhe->khe",
        probs_full.astype(jnp.bfloat16),
        heads_grad,
        preferred_element_type=jnp.float32,
    )
    query_grads = (
        jnp.einsum("hqk,khe->qhe", score_grad, key_rows, preferred_element_type=jnp.float32)
        * scale_factor
    )
    key_grad = (
        jnp.einsum("hqk,qhe->khe", score_grad, queries, preferred_element_type=jnp.float32)
        * scale_factor
    )
    return (query_grads, key_grad, value_grad)


def dp_scatter(partial, dimension):
    return lax.psum_scatter(partial, "dp", scatter_dimension=dimension, tiled=True)


def dp_gather(block, axis):
    return lax.all_gather(block, "dp", axis=axis, tiled=True)


def swap_pairs(count, bit):
    return [(i, i ^ bit) for i in range(count)]


def butterfly_sum(flat):
    count = lax.axis_size("dp")
    bit = 1
    while bit < count:
        flat = flat + lax.ppermute(flat, "dp", swap_pairs(count, bit))
        bit *= 2
    return flat + lax.ppermute(flat, "tensor", [(0, 1), (1, 0)])


def tensor_swap(block):
    return lax.ppermute(block, "tensor", [(0, 1), (1, 0)])


def tensor_gather(block):
    other = tensor_swap(block)
    first = lax.axis_index("tensor") == 0
    return jnp.where(
        first, jnp.concatenate([block, other], axis=0), jnp.concatenate([other, block], axis=0)
    )


def tensor_scatter(partial):
    rank = lax.axis_index("tensor")
    half = partial.shape[0] // 2
    mine = lax.dynamic_slice_in_dim(partial, rank * half, half, 0)
    theirs = lax.dynamic_slice_in_dim(partial, (1 - rank) * half, half, 0)
    return mine + tensor_swap(theirs)


def chip_gather_rows(block):
    count = lax.axis_size("dp")
    parity = lax.axis_index("dp") % 2
    half = block.shape[0] // 2
    halves = block.reshape((2, half) + block.shape[1:])
    outgoing = jnp.tile(halves, (count // 2,) + (1,) * block.ndim)
    got = lax.all_to_all(outgoing, "dp", split_axis=0, concat_axis=0, tiled=True)
    theirs = lax.ppermute(got, "dp", swap_pairs(count, 1))
    pair = jnp.where(parity == 0, jnp.stack([got, theirs], axis=1), jnp.stack([theirs, got], axis=1))
    return pair.reshape((count * 2 * half,) + block.shape[1:])


def chip_scatter_rows(partial):
    count = lax.axis_size("dp")
    parity = lax.axis_index("dp") % 2
    half = partial.shape[0] // count // 2
    blocks = partial.reshape((count, 2, half) + partial.shape[1:])
    keep = lax.dynamic_index_in_dim(blocks, parity, axis=1, keepdims=False)
    send = lax.dynamic_index_in_dim(blocks, 1 - parity, axis=1, keepdims=False)
    chip_sum = keep + lax.ppermute(send, "dp", swap_pairs(count, 1))
    got = lax.all_to_all(chip_sum, "dp", split_axis=0, concat_axis=0, tiled=True)
    got = got.reshape((count // 2, 2) + got.shape[1:])
    even = jnp.sum(got[:, 0], axis=0)
    odd = jnp.sum(got[:, 1], axis=0)
    return jnp.concatenate([even, odd], axis=0)


def scatter_layer(parts, proj_whole=False):
    qkv_part, proj_part, up_part, down_part = parts
    return (
        chip_scatter_rows(qkv_part),
        (dp_scatter(proj_part, 0) if proj_whole else chip_scatter_rows(proj_part)).T,
        dp_scatter(up_part, 0),
        chip_scatter_rows(down_part).T,
    )


def vector_step(params, gradients):
    return params - vector_rate * gradients * lax.rsqrt(
        jnp.mean(gradients * gradients, axis=-1, keepdims=True) + vector_eps
    )


def local(
    block_input,
    cotangent,
    segments,
    qkv_weight,
    proj_weight,
    up_weight,
    down_weight,
    norm_gains,
    biases,
    qkv_bias,
    up_bias,
    qkv_state,
    proj_state,
    up_state,
    down_state,
):
    tensor_rank = lax.axis_index("tensor")
    local_width = qkv_weight.shape[3]
    local_hidden = up_weight.shape[2]
    head_count = local_width // HD
    model_width = block_input.shape[1]
    segment_row = segments[0]
    cosine_table, sine_table = rotary_tables(segment_row)
    stream = block_input.astype(jnp.float32)
    saved_layers = []
    for layer_id in range(LAYERS):
        layer_weights = (
            dp_gather(qkv_weight[layer_id], 0)
            if layer_id == LAYERS - 1
            else chip_gather_rows(qkv_weight[layer_id]),
            chip_gather_rows(proj_weight[layer_id].T),
            dp_gather(up_weight[layer_id], 0),
            chip_gather_rows(down_weight[layer_id].T),
        )
        qkv_full, proj_full, up_full, down_full = layer_weights
        normed, inverse = normalize(stream)
        attn_rows = (normed * norm_gains[layer_id, 0] + biases[layer_id, 0]).astype(jnp.bfloat16)
        mlp_rows = (normed * norm_gains[layer_id, 1] + biases[layer_id, 1]).astype(jnp.bfloat16)
        both_in = tensor_gather(jnp.concatenate([attn_rows, mlp_rows], axis=1))
        attn_in, mlp_in = both_in[:, :model_width], both_in[:, model_width:]
        length = attn_in.shape[0]
        qkv_local_bias = lax.dynamic_slice_in_dim(
            qkv_bias[layer_id], tensor_rank * local_width, local_width, 1
        )
        qkv_pre = (
            jnp.einsum("ld,dcf->lcf", attn_in, qkv_full, preferred_element_type=jnp.float32)
            + qkv_local_bias
        )
        shaped = qkv_pre.reshape(length, 3, head_count, HD)
        queries = rotate(shaped[:, 0], cosine_table, sine_table).astype(jnp.bfloat16)
        key_rows = rotate(shaped[:, 1], cosine_table, sine_table).astype(jnp.bfloat16)
        values = shaped[:, 2].astype(jnp.bfloat16)
        heads_out, log_sums = attend(queries, key_rows, values, segment_row)
        heads_flat = heads_out.reshape(length, local_width)
        up_local_bias = lax.dynamic_slice_in_dim(
            up_bias[layer_id], tensor_rank * local_hidden, local_hidden, 0
        )
        up_pre = jnp.dot(mlp_in, up_full, preferred_element_type=jnp.float32) + up_local_bias
        act_low = gelu_exact(up_pre).astype(jnp.bfloat16)
        partial_sum = jnp.einsum(
            "lf,df->ld", heads_flat, proj_full, preferred_element_type=jnp.float32
        ) + jnp.einsum("lf,df->ld", act_low, down_full, preferred_element_type=jnp.float32)
        branch = tensor_scatter(partial_sum)
        saved_layers.append(
            (
                normed,
                inverse,
                attn_in,
                mlp_in,
                queries,
                key_rows,
                values,
                log_sums,
                heads_flat,
                up_pre,
                act_low,
                layer_weights,
            )
        )
        stream = stream + branch + biases[layer_id, 2] + biases[layer_id, 3]
    grad_stream = cotangent.astype(jnp.float32)
    gains_list = [None] * LAYERS
    biases_list = [None] * LAYERS
    qkv_bias_list = [None] * LAYERS
    up_bias_list = [None] * LAYERS
    weight_list = [None] * LAYERS
    for layer_id in reversed(range(LAYERS)):
        (
            normed,
            inverse,
            attn_in,
            mlp_in,
            queries,
            key_rows,
            values,
            log_sums,
            heads_flat,
            up_pre,
            act_low,
            layer_weights,
        ) = saved_layers[layer_id]
        qkv_full, proj_full, up_full, down_full = layer_weights
        length = attn_in.shape[0]
        out_bias_grad = jnp.sum(grad_stream, axis=0)
        branch_grad = tensor_gather(grad_stream.astype(jnp.bfloat16))
        down_part = jnp.einsum(
            "lf,ld->df", act_low, branch_grad, preferred_element_type=jnp.float32
        )
        act_grad = jnp.einsum(
            "ld,df->lf", branch_grad, down_full, preferred_element_type=jnp.float32
        )
        gelu_back = jax.vjp(gelu_exact, up_pre)[1]
        up_pre_grad = gelu_back(act_grad)[0].astype(jnp.bfloat16)
        up_bias_part = jnp.sum(up_pre_grad, axis=0, dtype=jnp.float32)
        up_part = jnp.einsum("ld,lf->df", mlp_in, up_pre_grad, preferred_element_type=jnp.float32)
        mlp_in_grad = jnp.einsum(
            "lf,df->ld", up_pre_grad, up_full, preferred_element_type=jnp.float32
        )
        proj_part = jnp.einsum(
            "lf,ld->df", heads_flat, branch_grad, preferred_element_type=jnp.float32
        )
        heads_grad = (
            jnp.einsum("ld,df->lf", branch_grad, proj_full, preferred_element_type=jnp.float32)
            .astype(jnp.bfloat16)
            .reshape(length, head_count, HD)
        )
        query_grad, key_grad, value_grad = attend_back(
            queries, key_rows, values, heads_grad, log_sums, segment_row
        )
        qkv_pre_grad = jnp.stack(
            [
                unrotate(query_grad, cosine_table, sine_table),
                unrotate(key_grad, cosine_table, sine_table),
                value_grad,
            ],
            axis=1,
        )
        qkv_pre_grad = qkv_pre_grad.reshape(length, 3, local_width).astype(jnp.bfloat16)
        qkv_bias_part = jnp.sum(qkv_pre_grad, axis=0, dtype=jnp.float32)
        qkv_part = jnp.einsum(
            "ld,lcf->dcf", attn_in, qkv_pre_grad, preferred_element_type=jnp.float32
        )
        attn_in_grad = jnp.einsum(
            "lcf,dcf->ld", qkv_pre_grad, qkv_full, preferred_element_type=jnp.float32
        )
        both_grad = tensor_scatter(jnp.concatenate([attn_in_grad, mlp_in_grad], axis=1))
        attn_rows_grad, mlp_rows_grad = both_grad[:, :model_width], both_grad[:, model_width:]
        gains_list[layer_id] = jnp.stack(
            [jnp.sum(attn_rows_grad * normed, axis=0), jnp.sum(mlp_rows_grad * normed, axis=0)]
        )
        biases_list[layer_id] = jnp.stack(
            [
                jnp.sum(attn_rows_grad, axis=0),
                jnp.sum(mlp_rows_grad, axis=0),
                out_bias_grad,
                out_bias_grad,
            ]
        )
        qkv_bias_list[layer_id] = lax.dynamic_update_slice_in_dim(
            jnp.zeros((3, model_width), jnp.float32), qkv_bias_part, tensor_rank * local_width, 1
        )
        up_bias_list[layer_id] = lax.dynamic_update_slice_in_dim(
            jnp.zeros((up_bias.shape[1],), jnp.float32), up_bias_part, tensor_rank * local_hidden, 0
        )
        normed_grad = (
            attn_rows_grad * norm_gains[layer_id, 0] + mlp_rows_grad * norm_gains[layer_id, 1]
        )
        normed_mean = jnp.mean(normed_grad, axis=-1, keepdims=True)
        product_mean = jnp.mean(normed_grad * normed, axis=-1, keepdims=True)
        grad_stream = grad_stream + inverse * (normed_grad - normed_mean - normed * product_mean)
        weight_list[layer_id] = (qkv_part, proj_part, up_part, down_part)
        if layer_id > 0:
            weight_list[layer_id] = scatter_layer(weight_list[layer_id], proj_whole=True)
            first_sum, grad_stream = lax.optimization_barrier((weight_list[layer_id][0], grad_stream))
            weight_list[layer_id] = (first_sum,) + weight_list[layer_id][1:]
    small_parts = (
        jnp.stack(gains_list),
        jnp.stack(biases_list),
        jnp.stack(qkv_bias_list),
        jnp.stack(up_bias_list),
    )
    flat = butterfly_sum(jnp.concatenate([part.reshape(-1) for part in small_parts]))
    small_sums = []
    offset = 0
    for part in small_parts:
        small_sums.append(flat[offset : offset + part.size].reshape(part.shape))
        offset += part.size
    gains_grad, biases_grad, qkv_bias_grad, up_bias_grad = small_sums
    flat, first_down = lax.optimization_barrier((flat, weight_list[0][3]))
    weight_list[0] = scatter_layer(weight_list[0][:3] + (first_down,))
    qkv_grad = jnp.stack([weight_list[layer_id][0] for layer_id in range(LAYERS)])
    proj_grad = jnp.stack([weight_list[layer_id][1] for layer_id in range(LAYERS)])
    up_grad = jnp.stack([weight_list[layer_id][2] for layer_id in range(LAYERS)])
    down_grad = jnp.stack([weight_list[layer_id][3] for layer_id in range(LAYERS)])
    qkv_state_new = momentum * qkv_state + qkv_grad
    proj_state_new = momentum * proj_state + proj_grad
    up_state_new = momentum * up_state + up_grad
    down_state_new = momentum * down_state + down_grad
    rows_local = qkv_state.shape[1]
    dp_count = lax.axis_size("dp")
    dp_rank = lax.axis_index("dp")
    slot_count = 4 * LAYERS
    sub = dp_count // slot_count
    piece_width = up_state.shape[2] // sub
    slot_mats = []
    for layer_id in range(LAYERS):
        slot_mats.append(qkv_state_new[layer_id].reshape(rows_local, 3 * local_width))
        slot_mats.append(proj_state_new[layer_id].T)
        slot_mats.append(up_state_new[layer_id])
        slot_mats.append(down_state_new[layer_id].T)
    pieces = []
    for mat in slot_mats:
        width = mat.shape[1] // sub
        split = mat.reshape(rows_local, sub, width).transpose(1, 0, 2)
        pieces.append(jnp.pad(split, ((0, 0), (0, 0), (0, piece_width - width))))
    outgoing = jnp.concatenate(pieces, axis=0)
    owned = lax.all_to_all(outgoing, "dp", split_axis=0, concat_axis=0, tiled=True)
    owned = owned.reshape(dp_count * rows_local, piece_width)
    owned, grad_stream = lax.optimization_barrier((owned, grad_stream))
    gram = jnp.dot(owned, owned.T, precision=ns_precision)
    bit = 1
    while bit < sub:
        gram = gram + lax.ppermute(gram, "dp", swap_pairs(dp_count, bit))
        bit *= 2
    first_core = dp_rank % 2 == 0
    half = gram.shape[0] // 2
    quarter = half // 2
    upper_part = gram[:half, : half + quarter]
    lower_part = jnp.concatenate([gram[:half, half + quarter :], gram[half:, half:]], axis=1)
    mine = jnp.where(first_core, upper_part, lower_part)
    mine = mine + lax.ppermute(mine, "tensor", [(0, 1), (1, 0)])
    other = lax.ppermute(mine, "dp", swap_pairs(dp_count, 1))
    upper_sum = jnp.where(first_core, mine, other)
    lower_sum = jnp.where(first_core, other, mine)
    corner = jnp.concatenate([upper_sum[:, half:], lower_sum[:, :quarter]], axis=1)
    gram = jnp.concatenate(
        [
            jnp.concatenate([upper_sum[:, :half], corner], axis=1),
            jnp.concatenate([corner.T, lower_sum[:, quarter:]], axis=1),
        ],
        axis=0,
    )
    norm_sq = jnp.trace(gram)
    scale = 1.0 / (jnp.sqrt(norm_sq) + frobenius_eps)
    current_gram = gram * (scale * scale)
    identity = jnp.eye(current_gram.shape[0], dtype=jnp.float32)
    accumulated = None
    for iteration in range(NS_ITERS):
        squared = jnp.dot(current_gram, current_gram, precision=ns_precision)
        polynomial = coef_first * identity + coef_second * current_gram + coef_third * squared
        if accumulated is None:
            accumulated = polynomial
        else:
            accumulated = jnp.dot(polynomial, accumulated, precision=ns_precision)
        if iteration + 1 < NS_ITERS:
            current_gram = jnp.dot(
                polynomial,
                jnp.dot(current_gram, polynomial, precision=ns_precision),
                precision=ns_precision,
            )
    current = jnp.dot(accumulated, owned * scale, precision=ns_precision)
    returned = lax.all_to_all(
        current.astype(jnp.bfloat16).reshape(dp_count, rows_local, piece_width),
        "dp",
        split_axis=0,
        concat_axis=0,
        tiled=True,
    ).reshape(slot_count, sub, rows_local, piece_width)
    my_rows = []
    for slot_id, mat in enumerate(slot_mats):
        width = mat.shape[1] // sub
        my_rows.append(
            returned[slot_id, :, :, :width]
            .astype(jnp.float32)
            .transpose(1, 0, 2)
            .reshape(rows_local, sub * width)
        )
    muon_step = muon_rate * match_rms
    qkv_list, proj_list, up_list, down_list = ([], [], [], [])
    for layer_id in range(LAYERS):
        base_slot = 4 * layer_id
        qkv_ortho = my_rows[base_slot].reshape(rows_local, 3, local_width)
        proj_ortho = my_rows[base_slot + 1].T
        up_ortho = my_rows[base_slot + 2]
        down_ortho = my_rows[base_slot + 3].T
        qkv_list.append(
            qkv_weight[layer_id].astype(jnp.float32) - muon_step * math.sqrt(3 * D) * qkv_ortho
        )
        proj_list.append(
            proj_weight[layer_id].astype(jnp.float32) - muon_step * math.sqrt(D) * proj_ortho
        )
        up_list.append(
            up_weight[layer_id].astype(jnp.float32) - muon_step * math.sqrt(FF) * up_ortho
        )
        down_list.append(
            down_weight[layer_id].astype(jnp.float32) - muon_step * math.sqrt(FF) * down_ortho
        )
    qkv_new = jnp.stack(qkv_list)
    proj_new = jnp.stack(proj_list)
    up_new = jnp.stack(up_list)
    down_new = jnp.stack(down_list)
    gains_new = vector_step(norm_gains, gains_grad)
    biases_new = vector_step(biases, biases_grad)
    qkv_bias_new = vector_step(qkv_bias, qkv_bias_grad)
    up_bias_new = vector_step(up_bias, up_bias_grad)
    return (
        stream,
        grad_stream,
        qkv_grad,
        proj_grad,
        up_grad,
        down_grad,
        gains_grad,
        biases_grad,
        qkv_bias_grad,
        up_bias_grad,
        qkv_new,
        proj_new,
        up_new,
        down_new,
        gains_new,
        biases_new,
        qkv_bias_new,
        up_bias_new,
        qkv_state_new,
        proj_state_new,
        up_state_new,
        down_state_new,
    )


def solution(mesh):
    return jax.shard_map(
        local,
        mesh=mesh,
        in_specs=(
            P(("dp", "tensor"), None),
            P(("dp", "tensor"), None),
            P("dp", None),
            P(None, "dp", None, "tensor"),
            P(None, "tensor", "dp"),
            P(None, "dp", "tensor"),
            P(None, "tensor", "dp"),
            P(),
            P(),
            P(),
            P(),
            P(None, "dp", None, "tensor"),
            P(None, "tensor", "dp"),
            P(None, "dp", "tensor"),
            P(None, "tensor", "dp"),
        ),
        out_specs=(
            P(("dp", "tensor"), None),
            P(("dp", "tensor"), None),
            P(None, "dp", None, "tensor"),
            P(None, "tensor", "dp"),
            P(None, "dp", "tensor"),
            P(None, "tensor", "dp"),
            P(),
            P(),
            P(),
            P(),
            P(None, "dp", None, "tensor"),
            P(None, "tensor", "dp"),
            P(None, "dp", "tensor"),
            P(None, "tensor", "dp"),
            P(),
            P(),
            P(),
            P(),
            P(None, "dp", None, "tensor"),
            P(None, "tensor", "dp"),
            P(None, "dp", "tensor"),
            P(None, "tensor", "dp"),
        ),
        check_vma=False,
    )
```

```python
import math

import jax
import jax.numpy as jnp
from jax import lax
from jax.sharding import PartitionSpec as P

D = 768
HD = 64
FF = 3072
ROT = 16
LAYERS = 2
NS_ITERS = 5


highest = lax.Precision.HIGHEST
ns_precision = lax.Precision.HIGH
norm_eps = 1e-05
masked_score = -1e30
coef_first = 3.4445
coef_second = -4.775
coef_third = 2.0315
momentum = 0.9
muon_rate = 0.2
match_rms = 0.2
vector_rate = 0.2
vector_eps = 1e-06
frobenius_eps = 1e-07


def rotary_tables(segment_row):
    length = segment_row.shape[0]
    indices = jnp.arange(length, dtype=jnp.int32)
    change = jnp.concatenate([jnp.ones((1,), dtype=bool), segment_row[1:] != segment_row[:-1]])
    starts = lax.cummax(jnp.where(change, indices, jnp.zeros_like(indices)), axis=0)
    positions = (indices - starts).astype(jnp.float32)
    half_rot = ROT // 2
    frequency = 10000.0 ** (-2.0 * jnp.arange(half_rot, dtype=jnp.float32) / ROT)
    angles = positions[:, None] * frequency[None, :]
    return (jnp.cos(angles), jnp.sin(angles))


def rotate(values, cosine_table, sine_table):
    half_rot = ROT // 2
    first_half = values[..., :half_rot]
    second_half = values[..., half_rot:ROT]
    cos_b = cosine_table[:, None, :]
    sin_b = sine_table[:, None, :]
    return jnp.concatenate(
        [
            first_half * cos_b - second_half * sin_b,
            second_half * cos_b + first_half * sin_b,
            values[..., ROT:],
        ],
        axis=-1,
    )


def unrotate(gradient, cosine_table, sine_table):
    half_rot = ROT // 2
    first_half = gradient[..., :half_rot]
    second_half = gradient[..., half_rot:ROT]
    cos_b = cosine_table[:, None, :]
    sin_b = sine_table[:, None, :]
    return jnp.concatenate(
        [
            first_half * cos_b + second_half * sin_b,
            second_half * cos_b - first_half * sin_b,
            gradient[..., ROT:],
        ],
        axis=-1,
    )


def normalize(stream):
    centered = stream - jnp.mean(stream, axis=-1, keepdims=True)
    inverse = lax.rsqrt(jnp.mean(centered * centered, axis=-1, keepdims=True) + norm_eps)
    return (centered * inverse, inverse)


def gelu_exact(values):
    return jax.nn.gelu(values, approximate=False)


def block_mask(segment_row, block_rows):
    query_pos = jnp.arange(block_rows, dtype=jnp.int32)
    key_pos = jnp.arange(segment_row.shape[0], dtype=jnp.int32)
    return (segment_row[:, None] == segment_row[None, :]) & (query_pos[:, None] >= key_pos[None, :])


def block_scores(queries, key_rows, allowed):
    scores = jnp.einsum(
        "qhe,khe->hqk", queries, key_rows, preferred_element_type=jnp.float32
    ) * queries.shape[-1] ** (-0.5)
    return jnp.where(allowed[None], scores, masked_score)


def attend(queries, key_rows, values, segment_row):
    length = queries.shape[0]
    block_rows = min(512, length)
    allowed = block_mask(segment_row, block_rows)
    scores = block_scores(queries, key_rows, allowed)
    row_peak = jnp.max(scores, axis=-1, keepdims=True)
    exponent = jnp.exp(scores - row_peak)
    row_total = jnp.sum(exponent, axis=-1, keepdims=True)
    probs_low = (exponent / row_total).astype(jnp.bfloat16)
    outputs = jnp.einsum(
        "hqk,khe->qhe", probs_low, values, preferred_element_type=jnp.float32
    ).astype(jnp.bfloat16)
    log_sums = row_peak + jnp.log(row_total)
    return (outputs, log_sums)


def attend_back(queries, key_rows, values, heads_grad, log_sums, segment_row):
    length = queries.shape[0]
    block_rows = min(512, length)
    scale_factor = queries.shape[-1] ** (-0.5)
    allowed = block_mask(segment_row, block_rows)
    scores = block_scores(queries, key_rows, allowed)
    probs_full = jnp.exp(scores - log_sums)
    probs_grad = jnp.einsum("qhe,khe->hqk", heads_grad, values, preferred_element_type=jnp.float32)
    row_dot = jnp.sum(probs_full * probs_grad, axis=-1, keepdims=True)
    score_grad = (probs_full * (probs_grad - row_dot)).astype(jnp.bfloat16)
    value_grad = jnp.einsum(
        "hqk,qhe->khe",
        probs_full.astype(jnp.bfloat16),
        heads_grad,
        preferred_element_type=jnp.float32,
    )
    query_grads = (
        jnp.einsum("hqk,khe->qhe", score_grad, key_rows, preferred_element_type=jnp.float32)
        * scale_factor
    )
    key_grad = (
        jnp.einsum("hqk,qhe->khe", score_grad, queries, preferred_element_type=jnp.float32)
        * scale_factor
    )
    return (query_grads, key_grad, value_grad)


def dp_scatter(partial, dimension):
    return lax.psum_scatter(partial, "dp", scatter_dimension=dimension, tiled=True)


def dp_gather(block, axis):
    return lax.all_gather(block, "dp", axis=axis, tiled=True)


def swap_pairs(count, bit):
    return [(i, i ^ bit) for i in range(count)]


def butterfly_sum(flat):
    count = lax.axis_size("dp")
    bit = 1
    while bit < count:
        flat = flat + lax.ppermute(flat, "dp", swap_pairs(count, bit))
        bit *= 2
    return flat + lax.ppermute(flat, "tensor", [(0, 1), (1, 0)])


def tensor_swap(block):
    return lax.ppermute(block, "tensor", [(0, 1), (1, 0)])


def tensor_gather(block):
    other = tensor_swap(block)
    first = lax.axis_index("tensor") == 0
    return jnp.where(
        first, jnp.concatenate([block, other], axis=0), jnp.concatenate([other, block], axis=0)
    )


def tensor_scatter(partial):
    rank = lax.axis_index("tensor")
    half = partial.shape[0] // 2
    mine = lax.dynamic_slice_in_dim(partial, rank * half, half, 0)
    theirs = lax.dynamic_slice_in_dim(partial, (1 - rank) * half, half, 0)
    return mine + tensor_swap(theirs)


def chip_gather_rows(block):
    count = lax.axis_size("dp")
    parity = lax.axis_index("dp") % 2
    half = block.shape[0] // 2
    halves = block.reshape((2, half) + block.shape[1:])
    outgoing = jnp.tile(halves, (count // 2,) + (1,) * block.ndim)
    got = lax.all_to_all(outgoing, "dp", split_axis=0, concat_axis=0, tiled=True)
    theirs = lax.ppermute(got, "dp", swap_pairs(count, 1))
    pair = jnp.where(parity == 0, jnp.stack([got, theirs], axis=1), jnp.stack([theirs, got], axis=1))
    return pair.reshape((count * 2 * half,) + block.shape[1:])


def chip_scatter_rows(partial):
    count = lax.axis_size("dp")
    parity = lax.axis_index("dp") % 2
    half = partial.shape[0] // count // 2
    blocks = partial.reshape((count, 2, half) + partial.shape[1:])
    keep = lax.dynamic_index_in_dim(blocks, parity, axis=1, keepdims=False)
    send = lax.dynamic_index_in_dim(blocks, 1 - parity, axis=1, keepdims=False)
    chip_sum = keep + lax.ppermute(send, "dp", swap_pairs(count, 1))
    got = lax.all_to_all(chip_sum, "dp", split_axis=0, concat_axis=0, tiled=True)
    got = got.reshape((count // 2, 2) + got.shape[1:])
    even = jnp.sum(got[:, 0], axis=0)
    odd = jnp.sum(got[:, 1], axis=0)
    return jnp.concatenate([even, odd], axis=0)


def scatter_layer(parts, proj_whole=False):
    qkv_part, proj_part, up_part, down_part = parts
    return (
        chip_scatter_rows(qkv_part),
        (dp_scatter(proj_part, 0) if proj_whole else chip_scatter_rows(proj_part)).T,
        dp_scatter(up_part, 0),
        chip_scatter_rows(down_part).T,
    )


def vector_step(params, gradients):
    return params - vector_rate * gradients * lax.rsqrt(
        jnp.mean(gradients * gradients, axis=-1, keepdims=True) + vector_eps
    )


def local(
    block_input,
    cotangent,
    segments,
    qkv_weight,
    proj_weight,
    up_weight,
    down_weight,
    norm_gains,
    biases,
    qkv_bias,
    up_bias,
    qkv_state,
    proj_state,
    up_state,
    down_state,
):
    tensor_rank = lax.axis_index("tensor")
    local_width = qkv_weight.shape[3]
    local_hidden = up_weight.shape[2]
    head_count = local_width // HD
    model_width = block_input.shape[1]
    segment_row = segments[0]
    cosine_table, sine_table = rotary_tables(segment_row)
    stream = block_input.astype(jnp.float32)
    saved_layers = []
    for layer_id in range(LAYERS):
        down_full = chip_gather_rows(down_weight[layer_id].T)
        proj_block = proj_weight[layer_id].T
        if layer_id == LAYERS - 1:
            proj_block, down_full = lax.optimization_barrier((proj_block, down_full))
        layer_weights = (
            dp_gather(qkv_weight[layer_id], 0)
            if layer_id == LAYERS - 1
            else chip_gather_rows(qkv_weight[layer_id]),
            chip_gather_rows(proj_block),
            dp_gather(up_weight[layer_id], 0),
            down_full,
        )
        qkv_full, proj_full, up_full, down_full = layer_weights
        normed, inverse = normalize(stream)
        attn_rows = (normed * norm_gains[layer_id, 0] + biases[layer_id, 0]).astype(jnp.bfloat16)
        mlp_rows = (normed * norm_gains[layer_id, 1] + biases[layer_id, 1]).astype(jnp.bfloat16)
        both_in = tensor_gather(jnp.concatenate([attn_rows, mlp_rows], axis=1))
        attn_in, mlp_in = both_in[:, :model_width], both_in[:, model_width:]
        length = attn_in.shape[0]
        qkv_local_bias = lax.dynamic_slice_in_dim(
            qkv_bias[layer_id], tensor_rank * local_width, local_width, 1
        )
        qkv_pre = (
            jnp.einsum("ld,dcf->lcf", attn_in, qkv_full, preferred_element_type=jnp.float32)
            + qkv_local_bias
        )
        shaped = qkv_pre.reshape(length, 3, head_count, HD)
        queries = rotate(shaped[:, 0], cosine_table, sine_table).astype(jnp.bfloat16)
        key_rows = rotate(shaped[:, 1], cosine_table, sine_table).astype(jnp.bfloat16)
        values = shaped[:, 2].astype(jnp.bfloat16)
        heads_out, log_sums = attend(queries, key_rows, values, segment_row)
        heads_flat = heads_out.reshape(length, local_width)
        up_local_bias = lax.dynamic_slice_in_dim(
            up_bias[layer_id], tensor_rank * local_hidden, local_hidden, 0
        )
        up_pre = jnp.dot(mlp_in, up_full, preferred_element_type=jnp.float32) + up_local_bias
        act_low = gelu_exact(up_pre).astype(jnp.bfloat16)
        partial_sum = jnp.einsum(
            "lf,df->ld", heads_flat, proj_full, preferred_element_type=jnp.float32
        ) + jnp.einsum("lf,df->ld", act_low, down_full, preferred_element_type=jnp.float32)
        branch = tensor_scatter(partial_sum)
        saved_layers.append(
            (
                normed,
                inverse,
                attn_in,
                mlp_in,
                queries,
                key_rows,
                values,
                log_sums,
                heads_flat,
                up_pre,
                act_low,
                layer_weights,
            )
        )
        stream = stream + branch + biases[layer_id, 2] + biases[layer_id, 3]
    grad_stream = cotangent.astype(jnp.float32)
    gains_list = [None] * LAYERS
    biases_list = [None] * LAYERS
    qkv_bias_list = [None] * LAYERS
    up_bias_list = [None] * LAYERS
    weight_list = [None] * LAYERS
    for layer_id in reversed(range(LAYERS)):
        (
            normed,
            inverse,
            attn_in,
            mlp_in,
            queries,
            key_rows,
            values,
            log_sums,
            heads_flat,
            up_pre,
            act_low,
            layer_weights,
        ) = saved_layers[layer_id]
        qkv_full, proj_full, up_full, down_full = layer_weights
        length = attn_in.shape[0]
        out_bias_grad = jnp.sum(grad_stream, axis=0)
        branch_grad = tensor_gather(grad_stream.astype(jnp.bfloat16))
        down_part = jnp.einsum(
            "lf,ld->df", act_low, branch_grad, preferred_element_type=jnp.float32
        )
        act_grad = jnp.einsum(
            "ld,df->lf", branch_grad, down_full, preferred_element_type=jnp.float32
        )
        gelu_back = jax.vjp(gelu_exact, up_pre)[1]
        up_pre_grad = gelu_back(act_grad)[0].astype(jnp.bfloat16)
        up_bias_part = jnp.sum(up_pre_grad, axis=0, dtype=jnp.float32)
        up_part = jnp.einsum("ld,lf->df", mlp_in, up_pre_grad, preferred_element_type=jnp.float32)
        mlp_in_grad = jnp.einsum(
            "lf,df->ld", up_pre_grad, up_full, preferred_element_type=jnp.float32
        )
        proj_part = jnp.einsum(
            "lf,ld->df", heads_flat, branch_grad, preferred_element_type=jnp.float32
        )
        heads_grad = (
            jnp.einsum("ld,df->lf", branch_grad, proj_full, preferred_element_type=jnp.float32)
            .astype(jnp.bfloat16)
            .reshape(length, head_count, HD)
        )
        query_grad, key_grad, value_grad = attend_back(
            queries, key_rows, values, heads_grad, log_sums, segment_row
        )
        qkv_pre_grad = jnp.stack(
            [
                unrotate(query_grad, cosine_table, sine_table),
                unrotate(key_grad, cosine_table, sine_table),
                value_grad,
            ],
            axis=1,
        )
        qkv_pre_grad = qkv_pre_grad.reshape(length, 3, local_width).astype(jnp.bfloat16)
        qkv_bias_part = jnp.sum(qkv_pre_grad, axis=0, dtype=jnp.float32)
        qkv_part = jnp.einsum(
            "ld,lcf->dcf", attn_in, qkv_pre_grad, preferred_element_type=jnp.float32
        )
        attn_in_grad = jnp.einsum(
            "lcf,dcf->ld", qkv_pre_grad, qkv_full, preferred_element_type=jnp.float32
        )
        both_grad = tensor_scatter(jnp.concatenate([attn_in_grad, mlp_in_grad], axis=1))
        attn_rows_grad, mlp_rows_grad = both_grad[:, :model_width], both_grad[:, model_width:]
        gains_list[layer_id] = jnp.stack(
            [jnp.sum(attn_rows_grad * normed, axis=0), jnp.sum(mlp_rows_grad * normed, axis=0)]
        )
        biases_list[layer_id] = jnp.stack(
            [
                jnp.sum(attn_rows_grad, axis=0),
                jnp.sum(mlp_rows_grad, axis=0),
                out_bias_grad,
                out_bias_grad,
            ]
        )
        qkv_bias_list[layer_id] = lax.dynamic_update_slice_in_dim(
            jnp.zeros((3, model_width), jnp.float32), qkv_bias_part, tensor_rank * local_width, 1
        )
        up_bias_list[layer_id] = lax.dynamic_update_slice_in_dim(
            jnp.zeros((up_bias.shape[1],), jnp.float32), up_bias_part, tensor_rank * local_hidden, 0
        )
        normed_grad = (
            attn_rows_grad * norm_gains[layer_id, 0] + mlp_rows_grad * norm_gains[layer_id, 1]
        )
        normed_mean = jnp.mean(normed_grad, axis=-1, keepdims=True)
        product_mean = jnp.mean(normed_grad * normed, axis=-1, keepdims=True)
        grad_stream = grad_stream + inverse * (normed_grad - normed_mean - normed * product_mean)
        weight_list[layer_id] = (qkv_part, proj_part, up_part, down_part)
        if layer_id > 0:
            weight_list[layer_id] = scatter_layer(weight_list[layer_id], proj_whole=True)
            first_sum, grad_stream = lax.optimization_barrier((weight_list[layer_id][0], grad_stream))
            weight_list[layer_id] = (first_sum,) + weight_list[layer_id][1:]
    small_parts = (
        jnp.stack(gains_list),
        jnp.stack(biases_list),
        jnp.stack(qkv_bias_list),
        jnp.stack(up_bias_list),
    )
    flat = butterfly_sum(jnp.concatenate([part.reshape(-1) for part in small_parts]))
    small_sums = []
    offset = 0
    for part in small_parts:
        small_sums.append(flat[offset : offset + part.size].reshape(part.shape))
        offset += part.size
    gains_grad, biases_grad, qkv_bias_grad, up_bias_grad = small_sums
    flat, first_down = lax.optimization_barrier((flat, weight_list[0][3]))
    weight_list[0] = scatter_layer(weight_list[0][:3] + (first_down,))
    qkv_grad = jnp.stack([weight_list[layer_id][0] for layer_id in range(LAYERS)])
    proj_grad = jnp.stack([weight_list[layer_id][1] for layer_id in range(LAYERS)])
    up_grad = jnp.stack([weight_list[layer_id][2] for layer_id in range(LAYERS)])
    down_grad = jnp.stack([weight_list[layer_id][3] for layer_id in range(LAYERS)])
    qkv_state_new = momentum * qkv_state + qkv_grad
    proj_state_new = momentum * proj_state + proj_grad
    up_state_new = momentum * up_state + up_grad
    down_state_new = momentum * down_state + down_grad
    rows_local = qkv_state.shape[1]
    dp_count = lax.axis_size("dp")
    dp_rank = lax.axis_index("dp")
    slot_count = 4 * LAYERS
    sub = dp_count // slot_count
    piece_width = up_state.shape[2] // sub
    slot_mats = []
    for layer_id in range(LAYERS):
        slot_mats.append(qkv_state_new[layer_id].reshape(rows_local, 3 * local_width))
        slot_mats.append(proj_state_new[layer_id].T)
        slot_mats.append(up_state_new[layer_id])
        slot_mats.append(down_state_new[layer_id].T)
    pieces = []
    for mat in slot_mats:
        width = mat.shape[1] // sub
        split = mat.reshape(rows_local, sub, width).transpose(1, 0, 2)
        pieces.append(jnp.pad(split, ((0, 0), (0, 0), (0, piece_width - width))))
    outgoing = jnp.concatenate(pieces, axis=0)
    owned = lax.all_to_all(outgoing, "dp", split_axis=0, concat_axis=0, tiled=True)
    owned = owned.reshape(dp_count * rows_local, piece_width)
    owned, grad_stream = lax.optimization_barrier((owned, grad_stream))
    gram = jnp.dot(owned, owned.T, precision=ns_precision)
    bit = 1
    while bit < sub:
        gram = gram + lax.ppermute(gram, "dp", swap_pairs(dp_count, bit))
        bit *= 2
    core_half = dp_rank % 2
    half_rows = gram.shape[0] // 2
    mine = lax.dynamic_slice_in_dim(gram, core_half * half_rows, half_rows, 0)
    mine = mine + lax.ppermute(mine, "tensor", [(0, 1), (1, 0)])
    other = lax.ppermute(mine, "dp", swap_pairs(dp_count, 1))
    gram = jnp.where(
        core_half == 0,
        jnp.concatenate([mine, other], axis=0),
        jnp.concatenate([other, mine], axis=0),
    )
    norm_sq = jnp.trace(gram)
    scale = 1.0 / (jnp.sqrt(norm_sq) + frobenius_eps)
    current_gram = gram * (scale * scale)
    identity = jnp.eye(current_gram.shape[0], dtype=jnp.float32)
    accumulated = None
    for iteration in range(NS_ITERS):
        squared = jnp.dot(current_gram, current_gram, precision=ns_precision)
        polynomial = coef_first * identity + coef_second * current_gram + coef_third * squared
        if accumulated is None:
            accumulated = polynomial
        else:
            accumulated = jnp.dot(polynomial, accumulated, precision=ns_precision)
        if iteration + 1 < NS_ITERS:
            current_gram = jnp.dot(
                polynomial,
                jnp.dot(current_gram, polynomial, precision=ns_precision),
                precision=ns_precision,
            )
    current = jnp.dot(accumulated, owned * scale, precision=ns_precision)
    returned = lax.all_to_all(
        current.astype(jnp.bfloat16).reshape(dp_count, rows_local, piece_width),
        "dp",
        split_axis=0,
        concat_axis=0,
        tiled=True,
    ).reshape(slot_count, sub, rows_local, piece_width)
    my_rows = []
    for slot_id, mat in enumerate(slot_mats):
        width = mat.shape[1] // sub
        my_rows.append(
            returned[slot_id, :, :, :width]
            .astype(jnp.float32)
            .transpose(1, 0, 2)
            .reshape(rows_local, sub * width)
        )
    muon_step = muon_rate * match_rms
    qkv_list, proj_list, up_list, down_list = ([], [], [], [])
    for layer_id in range(LAYERS):
        base_slot = 4 * layer_id
        qkv_ortho = my_rows[base_slot].reshape(rows_local, 3, local_width)
        proj_ortho = my_rows[base_slot + 1].T
        up_ortho = my_rows[base_slot + 2]
        down_ortho = my_rows[base_slot + 3].T
        qkv_list.append(
            qkv_weight[layer_id].astype(jnp.float32) - muon_step * math.sqrt(3 * D) * qkv_ortho
        )
        proj_list.append(
            proj_weight[layer_id].astype(jnp.float32) - muon_step * math.sqrt(D) * proj_ortho
        )
        up_list.append(
            up_weight[layer_id].astype(jnp.float32) - muon_step * math.sqrt(FF) * up_ortho
        )
        down_list.append(
            down_weight[layer_id].astype(jnp.float32) - muon_step * math.sqrt(FF) * down_ortho
        )
    qkv_new = jnp.stack(qkv_list)
    proj_new = jnp.stack(proj_list)
    up_new = jnp.stack(up_list)
    down_new = jnp.stack(down_list)
    gains_new = vector_step(norm_gains, gains_grad)
    biases_new = vector_step(biases, biases_grad)
    qkv_bias_new = vector_step(qkv_bias, qkv_bias_grad)
    up_bias_new = vector_step(up_bias, up_bias_grad)
    return (
        stream,
        grad_stream,
        qkv_grad,
        proj_grad,
        up_grad,
        down_grad,
        gains_grad,
        biases_grad,
        qkv_bias_grad,
        up_bias_grad,
        qkv_new,
        proj_new,
        up_new,
        down_new,
        gains_new,
        biases_new,
        qkv_bias_new,
        up_bias_new,
        qkv_state_new,
        proj_state_new,
        up_state_new,
        down_state_new,
    )


def solution(mesh):
    return jax.shard_map(
        local,
        mesh=mesh,
        in_specs=(
            P(("dp", "tensor"), None),
            P(("dp", "tensor"), None),
            P("dp", None),
            P(None, "dp", None, "tensor"),
            P(None, "tensor", "dp"),
            P(None, "dp", "tensor"),
            P(None, "tensor", "dp"),
            P(),
            P(),
            P(),
            P(),
            P(None, "dp", None, "tensor"),
            P(None, "tensor", "dp"),
            P(None, "dp", "tensor"),
            P(None, "tensor", "dp"),
        ),
        out_specs=(
            P(("dp", "tensor"), None),
            P(("dp", "tensor"), None),
            P(None, "dp", None, "tensor"),
            P(None, "tensor", "dp"),
            P(None, "dp", "tensor"),
            P(None, "tensor", "dp"),
            P(),
            P(),
            P(),
            P(),
            P(None, "dp", None, "tensor"),
            P(None, "tensor", "dp"),
            P(None, "dp", "tensor"),
            P(None, "tensor", "dp"),
            P(),
            P(),
            P(),
            P(),
            P(None, "dp", None, "tensor"),
            P(None, "tensor", "dp"),
            P(None, "dp", "tensor"),
            P(None, "tensor", "dp"),
        ),
        check_vma=False,
    )
```

```python
import math

import jax
import jax.numpy as jnp
from jax import lax
from jax.sharding import PartitionSpec as P

D = 768
HD = 64
FF = 3072
ROT = 16
LAYERS = 2
NS_ITERS = 5


highest = lax.Precision.HIGHEST
ns_precision = lax.Precision.HIGH
norm_eps = 1e-05
masked_score = -1e30
coef_first = 3.4445
coef_second = -4.775
coef_third = 2.0315
momentum = 0.9
muon_rate = 0.2
match_rms = 0.2
vector_rate = 0.2
vector_eps = 1e-06
frobenius_eps = 1e-07


def rotary_tables(segment_row):
    length = segment_row.shape[0]
    indices = jnp.arange(length, dtype=jnp.int32)
    change = jnp.concatenate([jnp.ones((1,), dtype=bool), segment_row[1:] != segment_row[:-1]])
    starts = lax.cummax(jnp.where(change, indices, jnp.zeros_like(indices)), axis=0)
    positions = (indices - starts).astype(jnp.float32)
    half_rot = ROT // 2
    frequency = 10000.0 ** (-2.0 * jnp.arange(half_rot, dtype=jnp.float32) / ROT)
    angles = positions[:, None] * frequency[None, :]
    return (jnp.cos(angles), jnp.sin(angles))


def rotate(values, cosine_table, sine_table):
    half_rot = ROT // 2
    first_half = values[..., :half_rot]
    second_half = values[..., half_rot:ROT]
    cos_b = cosine_table[:, None, :]
    sin_b = sine_table[:, None, :]
    return jnp.concatenate(
        [
            first_half * cos_b - second_half * sin_b,
            second_half * cos_b + first_half * sin_b,
            values[..., ROT:],
        ],
        axis=-1,
    )


def unrotate(gradient, cosine_table, sine_table):
    half_rot = ROT // 2
    first_half = gradient[..., :half_rot]
    second_half = gradient[..., half_rot:ROT]
    cos_b = cosine_table[:, None, :]
    sin_b = sine_table[:, None, :]
    return jnp.concatenate(
        [
            first_half * cos_b + second_half * sin_b,
            second_half * cos_b - first_half * sin_b,
            gradient[..., ROT:],
        ],
        axis=-1,
    )


def normalize(stream):
    centered = stream - jnp.mean(stream, axis=-1, keepdims=True)
    inverse = lax.rsqrt(jnp.mean(centered * centered, axis=-1, keepdims=True) + norm_eps)
    return (centered * inverse, inverse)


def gelu_exact(values):
    return jax.nn.gelu(values, approximate=False)


def block_mask(segment_row, block_rows):
    query_pos = jnp.arange(block_rows, dtype=jnp.int32)
    key_pos = jnp.arange(segment_row.shape[0], dtype=jnp.int32)
    return (segment_row[:, None] == segment_row[None, :]) & (query_pos[:, None] >= key_pos[None, :])


def block_scores(queries, key_rows, allowed):
    scores = jnp.einsum(
        "qhe,khe->hqk", queries, key_rows, preferred_element_type=jnp.float32
    ) * queries.shape[-1] ** (-0.5)
    return jnp.where(allowed[None], scores, masked_score)


def attend(queries, key_rows, values, segment_row):
    length = queries.shape[0]
    block_rows = min(512, length)
    allowed = block_mask(segment_row, block_rows)
    scores = block_scores(queries, key_rows, allowed)
    row_peak = jnp.max(scores, axis=-1, keepdims=True)
    exponent = jnp.exp(scores - row_peak)
    row_total = jnp.sum(exponent, axis=-1, keepdims=True)
    probs_low = (exponent / row_total).astype(jnp.bfloat16)
    outputs = jnp.einsum(
        "hqk,khe->qhe", probs_low, values, preferred_element_type=jnp.float32
    ).astype(jnp.bfloat16)
    log_sums = row_peak + jnp.log(row_total)
    return (outputs, log_sums)


def attend_back(queries, key_rows, values, heads_grad, log_sums, segment_row):
    length = queries.shape[0]
    block_rows = min(512, length)
    scale_factor = queries.shape[-1] ** (-0.5)
    allowed = block_mask(segment_row, block_rows)
    scores = block_scores(queries, key_rows, allowed)
    probs_full = jnp.exp(scores - log_sums)
    probs_grad = jnp.einsum("qhe,khe->hqk", heads_grad, values, preferred_element_type=jnp.float32)
    row_dot = jnp.sum(probs_full * probs_grad, axis=-1, keepdims=True)
    score_grad = (probs_full * (probs_grad - row_dot)).astype(jnp.bfloat16)
    value_grad = jnp.einsum(
        "hqk,qhe->khe",
        probs_full.astype(jnp.bfloat16),
        heads_grad,
        preferred_element_type=jnp.float32,
    )
    query_grads = (
        jnp.einsum("hqk,khe->qhe", score_grad, key_rows, preferred_element_type=jnp.float32)
        * scale_factor
    )
    key_grad = (
        jnp.einsum("hqk,qhe->khe", score_grad, queries, preferred_element_type=jnp.float32)
        * scale_factor
    )
    return (query_grads, key_grad, value_grad)


def dp_scatter(partial, dimension):
    return lax.psum_scatter(partial, "dp", scatter_dimension=dimension, tiled=True)


def dp_gather(block, axis):
    return lax.all_gather(block, "dp", axis=axis, tiled=True)


def swap_pairs(count, bit):
    return [(i, i ^ bit) for i in range(count)]


def butterfly_sum(flat):
    count = lax.axis_size("dp")
    bit = 1
    while bit < count:
        flat = flat + lax.ppermute(flat, "dp", swap_pairs(count, bit))
        bit *= 2
    return flat + lax.ppermute(flat, "tensor", [(0, 1), (1, 0)])


def tensor_swap(block):
    return lax.ppermute(block, "tensor", [(0, 1), (1, 0)])


def tensor_gather(block):
    other = tensor_swap(block)
    first = lax.axis_index("tensor") == 0
    return jnp.where(
        first, jnp.concatenate([block, other], axis=0), jnp.concatenate([other, block], axis=0)
    )


def tensor_scatter(partial):
    rank = lax.axis_index("tensor")
    half = partial.shape[0] // 2
    mine = lax.dynamic_slice_in_dim(partial, rank * half, half, 0)
    theirs = lax.dynamic_slice_in_dim(partial, (1 - rank) * half, half, 0)
    return mine + tensor_swap(theirs)


def chip_gather_rows(block):
    count = lax.axis_size("dp")
    parity = lax.axis_index("dp") % 2
    half = block.shape[0] // 2
    halves = block.reshape((2, half) + block.shape[1:])
    outgoing = jnp.tile(halves, (count // 2,) + (1,) * block.ndim)
    got = lax.all_to_all(outgoing, "dp", split_axis=0, concat_axis=0, tiled=True)
    theirs = lax.ppermute(got, "dp", swap_pairs(count, 1))
    pair = jnp.where(parity == 0, jnp.stack([got, theirs], axis=1), jnp.stack([theirs, got], axis=1))
    return pair.reshape((count * 2 * half,) + block.shape[1:])


def chip_scatter_rows(partial):
    count = lax.axis_size("dp")
    parity = lax.axis_index("dp") % 2
    half = partial.shape[0] // count // 2
    blocks = partial.reshape((count, 2, half) + partial.shape[1:])
    keep = lax.dynamic_index_in_dim(blocks, parity, axis=1, keepdims=False)
    send = lax.dynamic_index_in_dim(blocks, 1 - parity, axis=1, keepdims=False)
    chip_sum = keep + lax.ppermute(send, "dp", swap_pairs(count, 1))
    got = lax.all_to_all(chip_sum, "dp", split_axis=0, concat_axis=0, tiled=True)
    got = got.reshape((count // 2, 2) + got.shape[1:])
    even = jnp.sum(got[:, 0], axis=0)
    odd = jnp.sum(got[:, 1], axis=0)
    return jnp.concatenate([even, odd], axis=0)


def scatter_layer(parts, proj_whole=False):
    qkv_part, proj_part, up_part, down_part = parts
    return (
        chip_scatter_rows(qkv_part),
        (dp_scatter(proj_part, 0) if proj_whole else chip_scatter_rows(proj_part)).T,
        dp_scatter(up_part, 0),
        chip_scatter_rows(down_part).T,
    )


def vector_step(params, gradients):
    return params - vector_rate * gradients * lax.rsqrt(
        jnp.mean(gradients * gradients, axis=-1, keepdims=True) + vector_eps
    )


def local(
    block_input,
    cotangent,
    segments,
    qkv_weight,
    proj_weight,
    up_weight,
    down_weight,
    norm_gains,
    biases,
    qkv_bias,
    up_bias,
    qkv_state,
    proj_state,
    up_state,
    down_state,
):
    tensor_rank = lax.axis_index("tensor")
    local_width = qkv_weight.shape[3]
    local_hidden = up_weight.shape[2]
    head_count = local_width // HD
    model_width = block_input.shape[1]
    segment_row = segments[0]
    cosine_table, sine_table = rotary_tables(segment_row)
    stream = block_input.astype(jnp.float32)
    saved_layers = []
    for layer_id in range(LAYERS):
        layer_weights = (
            dp_gather(qkv_weight[layer_id], 0)
            if layer_id == LAYERS - 1
            else chip_gather_rows(qkv_weight[layer_id]),
            chip_gather_rows(proj_weight[layer_id].T),
            dp_gather(up_weight[layer_id], 0),
            chip_gather_rows(down_weight[layer_id].T),
        )
        qkv_full, proj_full, up_full, down_full = layer_weights
        normed, inverse = normalize(stream)
        attn_rows = (normed * norm_gains[layer_id, 0] + biases[layer_id, 0]).astype(jnp.bfloat16)
        mlp_rows = (normed * norm_gains[layer_id, 1] + biases[layer_id, 1]).astype(jnp.bfloat16)
        both_in = tensor_gather(jnp.concatenate([attn_rows, mlp_rows], axis=1))
        attn_in, mlp_in = both_in[:, :model_width], both_in[:, model_width:]
        length = attn_in.shape[0]
        qkv_local_bias = lax.dynamic_slice_in_dim(
            qkv_bias[layer_id], tensor_rank * local_width, local_width, 1
        )
        qkv_pre = (
            jnp.einsum("ld,dcf->lcf", attn_in, qkv_full, preferred_element_type=jnp.float32)
            + qkv_local_bias
        )
        shaped = qkv_pre.reshape(length, 3, head_count, HD)
        queries = rotate(shaped[:, 0], cosine_table, sine_table).astype(jnp.bfloat16)
        key_rows = rotate(shaped[:, 1], cosine_table, sine_table).astype(jnp.bfloat16)
        values = shaped[:, 2].astype(jnp.bfloat16)
        heads_out, log_sums = attend(queries, key_rows, values, segment_row)
        heads_flat = heads_out.reshape(length, local_width)
        up_local_bias = lax.dynamic_slice_in_dim(
            up_bias[layer_id], tensor_rank * local_hidden, local_hidden, 0
        )
        up_pre = jnp.dot(mlp_in, up_full, preferred_element_type=jnp.float32) + up_local_bias
        act_low = gelu_exact(up_pre).astype(jnp.bfloat16)
        partial_sum = jnp.einsum(
            "lf,df->ld", heads_flat, proj_full, preferred_element_type=jnp.float32
        ) + jnp.einsum("lf,df->ld", act_low, down_full, preferred_element_type=jnp.float32)
        branch = tensor_scatter(partial_sum)
        saved_layers.append(
            (
                normed,
                inverse,
                attn_in,
                mlp_in,
                queries,
                key_rows,
                values,
                log_sums,
                heads_flat,
                up_pre,
                act_low,
                layer_weights,
            )
        )
        stream = stream + branch + biases[layer_id, 2] + biases[layer_id, 3]
    grad_stream = cotangent.astype(jnp.float32)
    gains_list = [None] * LAYERS
    biases_list = [None] * LAYERS
    qkv_bias_list = [None] * LAYERS
    up_bias_list = [None] * LAYERS
    weight_list = [None] * LAYERS
    for layer_id in reversed(range(LAYERS)):
        (
            normed,
            inverse,
            attn_in,
            mlp_in,
            queries,
            key_rows,
            values,
            log_sums,
            heads_flat,
            up_pre,
            act_low,
            layer_weights,
        ) = saved_layers[layer_id]
        qkv_full, proj_full, up_full, down_full = layer_weights
        length = attn_in.shape[0]
        out_bias_grad = jnp.sum(grad_stream, axis=0)
        branch_grad = tensor_gather(grad_stream.astype(jnp.bfloat16))
        down_part = jnp.einsum(
            "lf,ld->df", act_low, branch_grad, preferred_element_type=jnp.float32
        )
        act_grad = jnp.einsum(
            "ld,df->lf", branch_grad, down_full, preferred_element_type=jnp.float32
        )
        gelu_back = jax.vjp(gelu_exact, up_pre)[1]
        up_pre_grad = gelu_back(act_grad)[0].astype(jnp.bfloat16)
        up_bias_part = jnp.sum(up_pre_grad, axis=0, dtype=jnp.float32)
        up_part = jnp.einsum("ld,lf->df", mlp_in, up_pre_grad, preferred_element_type=jnp.float32)
        mlp_in_grad = jnp.einsum(
            "lf,df->ld", up_pre_grad, up_full, preferred_element_type=jnp.float32
        )
        proj_part = jnp.einsum(
            "lf,ld->df", heads_flat, branch_grad, preferred_element_type=jnp.float32
        )
        heads_grad = (
            jnp.einsum("ld,df->lf", branch_grad, proj_full, preferred_element_type=jnp.float32)
            .astype(jnp.bfloat16)
            .reshape(length, head_count, HD)
        )
        query_grad, key_grad, value_grad = attend_back(
            queries, key_rows, values, heads_grad, log_sums, segment_row
        )
        qkv_pre_grad = jnp.stack(
            [
                unrotate(query_grad, cosine_table, sine_table),
                unrotate(key_grad, cosine_table, sine_table),
                value_grad,
            ],
            axis=1,
        )
        qkv_pre_grad = qkv_pre_grad.reshape(length, 3, local_width).astype(jnp.bfloat16)
        qkv_bias_part = jnp.sum(qkv_pre_grad, axis=0, dtype=jnp.float32)
        qkv_part = jnp.einsum(
            "ld,lcf->dcf", attn_in, qkv_pre_grad, preferred_element_type=jnp.float32
        )
        attn_in_grad = jnp.einsum(
            "lcf,dcf->ld", qkv_pre_grad, qkv_full, preferred_element_type=jnp.float32
        )
        both_grad = tensor_scatter(jnp.concatenate([attn_in_grad, mlp_in_grad], axis=1))
        attn_rows_grad, mlp_rows_grad = both_grad[:, :model_width], both_grad[:, model_width:]
        gains_list[layer_id] = jnp.stack(
            [jnp.sum(attn_rows_grad * normed, axis=0), jnp.sum(mlp_rows_grad * normed, axis=0)]
        )
        biases_list[layer_id] = jnp.stack(
            [
                jnp.sum(attn_rows_grad, axis=0),
                jnp.sum(mlp_rows_grad, axis=0),
                out_bias_grad,
                out_bias_grad,
            ]
        )
        qkv_bias_list[layer_id] = lax.dynamic_update_slice_in_dim(
            jnp.zeros((3, model_width), jnp.float32), qkv_bias_part, tensor_rank * local_width, 1
        )
        up_bias_list[layer_id] = lax.dynamic_update_slice_in_dim(
            jnp.zeros((up_bias.shape[1],), jnp.float32), up_bias_part, tensor_rank * local_hidden, 0
        )
        normed_grad = (
            attn_rows_grad * norm_gains[layer_id, 0] + mlp_rows_grad * norm_gains[layer_id, 1]
        )
        normed_mean = jnp.mean(normed_grad, axis=-1, keepdims=True)
        product_mean = jnp.mean(normed_grad * normed, axis=-1, keepdims=True)
        grad_stream = grad_stream + inverse * (normed_grad - normed_mean - normed * product_mean)
        weight_list[layer_id] = (qkv_part, proj_part, up_part, down_part)
        if layer_id > 0:
            weight_list[layer_id] = scatter_layer(weight_list[layer_id], proj_whole=True)
            first_sum, grad_stream = lax.optimization_barrier((weight_list[layer_id][0], grad_stream))
            weight_list[layer_id] = (first_sum,) + weight_list[layer_id][1:]
    small_parts = (
        jnp.stack(gains_list),
        jnp.stack(biases_list),
        jnp.stack(qkv_bias_list),
        jnp.stack(up_bias_list),
    )
    flat = butterfly_sum(jnp.concatenate([part.reshape(-1) for part in small_parts]))
    small_sums = []
    offset = 0
    for part in small_parts:
        small_sums.append(flat[offset : offset + part.size].reshape(part.shape))
        offset += part.size
    gains_grad, biases_grad, qkv_bias_grad, up_bias_grad = small_sums
    flat, first_down = lax.optimization_barrier((flat, weight_list[0][3]))
    weight_list[0] = scatter_layer(weight_list[0][:3] + (first_down,), proj_whole=True)
    qkv_grad = jnp.stack([weight_list[layer_id][0] for layer_id in range(LAYERS)])
    proj_grad = jnp.stack([weight_list[layer_id][1] for layer_id in range(LAYERS)])
    up_grad = jnp.stack([weight_list[layer_id][2] for layer_id in range(LAYERS)])
    down_grad = jnp.stack([weight_list[layer_id][3] for layer_id in range(LAYERS)])
    qkv_state_new = momentum * qkv_state + qkv_grad
    proj_state_new = momentum * proj_state + proj_grad
    up_state_new = momentum * up_state + up_grad
    down_state_new = momentum * down_state + down_grad
    rows_local = qkv_state.shape[1]
    dp_count = lax.axis_size("dp")
    dp_rank = lax.axis_index("dp")
    slot_count = 4 * LAYERS
    sub = dp_count // slot_count
    piece_width = up_state.shape[2] // sub
    slot_mats = []
    for layer_id in range(LAYERS):
        slot_mats.append(qkv_state_new[layer_id].reshape(rows_local, 3 * local_width))
        slot_mats.append(proj_state_new[layer_id].T)
        slot_mats.append(up_state_new[layer_id])
        slot_mats.append(down_state_new[layer_id].T)
    pieces = []
    for mat in slot_mats:
        width = mat.shape[1] // sub
        split = mat.reshape(rows_local, sub, width).transpose(1, 0, 2)
        pieces.append(jnp.pad(split, ((0, 0), (0, 0), (0, piece_width - width))))
    outgoing = jnp.concatenate(pieces, axis=0)
    owned = lax.all_to_all(outgoing, "dp", split_axis=0, concat_axis=0, tiled=True)
    owned = owned.reshape(dp_count * rows_local, piece_width)
    owned, grad_stream = lax.optimization_barrier((owned, grad_stream))
    gram = jnp.dot(owned, owned.T, precision=ns_precision)
    bit = 1
    while bit < sub:
        gram = gram + lax.ppermute(gram, "dp", swap_pairs(dp_count, bit))
        bit *= 2
    core_half = dp_rank % 2
    half_rows = gram.shape[0] // 2
    mine = lax.dynamic_slice_in_dim(gram, core_half * half_rows, half_rows, 0)
    mine = mine + lax.ppermute(mine, "tensor", [(0, 1), (1, 0)])
    other = lax.ppermute(mine, "dp", swap_pairs(dp_count, 1))
    gram = jnp.where(
        core_half == 0,
        jnp.concatenate([mine, other], axis=0),
        jnp.concatenate([other, mine], axis=0),
    )
    norm_sq = jnp.trace(gram)
    scale = 1.0 / (jnp.sqrt(norm_sq) + frobenius_eps)
    current_gram = gram * (scale * scale)
    identity = jnp.eye(current_gram.shape[0], dtype=jnp.float32)
    accumulated = None
    for iteration in range(NS_ITERS):
        squared = jnp.dot(current_gram, current_gram, precision=ns_precision)
        polynomial = coef_first * identity + coef_second * current_gram + coef_third * squared
        if accumulated is None:
            accumulated = polynomial
        else:
            accumulated = jnp.dot(polynomial, accumulated, precision=ns_precision)
        if iteration + 1 < NS_ITERS:
            current_gram = jnp.dot(
                polynomial,
                jnp.dot(current_gram, polynomial, precision=ns_precision),
                precision=ns_precision,
            )
    current = jnp.dot(accumulated, owned * scale, precision=ns_precision)
    returned = lax.all_to_all(
        current.astype(jnp.bfloat16).reshape(dp_count, rows_local, piece_width),
        "dp",
        split_axis=0,
        concat_axis=0,
        tiled=True,
    ).reshape(slot_count, sub, rows_local, piece_width)
    my_rows = []
    for slot_id, mat in enumerate(slot_mats):
        width = mat.shape[1] // sub
        my_rows.append(
            returned[slot_id, :, :, :width]
            .astype(jnp.float32)
            .transpose(1, 0, 2)
            .reshape(rows_local, sub * width)
        )
    muon_step = muon_rate * match_rms
    qkv_list, proj_list, up_list, down_list = ([], [], [], [])
    for layer_id in range(LAYERS):
        base_slot = 4 * layer_id
        qkv_ortho = my_rows[base_slot].reshape(rows_local, 3, local_width)
        proj_ortho = my_rows[base_slot + 1].T
        up_ortho = my_rows[base_slot + 2]
        down_ortho = my_rows[base_slot + 3].T
        qkv_list.append(
            qkv_weight[layer_id].astype(jnp.float32) - muon_step * math.sqrt(3 * D) * qkv_ortho
        )
        proj_list.append(
            proj_weight[layer_id].astype(jnp.float32) - muon_step * math.sqrt(D) * proj_ortho
        )
        up_list.append(
            up_weight[layer_id].astype(jnp.float32) - muon_step * math.sqrt(FF) * up_ortho
        )
        down_list.append(
            down_weight[layer_id].astype(jnp.float32) - muon_step * math.sqrt(FF) * down_ortho
        )
    qkv_new = jnp.stack(qkv_list)
    proj_new = jnp.stack(proj_list)
    up_new = jnp.stack(up_list)
    down_new = jnp.stack(down_list)
    gains_new = vector_step(norm_gains, gains_grad)
    biases_new = vector_step(biases, biases_grad)
    qkv_bias_new = vector_step(qkv_bias, qkv_bias_grad)
    up_bias_new = vector_step(up_bias, up_bias_grad)
    return (
        stream,
        grad_stream,
        qkv_grad,
        proj_grad,
        up_grad,
        down_grad,
        gains_grad,
        biases_grad,
        qkv_bias_grad,
        up_bias_grad,
        qkv_new,
        proj_new,
        up_new,
        down_new,
        gains_new,
        biases_new,
        qkv_bias_new,
        up_bias_new,
        qkv_state_new,
        proj_state_new,
        up_state_new,
        down_state_new,
    )


def solution(mesh):
    return jax.shard_map(
        local,
        mesh=mesh,
        in_specs=(
            P(("dp", "tensor"), None),
            P(("dp", "tensor"), None),
            P("dp", None),
            P(None, "dp", None, "tensor"),
            P(None, "tensor", "dp"),
            P(None, "dp", "tensor"),
            P(None, "tensor", "dp"),
            P(),
            P(),
            P(),
            P(),
            P(None, "dp", None, "tensor"),
            P(None, "tensor", "dp"),
            P(None, "dp", "tensor"),
            P(None, "tensor", "dp"),
        ),
        out_specs=(
            P(("dp", "tensor"), None),
            P(("dp", "tensor"), None),
            P(None, "dp", None, "tensor"),
            P(None, "tensor", "dp"),
            P(None, "dp", "tensor"),
            P(None, "tensor", "dp"),
            P(),
            P(),
            P(),
            P(),
            P(None, "dp", None, "tensor"),
            P(None, "tensor", "dp"),
            P(None, "dp", "tensor"),
            P(None, "tensor", "dp"),
            P(),
            P(),
            P(),
            P(),
            P(None, "dp", None, "tensor"),
            P(None, "tensor", "dp"),
            P(None, "dp", "tensor"),
            P(None, "tensor", "dp"),
        ),
        check_vma=False,
    )
```
